32 devices in a mesh: outer: 4 (over y, x), inner: 8 (over z, core).
Axes of the slice: x: 2, y: 2, z: 4, core: 2. Of those that a mesh axis runs over, the one named last changes fastest.
Arguments:
- tokens: bfloat16 [12288, 1024], P(('outer', 'inner')), may hold values from -6 to 6
- log_decay: float32 [12288, 16], P(('outer', 'inner')), may hold values from -1 to 0, as said below
- query_weight: bfloat16 [1024, 1024], replicated, may hold values from -0.1875 to 0.1875
- key_weight: bfloat16 [1024, 1024], replicated, may hold values from -0.1875 to 0.1875
- value_weight: bfloat16 [1024, 1024], replicated, may hold values from -0.1875 to 0.1875
- norm_gain: float32 [1024], replicated, may hold values from 0.1 to 1.9
- output_weight: bfloat16 [1024, 1024], replicated, may hold values from -0.1875 to 0.1875
Outputs:
- mixed: bfloat16 [12288, 1024], P(('outer', 'inner'))
The draws below stay inside these ranges and needn't reach their ends.
Inputs may be any that keep to these rules, and one draw needn't show every extreme that they name: log_decay is negative.
All inputs are finite; a program needn't handle non-finite values.
Results may differ from the reference program's by a relative error of at most 0.0063.
Values sent between devices are 32-bit elements; how exact they have to be, the bound alone decides.
No kernel may reach another device: no remote copies, remote signals or barrier semaphores. Data moves between devices by JAX's collectives and lax.ppermute only.
A program may use at most 320 MiB of HBM per device.

```python
import math
import jax
import jax.numpy as jnp
from jax import lax

D = 1024
HEAD_COUNT = 16
HEAD_DIM = 64
TOK_DEV = 384
TOKEN_COUNT = 12288


def draw_log_decay(key, part):
    token_parts = jax.random.split(key, 6)
    slow_share = 0.5
    picked = jax.random.uniform(token_parts[0], (HEAD_COUNT,)) < slow_share
    fast_rate = jnp.exp(jax.random.uniform(token_parts[1], (HEAD_COUNT,), minval=math.log(1.0 / 1000.0), maxval=math.log(1.0 / 40.0)))
    slow_rate = 0.25 * math.log(10.0) / TOKEN_COUNT
    base = jnp.where(picked, slow_rate, fast_rate)
    block_count = TOKEN_COUNT // TOK_DEV
    block_factor = jnp.exp(jax.random.uniform(token_parts[2], (block_count,), minval=-math.log(2.0), maxval=math.log(2.0)))
    positions = jnp.arange(TOKEN_COUNT) // TOK_DEV
    rough = jnp.exp(jax.random.uniform(token_parts[3], (TOKEN_COUNT, HEAD_COUNT), minval=-math.log(2.0), maxval=math.log(2.0)))
    decay_rate = base[None, :] * block_factor[positions][:, None] * rough
    decay_power = jax.random.uniform(token_parts[4], (TOKEN_COUNT, HEAD_COUNT)) < 2.0 / TOKEN_COUNT
    training_loss = jnp.log(jax.random.uniform(token_parts[5], (TOKEN_COUNT, HEAD_COUNT), minval=0.5, maxval=0.8))
    return (jnp.where(decay_power, training_loss, 0.0) - decay_rate).astype(jnp.float32)


def steps_of(stream_key, shape, pieces, least, top_value):
    def one(dim, shards_of):
        draws = jax.random.uniform(jax.random.fold_in(jax.random.fold_in(stream_key, 6), dim), (shards_of,), jnp.float32, least / len(pieces), top_value / len(pieces))
        return jnp.repeat(jnp.exp(draws), shape[dim] // shards_of).reshape((-1,) + (1,) * (len(shape) - dim - 1))

    factor_of = one(*pieces[0])
    for cut in pieces[1:]:
        factor_of = factor_of * one(*cut)
    return factor_of


def bell_draw(key, shape, spread, bound, cuts=(), dtype=jnp.bfloat16):
    values = jax.random.normal(key, shape, jnp.float32) * spread
    if len(cuts) > 0:
        values = steps_of(key, shape, cuts, -0.22, 0.18) * values
    return jnp.clip(values, min=-bound, max=bound).astype(dtype)


def setup_inputs(seed: int = 0) -> dict:
    seeds = jax.random.split(jax.random.key(seed), 8)
    tokens = bell_draw(seeds[0], (TOKEN_COUNT, D), 1.0, 6.0, ((0, 32),))
    log_decay = draw_log_decay(jax.random.fold_in(seeds[7], 71), 0)
    query_weight = bell_draw(seeds[2], (D, D), D ** -0.5, 0.1875)
    key_weight = bell_draw(seeds[3], (D, D), D ** -0.5, 0.1875)
    value_weight = bell_draw(seeds[4], (D, D), D ** -0.5, 0.1875)
    norm_gain = jnp.clip(1.0 + 0.18 * jax.random.normal(seeds[5], (D,), jnp.float32), 0.1, 1.9)
    output_weight = bell_draw(seeds[6], (D, D), D ** -0.5, 0.1875)
    return {"tokens": tokens, "log_decay": log_decay, "query_weight": query_weight, "key_weight": key_weight, "value_weight": value_weight, "norm_gain": norm_gain, "output_weight": output_weight}


def local_head(q_head, k_head, v_head, g_head):
    cum = jnp.cumsum(g_head)
    count = cum.shape[0]
    rows = lax.broadcasted_iota(jnp.int32, (count, count), 0)
    cols = lax.broadcasted_iota(jnp.int32, (count, count), 1)
    lower = cols <= rows
    diff = jnp.where(lower, cum[:, None] - cum[None, :], 0.0)
    decay = jnp.where(lower, jnp.exp(diff), 0.0)
    scores = jnp.dot(q_head, k_head.T, preferred_element_type=jnp.float32)
    weights = (scores * decay).astype(jnp.bfloat16)
    intra = jnp.dot(weights, v_head, preferred_element_type=jnp.float32)
    last = cum[-1]
    scaled = (k_head.astype(jnp.float32) * jnp.exp(last - cum)[:, None]).astype(jnp.bfloat16)
    local = jnp.dot(scaled.T, v_head, preferred_element_type=jnp.float32)
    return (intra, local, jnp.exp(last))

def project(block, query_weight, key_weight, value_weight, heads):
    count = block.shape[0]
    queries = jax.nn.silu(jnp.dot(block, query_weight, preferred_element_type=jnp.float32)).astype(jnp.bfloat16)
    keys = jax.nn.silu(jnp.dot(block, key_weight, preferred_element_type=jnp.float32)).astype(jnp.bfloat16)
    value_rows = jnp.dot(block, value_weight, preferred_element_type=jnp.float32).astype(jnp.bfloat16)
    split = lambda arr: arr.reshape(count, heads, -1).transpose(1, 0, 2)
    return (split(queries), split(keys), split(value_rows))

def finish(intra, queries, g_block, incoming, norm_gain, output_weight):
    cum = jnp.cumsum(g_block, axis=0)
    qfloat = queries.astype(jnp.float32)
    inter = jnp.einsum('htd,hde->the', qfloat, incoming, precision=lax.Precision.HIGHEST) * jnp.exp(cum)[:, :, None]
    attended = intra.transpose(1, 0, 2) + inter
    scale = lax.rsqrt(lax.optimization_barrier(jnp.mean(attended * attended, axis=-1, keepdims=True)) + 1e-05)
    count = attended.shape[0]
    normalized_output = ((attended * scale).reshape(count, -1) * norm_gain).astype(jnp.bfloat16)
    return jnp.dot(normalized_output, output_weight, preferred_element_type=jnp.float32).astype(jnp.bfloat16)

def reference(tokens, log_decay, query_weight, key_weight, value_weight, norm_gain, output_weight):
    blocks = TOKEN_COUNT // TOK_DEV
    token_blocks = tokens.reshape(blocks, TOK_DEV, D)
    decay_blocks = log_decay.reshape(blocks, TOK_DEV, HEAD_COUNT)

    def step(state, item):
        block, g_block = item
        queries, keys, value_rows = project(block, query_weight, key_weight, value_weight, HEAD_COUNT)
        intra, local, fall = lax.map(lambda token_parts: local_head(*token_parts), (queries, keys, value_rows, g_block.T))
        result = finish(intra, queries, g_block, state, norm_gain, output_weight)
        return (fall[:, None, None] * state + local, result)
    start = jnp.zeros((HEAD_COUNT, HEAD_DIM, HEAD_DIM), jnp.float32)
    final, outputs = lax.scan(step, start, (token_blocks, decay_blocks))
    return outputs.reshape(TOKEN_COUNT, D)
```

```python
import jax
import jax.numpy as jnp
from jax import lax
from jax.sharding import PartitionSpec as P

AXES = ("outer", "inner")


def combine(earlier, later):
    g_e, s_e = earlier
    g_l, s_l = later
    return (g_e + g_l, jnp.exp(g_l)[:, None, None] * s_e + s_l)


def exclusive_scan(own, count):
    before = (jnp.zeros_like(own[0]), jnp.zeros_like(own[1]))
    through = own
    shift = 1
    while shift < count:
        perm = [(i, i + shift) for i in range(count - shift)]
        got = jax.tree.map(lambda part: lax.ppermute(part, AXES, perm), through)
        before = combine(got, before)
        shift *= 2
        if shift < count:
            through = combine(before, own)
    return before[1]


def shards(count, tokens, log_decay, query_weight, key_weight, value_weight, norm_gain, output_weight):
    rows = tokens.shape[0]
    heads = log_decay.shape[1]
    f32 = jnp.float32
    keys = jax.nn.silu(jnp.dot(tokens, key_weight, preferred_element_type=f32)).astype(jnp.bfloat16)
    value_rows = jnp.dot(tokens, value_weight, preferred_element_type=f32).astype(jnp.bfloat16)
    keys = keys.reshape(rows, heads, -1)
    value_rows = value_rows.reshape(rows, heads, -1)
    cum = jnp.cumsum(log_decay, axis=0)
    last = cum[-1]
    scaled = (keys.astype(f32) * jnp.exp(last[None, :] - cum)[:, :, None]).astype(jnp.bfloat16)
    local = jnp.einsum("thd,the->hde", scaled, value_rows, preferred_element_type=f32)
    incoming = exclusive_scan((last, local), count)

    queries = jax.nn.silu(jnp.dot(tokens, query_weight, preferred_element_type=f32)).astype(jnp.bfloat16)
    queries = queries.reshape(rows, heads, -1)
    t_idx = lax.broadcasted_iota(jnp.int32, (rows, rows), 0)
    s_idx = lax.broadcasted_iota(jnp.int32, (rows, rows), 1)
    lower = (s_idx <= t_idx)[None]
    cum_h = cum.T
    diff = jnp.where(lower, cum_h[:, :, None] - cum_h[:, None, :], 0.0)
    decay = jnp.where(lower, jnp.exp(diff), 0.0)
    scores = jnp.einsum("thd,shd->hts", queries, keys, preferred_element_type=f32)
    weights = (scores * decay).astype(jnp.bfloat16)
    intra = jnp.einsum("hts,shd->thd", weights, value_rows, preferred_element_type=f32)

    qfloat = queries.astype(f32)
    inter = (
        jnp.einsum("thd,hde->the", qfloat, incoming, precision=lax.Precision.HIGHEST)
        * jnp.exp(cum)[:, :, None]
    )
    attended = intra + inter
    scale = lax.rsqrt(jnp.mean(attended * attended, axis=-1, keepdims=True) + 1e-05)
    normalized_output = ((attended * scale).reshape(rows, -1) * norm_gain).astype(jnp.bfloat16)
    return jnp.dot(normalized_output, output_weight, preferred_element_type=f32).astype(jnp.bfloat16)


def solution(mesh):
    count = mesh.shape["outer"] * mesh.shape["inner"]
    in_specs = (P(AXES, None), P(AXES, None), P(), P(), P(), P(), P())
    out_specs = P(AXES, None)
    body = lambda *args: shards(count, *args)
    return jax.shard_map(body, mesh=mesh, in_specs=in_specs, out_specs=out_specs, check_vma=False)
```

```python
import jax
import jax.numpy as jnp
from jax import lax
from jax.sharding import PartitionSpec as P

AXES = ("outer", "inner")


def combine(earlier, later, heads):
    body = earlier.shape[0] - 8
    scale = jnp.concatenate(
        [jnp.repeat(jnp.exp(later[body, :heads]), body // heads), jnp.ones((8,), later.dtype)]
    )
    return scale[:, None] * earlier + later


def exclusive_scan(own, count, heads):
    before = jnp.zeros_like(own)
    through = own
    shift = 1
    while shift < count:
        perm = [(i, i + shift) for i in range(count - shift)]
        got = lax.ppermute(through, AXES, perm)
        before = combine(got, before, heads)
        shift *= 2
        if shift < count:
            through = combine(before, own, heads)
    return before[:-8]


def shards(count, tokens, log_decay, query_weight, key_weight, value_weight, norm_gain, output_weight):
    rows = tokens.shape[0]
    heads = log_decay.shape[1]
    f32 = jnp.float32
    keys = jax.nn.silu(jnp.dot(tokens, key_weight, preferred_element_type=f32)).astype(jnp.bfloat16)
    value_rows = jnp.dot(tokens, value_weight, preferred_element_type=f32).astype(jnp.bfloat16)
    keys = keys.reshape(rows, heads, -1)
    value_rows = value_rows.reshape(rows, heads, -1)
    cum = jnp.cumsum(log_decay, axis=0)
    last = cum[-1]
    scaled = (keys.astype(f32) * jnp.exp(last[None, :] - cum)[:, :, None]).astype(jnp.bfloat16)
    local = jnp.einsum("thd,the->hde", scaled, value_rows, preferred_element_type=f32)
    lanes = 128
    packed = jnp.concatenate(
        [local.reshape(-1, lanes), jnp.zeros((8, lanes), f32).at[0, :heads].set(last)], axis=0
    )
    incoming = exclusive_scan(packed, count, heads).reshape(local.shape)

    queries = jax.nn.silu(jnp.dot(tokens, query_weight, preferred_element_type=f32)).astype(jnp.bfloat16)
    queries = queries.reshape(rows, heads, -1)
    t_idx = lax.broadcasted_iota(jnp.int32, (rows, rows), 0)
    s_idx = lax.broadcasted_iota(jnp.int32, (rows, rows), 1)
    lower = (s_idx <= t_idx)[None]
    cum_h = cum.T
    diff = jnp.where(lower, cum_h[:, :, None] - cum_h[:, None, :], 0.0)
    decay = jnp.where(lower, jnp.exp(diff), 0.0)
    scores = jnp.einsum("thd,shd->hts", queries, keys, preferred_element_type=f32)
    weights = (scores * decay).astype(jnp.bfloat16)
    intra = jnp.einsum("hts,shd->thd", weights, value_rows, preferred_element_type=f32)

    qfloat = queries.astype(f32)
    inter = (
        jnp.einsum("thd,hde->the", qfloat, incoming, precision=lax.Precision.HIGHEST)
        * jnp.exp(cum)[:, :, None]
    )
    attended = intra + inter
    scale = lax.rsqrt(jnp.mean(attended * attended, axis=-1, keepdims=True) + 1e-05)
    normalized_output = ((attended * scale).reshape(rows, -1) * norm_gain).astype(jnp.bfloat16)
    return jnp.dot(normalized_output, output_weight, preferred_element_type=f32).astype(jnp.bfloat16)


def solution(mesh):
    count = mesh.shape["outer"] * mesh.shape["inner"]
    in_specs = (P(AXES, None), P(AXES, None), P(), P(), P(), P(), P())
    out_specs = P(AXES, None)
    body = lambda *args: shards(count, *args)
    return jax.shard_map(body, mesh=mesh, in_specs=in_specs, out_specs=out_specs, check_vma=False)
```

```python
import jax
import jax.numpy as jnp
from jax import lax
from jax.sharding import PartitionSpec as P

AXES = ("outer", "inner")


def combine(earlier, later, heads):
    body = earlier.shape[0] - 8
    scale = jnp.concatenate(
        [jnp.repeat(jnp.exp(later[body, :heads]), body // heads), jnp.ones((8,), later.dtype)]
    )
    return scale[:, None] * earlier + later


def half_of(whole, half, heads):
    body = whole.shape[0] - 8
    part = heads // 2
    rows = body // 2
    states = jnp.where(half == 0, whole[:rows], whole[rows:body])
    logs = jnp.where(half == 0, whole[body, :part], whole[body, part:heads])
    return jnp.concatenate([states, jnp.zeros((8, whole.shape[1]), whole.dtype).at[0, :part].set(logs)])


def join_halves(first, second, heads):
    body = first.shape[0] - 8
    part = heads // 2
    logs = jnp.concatenate([first[body, :part], second[body, :part]])
    tail = jnp.zeros((8, first.shape[1]), first.dtype).at[0, :heads].set(logs)
    return jnp.concatenate([first[:body], second[:body], tail])


def exclusive_scan(own, count, heads):
    flat = lax.axis_index(AXES)
    core = flat % 2
    chip = flat // 2
    chips = count // 2
    partner = [(i, i ^ 1) for i in range(count)]
    other = lax.ppermute(own, AXES, partner)
    pooled = jnp.where(core == 0, combine(own, other, heads), combine(other, own, heads))
    through = half_of(pooled, core, heads)
    before = jnp.zeros_like(through)
    bit = 1
    while bit < chips:
        perm = [(i, i ^ (2 * bit)) for i in range(count)]
        got = lax.ppermute(through, AXES, perm)
        lower = (chip & bit) != 0
        before = jnp.where(lower, combine(got, before, heads // 2), before)
        bit *= 2
        if bit < chips:
            through = jnp.where(lower, combine(got, through, heads // 2), combine(through, got, heads // 2))
    swapped = lax.ppermute(before, AXES, partner)
    whole = jnp.where(core == 0, join_halves(before, swapped, heads), join_halves(swapped, before, heads))
    whole = jnp.where(core == 0, whole, combine(whole, other, heads))
    return whole[:-8]


def shards(count, tokens, log_decay, query_weight, key_weight, value_weight, norm_gain, output_weight):
    rows = tokens.shape[0]
    heads = log_decay.shape[1]
    f32 = jnp.float32
    keys = jax.nn.silu(jnp.dot(tokens, key_weight, preferred_element_type=f32)).astype(jnp.bfloat16)
    value_rows = jnp.dot(tokens, value_weight, preferred_element_type=f32).astype(jnp.bfloat16)
    keys = keys.reshape(rows, heads, -1)
    value_rows = value_rows.reshape(rows, heads, -1)
    cum = jnp.cumsum(log_decay, axis=0)
    last = cum[-1]
    scaled = (keys.astype(f32) * jnp.exp(last[None, :] - cum)[:, :, None]).astype(jnp.bfloat16)
    local = jnp.einsum("thd,the->hde", scaled, value_rows, preferred_element_type=f32)
    lanes = 128
    packed = jnp.concatenate(
        [local.reshape(-1, lanes), jnp.zeros((8, lanes), f32).at[0, :heads].set(last)], axis=0
    )
    incoming = exclusive_scan(packed, count, heads).reshape(local.shape)

    queries = jax.nn.silu(jnp.dot(tokens, query_weight, preferred_element_type=f32)).astype(jnp.bfloat16)
    queries = queries.reshape(rows, heads, -1)
    t_idx = lax.broadcasted_iota(jnp.int32, (rows, rows), 0)
    s_idx = lax.broadcasted_iota(jnp.int32, (rows, rows), 1)
    lower = (s_idx <= t_idx)[None]
    cum_h = cum.T
    diff = jnp.where(lower, cum_h[:, :, None] - cum_h[:, None, :], 0.0)
    decay = jnp.where(lower, jnp.exp(diff), 0.0)
    scores = jnp.einsum("thd,shd->hts", queries, keys, preferred_element_type=f32)
    weights = (scores * decay).astype(jnp.bfloat16)
    intra = jnp.einsum("hts,shd->thd", weights, value_rows, preferred_element_type=f32)

    qfloat = queries.astype(f32)
    inter = (
        jnp.einsum("thd,hde->the", qfloat, incoming, precision=lax.Precision.HIGHEST)
        * jnp.exp(cum)[:, :, None]
    )
    attended = intra + inter
    scale = lax.rsqrt(jnp.mean(attended * attended, axis=-1, keepdims=True) + 1e-05)
    normalized_output = ((attended * scale).reshape(rows, -1) * norm_gain).astype(jnp.bfloat16)
    return jnp.dot(normalized_output, output_weight, preferred_element_type=f32).astype(jnp.bfloat16)


def solution(mesh):
    count = mesh.shape["outer"] * mesh.shape["inner"]
    in_specs = (P(AXES, None), P(AXES, None), P(), P(), P(), P(), P())
    out_specs = P(AXES, None)
    body = lambda *args: shards(count, *args)
    return jax.shard_map(body, mesh=mesh, in_specs=in_specs, out_specs=out_specs, check_vma=False)
```

```python
import jax
import jax.numpy as jnp
from jax import lax
from jax.sharding import PartitionSpec as P

AXES = ("outer", "inner")


def combine(earlier, later, heads):
    body = earlier.shape[0] - 8
    scale = jnp.concatenate(
        [jnp.repeat(jnp.exp(later[body, :heads]), body // heads), jnp.ones((8,), later.dtype)]
    )
    return scale[:, None] * earlier + later


def half_of(whole, half, heads):
    body = whole.shape[0] - 8
    part = heads // 2
    rows = body // 2
    states = jnp.where(half == 0, whole[:rows], whole[rows:body])
    logs = jnp.where(half == 0, whole[body, :part], whole[body, part:heads])
    return jnp.concatenate([states, jnp.zeros((8, whole.shape[1]), whole.dtype).at[0, :part].set(logs)])


def join_halves(first, second, heads):
    body = first.shape[0] - 8
    part = heads // 2
    logs = jnp.concatenate([first[body, :part], second[body, :part]])
    tail = jnp.zeros((8, first.shape[1]), first.dtype).at[0, :heads].set(logs)
    return jnp.concatenate([first[:body], second[:body], tail])


def exclusive_scan(own, count, heads):
    flat = lax.axis_index(AXES)
    core = flat % 2
    chip = flat // 2
    chips = count // 2
    partner = [(i, i ^ 1) for i in range(count)]
    other = lax.ppermute(own, AXES, partner)
    pooled = jnp.where(core == 0, combine(own, other, heads), combine(other, own, heads))
    through = half_of(pooled, core, heads)
    before = jnp.zeros_like(through)
    received = []
    bit = 1
    while bit < chips:
        perm = [(i, i ^ (2 * bit)) for i in range(count)]
        got = lax.ppermute(through, AXES, perm)
        received.append(got)
        lower = (chip & bit) != 0
        before = jnp.where(lower, combine(got, before, heads // 2), before)
        bit *= 2
        if bit < chips:
            through = jnp.where(lower, combine(got, through, heads // 2), combine(through, got, heads // 2))
    swapped = lax.ppermute(before, AXES, partner)
    whole = jnp.where(core == 0, join_halves(before, swapped, heads), join_halves(swapped, before, heads))
    whole = jnp.where(core == 0, whole, combine(whole, other, heads))
    return whole[:-8], received


def shards(count, tokens, log_decay, query_weight, key_weight, value_weight, norm_gain, output_weight):
    rows = tokens.shape[0]
    heads = log_decay.shape[1]
    f32 = jnp.float32
    keys = jax.nn.silu(jnp.dot(tokens, key_weight, preferred_element_type=f32)).astype(jnp.bfloat16)
    value_rows = jnp.dot(tokens, value_weight, preferred_element_type=f32).astype(jnp.bfloat16)
    keys = keys.reshape(rows, heads, -1)
    value_rows = value_rows.reshape(rows, heads, -1)
    cum = jnp.cumsum(log_decay, axis=0)
    last = cum[-1]
    scaled = (keys.astype(f32) * jnp.exp(last[None, :] - cum)[:, :, None]).astype(jnp.bfloat16)
    local = jnp.einsum("thd,the->hde", scaled, value_rows, preferred_element_type=f32)
    lanes = 128
    packed = jnp.concatenate(
        [local.reshape(-1, lanes), jnp.zeros((8, lanes), f32).at[0, :heads].set(last)], axis=0
    )
    incoming, received = exclusive_scan(packed, count, heads)
    incoming = incoming.reshape(local.shape)
    gate = lambda value, round_: lax.optimization_barrier((value, received[min(round_, len(received) - 1)]))[0]

    queries = jax.nn.silu(
        jnp.dot(gate(tokens, 0), query_weight, preferred_element_type=f32)
    ).astype(jnp.bfloat16)
    queries = queries.reshape(rows, heads, -1)
    t_idx = lax.broadcasted_iota(jnp.int32, (rows, rows), 0)
    s_idx = lax.broadcasted_iota(jnp.int32, (rows, rows), 1)
    lower = (s_idx <= t_idx)[None]
    cum_h = cum.T
    diff = jnp.where(lower, cum_h[:, :, None] - cum_h[:, None, :], 0.0)
    decay = jnp.where(lower, jnp.exp(diff), 0.0)
    parts = []
    half = heads // 2
    for part in range(2):
        pick = slice(part * half, (part + 1) * half)
        scores = jnp.einsum(
            "thd,shd->hts", gate(queries[:, pick], part + 1), keys[:, pick], preferred_element_type=f32
        )
        weights = (scores * decay[pick]).astype(jnp.bfloat16)
        parts.append(jnp.einsum("hts,shd->thd", weights, value_rows[:, pick], preferred_element_type=f32))
    intra = jnp.concatenate(parts, axis=1)

    qfloat = queries.astype(f32)
    inter = (
        jnp.einsum("thd,hde->the", qfloat, incoming, precision=lax.Precision.HIGHEST)
        * jnp.exp(cum)[:, :, None]
    )
    attended = intra + inter
    scale = lax.rsqrt(jnp.mean(attended * attended, axis=-1, keepdims=True) + 1e-05)
    normalized_output = ((attended * scale).reshape(rows, -1) * norm_gain).astype(jnp.bfloat16)
    return jnp.dot(normalized_output, output_weight, preferred_element_type=f32).astype(jnp.bfloat16)


def solution(mesh):
    count = mesh.shape["outer"] * mesh.shape["inner"]
    in_specs = (P(AXES, None), P(AXES, None), P(), P(), P(), P(), P())
    out_specs = P(AXES, None)
    body = lambda *args: shards(count, *args)
    return jax.shard_map(body, mesh=mesh, in_specs=in_specs, out_specs=out_specs, check_vma=False)
```

```python
import functools

import jax
import jax.numpy as jnp
from jax import lax
from jax.experimental import pallas as pl
from jax.sharding import PartitionSpec as P

AXES = ("outer", "inner")

LANES = 128


def intra_kernel(q_ref, k_ref, v_ref, cum_ref, cum_t_ref, o_ref, *, head_dim):
    f32 = jnp.float32
    pair = pl.program_id(0)
    group = LANES // head_dim
    rows = q_ref.shape[0]
    heads = cum_ref.shape[1]
    q = q_ref[...]
    k = k_ref[...]
    v = v_ref[...]
    lane_head = lax.broadcasted_iota(jnp.int32, q.shape, 1) // head_dim
    t_i = lax.broadcasted_iota(jnp.int32, (rows, rows), 0)
    s_i = lax.broadcasted_iota(jnp.int32, (rows, rows), 1)
    lower = s_i <= t_i
    cum = cum_ref[...]
    cum_t = cum_t_ref[...]
    col_head = lax.broadcasted_iota(jnp.int32, cum.shape, 1)
    row_head = lax.broadcasted_iota(jnp.int32, cum_t.shape, 0)
    out = None
    for j in range(group):
        head = pair * group + j
        mine = lane_head == j
        q_j = jnp.where(mine, q, jnp.zeros_like(q))
        scores = lax.dot_general(q_j, k, (((1,), (1,)), ((), ())), preferred_element_type=f32)
        col = jnp.sum(jnp.where(col_head == head, cum, 0.0), axis=1, keepdims=True)
        row = jnp.sum(jnp.where(row_head == head, cum_t, 0.0), axis=0, keepdims=True)
        diff = jnp.where(lower, col - row, 0.0)
        decay = jnp.where(lower, jnp.exp(diff), 0.0)
        weights = (scores * decay).astype(jnp.bfloat16)
        o_j = jnp.dot(weights, v, preferred_element_type=f32)
        out = o_j if out is None else jnp.where(mine, o_j, out)
    o_ref[...] = out


def intra_attention(queries, keys, value_rows, cum, head_dim):
    rows, width = queries.shape
    heads = cum.shape[1]
    block = pl.BlockSpec((rows, LANES), lambda p: (0, p))
    whole = lambda shape: pl.BlockSpec(shape, lambda p: (0, 0))
    flops = 4 * rows * rows * LANES * (LANES // head_dim) * (width // LANES)
    return pl.pallas_call(
        functools.partial(intra_kernel, head_dim=head_dim),
        grid=(width // LANES,),
        in_specs=[block, block, block, whole((rows, heads)), whole((heads, rows))],
        out_specs=block,
        out_shape=jax.ShapeDtypeStruct((rows, width), jnp.float32),
        cost_estimate=pl.CostEstimate(
            flops=flops, transcendentals=rows * rows * heads, bytes_accessed=rows * width * 10
        ),
    )(queries, keys, value_rows, cum, cum.T)


def combine(earlier, later, heads):
    body = earlier.shape[0] - 8
    scale = jnp.concatenate(
        [jnp.repeat(jnp.exp(later[body, :heads]), body // heads), jnp.ones((8,), later.dtype)]
    )
    return scale[:, None] * earlier + later


def half_of(whole, half, heads):
    body = whole.shape[0] - 8
    part = heads // 2
    rows = body // 2
    states = jnp.where(half == 0, whole[:rows], whole[rows:body])
    logs = jnp.where(half == 0, whole[body, :part], whole[body, part:heads])
    return jnp.concatenate([states, jnp.zeros((8, whole.shape[1]), whole.dtype).at[0, :part].set(logs)])


def join_halves(first, second, heads):
    body = first.shape[0] - 8
    part = heads // 2
    logs = jnp.concatenate([first[body, :part], second[body, :part]])
    tail = jnp.zeros((8, first.shape[1]), first.dtype).at[0, :heads].set(logs)
    return jnp.concatenate([first[:body], second[:body], tail])


def exclusive_scan(own, count, heads):
    flat = lax.axis_index(AXES)
    core = flat % 2
    chip = flat // 2
    chips = count // 2
    partner = [(i, i ^ 1) for i in range(count)]
    other = lax.ppermute(own, AXES, partner)
    pooled = jnp.where(core == 0, combine(own, other, heads), combine(other, own, heads))
    through = half_of(pooled, core, heads)
    before = jnp.zeros_like(through)
    received = []
    bit = 1
    while bit < chips:
        perm = [(i, i ^ (2 * bit)) for i in range(count)]
        got = lax.ppermute(through, AXES, perm)
        received.append(got)
        lower = (chip & bit) != 0
        before = jnp.where(lower, combine(got, before, heads // 2), before)
        bit *= 2
        if bit < chips:
            through = jnp.where(lower, combine(got, through, heads // 2), combine(through, got, heads // 2))
    swapped = lax.ppermute(before, AXES, partner)
    whole = jnp.where(core == 0, join_halves(before, swapped, heads), join_halves(swapped, before, heads))
    whole = jnp.where(core == 0, whole, combine(whole, other, heads))
    return whole[:-8], received


def shards(count, tokens, log_decay, query_weight, key_weight, value_weight, norm_gain, output_weight):
    rows = tokens.shape[0]
    heads = log_decay.shape[1]
    f32 = jnp.float32
    keys = jax.nn.silu(jnp.dot(tokens, key_weight, preferred_element_type=f32)).astype(jnp.bfloat16)
    value_rows = jnp.dot(tokens, value_weight, preferred_element_type=f32).astype(jnp.bfloat16)
    keys = keys.reshape(rows, heads, -1)
    value_rows = value_rows.reshape(rows, heads, -1)
    cum = jnp.cumsum(log_decay, axis=0)
    last = cum[-1]
    scaled = (keys.astype(f32) * jnp.exp(last[None, :] - cum)[:, :, None]).astype(jnp.bfloat16)
    local = jnp.einsum("thd,the->hde", scaled, value_rows, preferred_element_type=f32)
    lanes = 128
    packed = jnp.concatenate(
        [local.reshape(-1, lanes), jnp.zeros((8, lanes), f32).at[0, :heads].set(last)], axis=0
    )
    incoming, received = exclusive_scan(packed, count, heads)
    incoming = incoming.reshape(local.shape)
    gate = lambda value, round_: lax.optimization_barrier((value, received[min(round_, len(received) - 1)]))[0]

    queries = jax.nn.silu(
        jnp.dot(gate(tokens, 0), query_weight, preferred_element_type=f32)
    ).astype(jnp.bfloat16)
    intra = intra_attention(
        gate(queries, 1), keys.reshape(rows, -1), value_rows.reshape(rows, -1), cum, keys.shape[-1]
    ).reshape(rows, heads, -1)
    queries = queries.reshape(rows, heads, -1)

    qfloat = queries.astype(f32)
    inter = (
        jnp.einsum("thd,hde->the", qfloat, incoming, precision=lax.Precision.HIGHEST)
        * jnp.exp(cum)[:, :, None]
    )
    attended = intra + inter
    scale = lax.rsqrt(jnp.mean(attended * attended, axis=-1, keepdims=True) + 1e-05)
    normalized_output = ((attended * scale).reshape(rows, -1) * norm_gain).astype(jnp.bfloat16)
    return jnp.dot(normalized_output, output_weight, preferred_element_type=f32).astype(jnp.bfloat16)


def solution(mesh):
    count = mesh.shape["outer"] * mesh.shape["inner"]
    in_specs = (P(AXES, None), P(AXES, None), P(), P(), P(), P(), P())
    out_specs = P(AXES, None)
    body = lambda *args: shards(count, *args)
    return jax.shard_map(body, mesh=mesh, in_specs=in_specs, out_specs=out_specs, check_vma=False)
```

```python
import functools

import jax
import jax.numpy as jnp
from jax import lax
from jax.experimental import pallas as pl
from jax.sharding import PartitionSpec as P

AXES = ("outer", "inner")

LANES = 128


def intra_kernel(q_ref, k_ref, v_ref, cum_ref, cum_t_ref, o_ref, *, head_dim):
    f32 = jnp.float32
    pair = pl.program_id(0)
    group = LANES // head_dim
    rows = q_ref.shape[0]
    heads = cum_ref.shape[1]
    q = q_ref[...]
    k = k_ref[...]
    v = v_ref[...]
    lane_head = lax.broadcasted_iota(jnp.int32, q.shape, 1) // head_dim
    t_i = lax.broadcasted_iota(jnp.int32, (rows, rows), 0)
    s_i = lax.broadcasted_iota(jnp.int32, (rows, rows), 1)
    lower = s_i <= t_i
    cum = cum_ref[...]
    cum_t = cum_t_ref[...]
    col_head = lax.broadcasted_iota(jnp.int32, cum.shape, 1)
    row_head = lax.broadcasted_iota(jnp.int32, cum_t.shape, 0)
    out = None
    for j in range(group):
        head = pair * group + j
        mine = lane_head == j
        q_j = jnp.where(mine, q, jnp.zeros_like(q))
        scores = lax.dot_general(q_j, k, (((1,), (1,)), ((), ())), preferred_element_type=f32)
        col = jnp.sum(jnp.where(col_head == head, cum, 0.0), axis=1, keepdims=True)
        row = jnp.sum(jnp.where(row_head == head, cum_t, 0.0), axis=0, keepdims=True)
        diff = jnp.where(lower, col - row, 0.0)
        decay = jnp.where(lower, jnp.exp(diff), 0.0)
        weights = (scores * decay).astype(jnp.bfloat16)
        o_j = jnp.dot(weights, v, preferred_element_type=f32)
        out = o_j if out is None else jnp.where(mine, o_j, out)
    o_ref[...] = out


def intra_attention(queries, keys, value_rows, cum, head_dim):
    rows, width = queries.shape
    heads = cum.shape[1]
    block = pl.BlockSpec((rows, LANES), lambda p: (0, p))
    whole = lambda shape: pl.BlockSpec(shape, lambda p: (0, 0))
    flops = 4 * rows * rows * LANES * (LANES // head_dim) * (width // LANES)
    return pl.pallas_call(
        functools.partial(intra_kernel, head_dim=head_dim),
        grid=(width // LANES,),
        in_specs=[block, block, block, whole((rows, heads)), whole((heads, rows))],
        out_specs=block,
        out_shape=jax.ShapeDtypeStruct((rows, width), jnp.float32),
        cost_estimate=pl.CostEstimate(
            flops=flops, transcendentals=rows * rows * heads, bytes_accessed=rows * width * 10
        ),
    )(queries, keys, value_rows, cum, cum.T)


def combine(earlier, later):
    body = earlier.shape[1] - 8
    row = lax.broadcasted_iota(jnp.int32, earlier.shape, 1)
    scale = jnp.where(row < body, jnp.exp(later[:, body : body + 1, :]), 1.0)
    return scale * earlier + later


def exclusive_scan(own, count):
    flat = lax.axis_index(AXES)
    core = flat % 2
    chip = flat // 2
    chips = count // 2
    half = own.shape[0] // 2
    partner = [(i, i ^ 1) for i in range(count)]
    other = lax.ppermute(own, AXES, partner)
    pooled = jnp.where(core == 0, combine(own, other), combine(other, own))
    through = jnp.where(core == 0, pooled[:half], pooled[half:])
    before = jnp.zeros_like(through)
    received = []
    bit = 1
    while bit < chips:
        perm = [(i, i ^ (2 * bit)) for i in range(count)]
        got = lax.ppermute(through, AXES, perm)
        received.append(got)
        lower = (chip & bit) != 0
        before = jnp.where(lower, combine(got, before), before)
        bit *= 2
        if bit < chips:
            through = jnp.where(lower, combine(got, through), combine(through, got))
    swapped = lax.ppermute(before, AXES, partner)
    whole = jnp.where(
        core == 0, jnp.concatenate([before, swapped]), jnp.concatenate([swapped, before])
    )
    whole = jnp.where(core == 0, whole, combine(whole, other))
    return whole[:, :-8], received


def shards(count, tokens, log_decay, query_weight, key_weight, value_weight, norm_gain, output_weight):
    rows = tokens.shape[0]
    heads = log_decay.shape[1]
    f32 = jnp.float32
    keys = jax.nn.silu(jnp.dot(tokens, key_weight, preferred_element_type=f32)).astype(jnp.bfloat16)
    value_rows = jnp.dot(tokens, value_weight, preferred_element_type=f32).astype(jnp.bfloat16)
    keys = keys.reshape(rows, heads, -1)
    value_rows = value_rows.reshape(rows, heads, -1)
    cum = jnp.cumsum(log_decay, axis=0)
    last = cum[-1]
    scaled = (keys.astype(f32) * jnp.exp(last[None, :] - cum)[:, :, None]).astype(jnp.bfloat16)
    local = jnp.einsum("thd,the->hde", scaled, value_rows, preferred_element_type=f32)
    dim = local.shape[-1]
    group = LANES // dim
    pairs = heads // group
    side = local.reshape(pairs, group, dim, dim).transpose(0, 2, 1, 3).reshape(pairs, dim, LANES)
    logs = jnp.broadcast_to(jnp.repeat(last.reshape(pairs, group), dim, axis=1)[:, None, :], (pairs, 8, LANES))
    logs = jnp.where(lax.broadcasted_iota(jnp.int32, logs.shape, 1) == 0, logs, 0.0)
    packed = jnp.concatenate([side, logs], axis=1)
    incoming, received = exclusive_scan(packed, count)
    incoming = incoming.reshape(pairs, dim, group, dim).transpose(0, 2, 1, 3).reshape(local.shape)
    gate = lambda value, round_: lax.optimization_barrier((value, received[min(round_, len(received) - 1)]))[0]

    queries = jax.nn.silu(
        jnp.dot(gate(tokens, 0), query_weight, preferred_element_type=f32)
    ).astype(jnp.bfloat16)
    intra = intra_attention(
        gate(queries, 1), keys.reshape(rows, -1), value_rows.reshape(rows, -1), cum, keys.shape[-1]
    ).reshape(rows, heads, -1)
    queries = queries.reshape(rows, heads, -1)

    qfloat = queries.astype(f32)
    inter = (
        jnp.einsum("thd,hde->the", qfloat, incoming, precision=lax.Precision.HIGHEST)
        * jnp.exp(cum)[:, :, None]
    )
    attended = intra + inter
    scale = lax.rsqrt(jnp.mean(attended * attended, axis=-1, keepdims=True) + 1e-05)
    normalized_output = ((attended * scale).reshape(rows, -1) * norm_gain).astype(jnp.bfloat16)
    return jnp.dot(normalized_output, output_weight, preferred_element_type=f32).astype(jnp.bfloat16)


def solution(mesh):
    count = mesh.shape["outer"] * mesh.shape["inner"]
    in_specs = (P(AXES, None), P(AXES, None), P(), P(), P(), P(), P())
    out_specs = P(AXES, None)
    body = lambda *args: shards(count, *args)
    return jax.shard_map(body, mesh=mesh, in_specs=in_specs, out_specs=out_specs, check_vma=False)
```

```python
import functools

import jax
import jax.numpy as jnp
from jax import lax
from jax.experimental import pallas as pl
from jax.sharding import PartitionSpec as P


AXES = ("outer", "inner")

LANES = 128


def intra_kernel(q_ref, k_ref, v_ref, cum_ref, cum_t_ref, o_ref, *, head_dim, first):
    f32 = jnp.float32
    pair = pl.program_id(0) + first
    group = LANES // head_dim
    rows = q_ref.shape[0]
    q = q_ref[...]
    k = k_ref[...]
    v = v_ref[...]
    lane_head = lax.broadcasted_iota(jnp.int32, q.shape, 1) // head_dim
    t_i = lax.broadcasted_iota(jnp.int32, (rows, rows), 0)
    s_i = lax.broadcasted_iota(jnp.int32, (rows, rows), 1)
    lower = s_i <= t_i
    cum = cum_ref[...]
    cum_t = cum_t_ref[...]
    col_head = lax.broadcasted_iota(jnp.int32, cum.shape, 1)
    row_head = lax.broadcasted_iota(jnp.int32, cum_t.shape, 0)
    out = None
    for j in range(group):
        head = pair * group + j
        mine = lane_head == j
        q_j = jnp.where(mine, q, jnp.zeros_like(q))
        scores = lax.dot_general(q_j, k, (((1,), (1,)), ((), ())), preferred_element_type=f32)
        col = jnp.sum(jnp.where(col_head == head, cum, 0.0), axis=1, keepdims=True)
        row = jnp.sum(jnp.where(row_head == head, cum_t, 0.0), axis=0, keepdims=True)
        diff = jnp.where(lower, col - row, 0.0)
        decay = jnp.where(lower, jnp.exp(diff), 0.0)
        weights = (scores * decay).astype(jnp.bfloat16)
        o_j = jnp.dot(weights, v, preferred_element_type=f32)
        out = o_j if out is None else jnp.where(mine, o_j, out)
    o_ref[...] = out


def intra_attention(queries, keys, value_rows, cum, head_dim, first, stop):
    rows, _ = queries.shape
    heads = cum.shape[1]
    block = pl.BlockSpec((rows, LANES), lambda p: (0, p + first))
    out_block = pl.BlockSpec((rows, LANES), lambda p: (0, p))
    whole = lambda shape: pl.BlockSpec(shape, lambda p: (0, 0))
    steps = stop - first
    flops = 4 * rows * rows * LANES * (LANES // head_dim) * steps
    return pl.pallas_call(
        functools.partial(intra_kernel, head_dim=head_dim, first=first),
        grid=(steps,),
        in_specs=[block, block, block, whole((rows, heads)), whole((heads, rows))],
        out_specs=out_block,
        out_shape=jax.ShapeDtypeStruct((rows, steps * LANES), jnp.float32),
        cost_estimate=pl.CostEstimate(
            flops=flops,
            transcendentals=rows * rows * steps * (LANES // head_dim),
            bytes_accessed=rows * steps * LANES * 10,
        ),
    )(queries, keys, value_rows, cum, cum.T)


def combine(earlier, later):
    body = earlier.shape[1] - 8
    row = lax.broadcasted_iota(jnp.int32, earlier.shape, 1)
    scale = jnp.where(row < body, jnp.exp(later[:, body : body + 1, :]), 1.0)
    return scale * earlier + later


def exclusive_scan(own, count):
    flat = lax.axis_index(AXES)
    core = flat % 2
    chip = flat // 2
    chips = count // 2
    half = own.shape[0] // 2
    partner = [(i, i ^ 1) for i in range(count)]
    other = lax.ppermute(own, AXES, partner)
    pooled = jnp.where(core == 0, combine(own, other), combine(other, own))
    through = jnp.where(core == 0, pooled[:half], pooled[half:])
    before = jnp.zeros_like(through)
    received = []
    bit = 1
    while bit < chips:
        perm = [(i, i ^ (2 * bit)) for i in range(count)]
        got = lax.ppermute(through, AXES, perm)
        received.append(got)
        lower = (chip & bit) != 0
        before = jnp.where(lower, combine(got, before), before)
        bit *= 2
        if bit < chips:
            through = jnp.where(lower, combine(got, through), combine(through, got))
    swapped = lax.ppermute(before, AXES, partner)
    whole = jnp.where(
        core == 0, jnp.concatenate([before, swapped]), jnp.concatenate([swapped, before])
    )
    whole = jnp.where(core == 0, whole, combine(whole, other))
    return whole[:, :-8], received


def layer(count, tokens, log_decay, query_weight, key_weight, value_weight, norm_gain, output_weight):
    rows = tokens.shape[0]
    heads = log_decay.shape[1]
    f32 = jnp.float32
    keys = jax.nn.silu(jnp.dot(tokens, key_weight, preferred_element_type=f32)).astype(jnp.bfloat16)
    value_rows = jnp.dot(tokens, value_weight, preferred_element_type=f32).astype(jnp.bfloat16)
    keys = keys.reshape(rows, heads, -1)
    value_rows = value_rows.reshape(rows, heads, -1)
    cum = jnp.cumsum(log_decay, axis=0)
    last = cum[-1]
    scaled = (keys.astype(f32) * jnp.exp(last[None, :] - cum)[:, :, None]).astype(jnp.bfloat16)
    local = jnp.einsum("thd,the->hde", scaled, value_rows, preferred_element_type=f32)
    dim = local.shape[-1]
    group = LANES // dim
    pairs = heads // group
    side = local.reshape(pairs, group, dim, dim).transpose(0, 2, 1, 3).reshape(pairs, dim, LANES)
    logs = jnp.broadcast_to(jnp.repeat(last.reshape(pairs, group), dim, axis=1)[:, None, :], (pairs, 8, LANES))
    logs = jnp.where(lax.broadcasted_iota(jnp.int32, logs.shape, 1) == 0, logs, 0.0)
    packed = jnp.concatenate([side, logs], axis=1)
    incoming, _ = exclusive_scan(packed, count)
    incoming = incoming.reshape(pairs, dim, group, dim).transpose(0, 2, 1, 3).reshape(local.shape)
    queries = jax.nn.silu(
        jnp.dot(tokens, query_weight, preferred_element_type=f32)
    ).astype(jnp.bfloat16)
    flat_k, flat_v = keys.reshape(rows, -1), value_rows.reshape(rows, -1)
    blocks = flat_k.shape[1] // LANES
    parts = []
    for first, stop in ((0, blocks // 2), (blocks // 2, blocks)):
        parts.append(intra_attention(queries, flat_k, flat_v, cum, dim, first, stop))
    intra = jnp.concatenate(parts, axis=1).reshape(rows, heads, -1)
    queries = queries.reshape(rows, heads, -1)

    qfloat = queries.astype(f32)
    inter = (
        jnp.einsum("thd,hde->the", qfloat, incoming, precision=lax.Precision.HIGHEST)
        * jnp.exp(cum)[:, :, None]
    )
    attended = intra + inter
    scale = lax.rsqrt(jnp.mean(attended * attended, axis=-1, keepdims=True) + 1e-05)
    normalized_output = ((attended * scale).reshape(rows, -1) * norm_gain).astype(jnp.bfloat16)
    return jnp.dot(normalized_output, output_weight, preferred_element_type=f32).astype(jnp.bfloat16)


def solution(mesh):
    count = mesh.shape["outer"] * mesh.shape["inner"]
    in_specs = (P(AXES, None), P(AXES, None), P(), P(), P(), P(), P())
    out_specs = P(AXES, None)
    body = lambda *args: layer(count, *args)
    return jax.shard_map(body, mesh=mesh, in_specs=in_specs, out_specs=out_specs, check_vma=False)
```

```python
import functools

import jax
import jax.numpy as jnp
from jax import lax
from jax.experimental import pallas as pl
from jax.sharding import PartitionSpec as P


AXES = ("outer", "inner")

LANES = 128


def intra_kernel(q_ref, k_ref, v_ref, cum_ref, cum_t_ref, *rest, head_dim, first):
    o_ref = rest[-1]
    f32 = jnp.float32
    pair = pl.program_id(0) + first
    group = LANES // head_dim
    rows = q_ref.shape[0]
    q = q_ref[...]
    k = k_ref[...]
    v = v_ref[...]
    lane_head = lax.broadcasted_iota(jnp.int32, q.shape, 1) // head_dim
    t_i = lax.broadcasted_iota(jnp.int32, (rows, rows), 0)
    s_i = lax.broadcasted_iota(jnp.int32, (rows, rows), 1)
    lower = s_i <= t_i
    cum = cum_ref[...]
    cum_t = cum_t_ref[...]
    col_head = lax.broadcasted_iota(jnp.int32, cum.shape, 1)
    row_head = lax.broadcasted_iota(jnp.int32, cum_t.shape, 0)
    out = None
    for j in range(group):
        head = pair * group + j
        mine = lane_head == j
        q_j = jnp.where(mine, q, jnp.zeros_like(q))
        scores = lax.dot_general(q_j, k, (((1,), (1,)), ((), ())), preferred_element_type=f32)
        col = jnp.sum(jnp.where(col_head == head, cum, 0.0), axis=1, keepdims=True)
        row = jnp.sum(jnp.where(row_head == head, cum_t, 0.0), axis=0, keepdims=True)
        diff = jnp.where(lower, col - row, 0.0)
        decay = jnp.where(lower, jnp.exp(diff), 0.0)
        weights = (scores * decay).astype(jnp.bfloat16)
        o_j = jnp.dot(weights, v, preferred_element_type=f32)
        out = o_j if out is None else jnp.where(mine, o_j, out)
    o_ref[...] = out


def intra_attention(queries, keys, value_rows, cum, head_dim, first, stop, into=None):
    rows, width = queries.shape
    heads = cum.shape[1]
    block = pl.BlockSpec((rows, LANES), lambda p: (0, p + first))
    out_block = block
    extra = () if into is None else (into,)
    extra_specs = [] if into is None else [pl.BlockSpec(memory_space=pl.ANY)]
    whole = lambda shape: pl.BlockSpec(shape, lambda p: (0, 0))
    steps = stop - first
    flops = 4 * rows * rows * LANES * (LANES // head_dim) * steps
    return pl.pallas_call(
        functools.partial(intra_kernel, head_dim=head_dim, first=first),
        grid=(steps,),
        in_specs=[block, block, block, whole((rows, heads)), whole((heads, rows))] + extra_specs,
        out_specs=out_block,
        out_shape=jax.ShapeDtypeStruct((rows, width), jnp.float32),
        input_output_aliases={} if into is None else {5: 0},
        cost_estimate=pl.CostEstimate(
            flops=flops,
            transcendentals=rows * rows * steps * (LANES // head_dim),
            bytes_accessed=rows * steps * LANES * 10,
        ),
    )(queries, keys, value_rows, cum, cum.T, *extra)


def head_column(table, head):
    lane = lax.broadcasted_iota(jnp.int32, table.shape, 1)
    return jnp.sum(jnp.where(lane == head, table, 0.0), axis=1, keepdims=True)


def local_kernel(k_ref, v_ref, cum_ref, o_ref, *, head_dim):
    f32 = jnp.float32
    pair = pl.program_id(0)
    group = LANES // head_dim
    rows = k_ref.shape[0]
    cum = cum_ref[...]
    lane_head = lax.broadcasted_iota(jnp.int32, (rows, LANES), 1) // head_dim
    weight = jnp.zeros((rows, LANES), f32)
    logs = jnp.zeros((1, LANES), f32)
    for j in range(group):
        col = head_column(cum, pair * group + j)
        last = col[rows - 1 :, :]
        weight = jnp.where(lane_head == j, jnp.exp(last - col), weight)
        logs = jnp.where(lane_head[:1] == j, last, logs)
    scaled = (k_ref[...].astype(f32) * weight).astype(jnp.bfloat16)
    state = lax.dot_general(scaled, v_ref[...], (((0,), (0,)), ((), ())), preferred_element_type=f32)
    lane = lax.broadcasted_iota(jnp.int32, (head_dim, LANES), 1) // head_dim
    packed = state[:head_dim]
    for j in range(1, group):
        packed = jnp.where(lane == j, state[j * head_dim : (j + 1) * head_dim], packed)
    o_ref[0, :head_dim, :] = packed
    tail_row = lax.broadcasted_iota(jnp.int32, (8, LANES), 0)
    o_ref[0, head_dim:, :] = jnp.where(tail_row == 0, jnp.broadcast_to(logs, (8, LANES)), 0.0)


def local_states(keys, value_rows, cum, head_dim):
    rows, width = keys.shape
    heads = cum.shape[1]
    pairs = width // LANES
    block = pl.BlockSpec((rows, LANES), lambda p: (0, p))
    return pl.pallas_call(
        functools.partial(local_kernel, head_dim=head_dim),
        grid=(pairs,),
        in_specs=[block, block, pl.BlockSpec((rows, heads), lambda p: (0, 0))],
        out_specs=pl.BlockSpec((1, head_dim + 8, LANES), lambda p: (p, 0, 0)),
        out_shape=jax.ShapeDtypeStruct((pairs, head_dim + 8, LANES), jnp.float32),
        cost_estimate=pl.CostEstimate(
            flops=2 * rows * LANES * LANES * pairs, transcendentals=rows * heads, bytes_accessed=rows * width * 4
        ),
    )(keys, value_rows, cum)


def finish_kernel(q_ref, intra_ref, state_ref, cum_ref, gain_ref, o_ref, *, head_dim):
    f32 = jnp.float32
    bf16 = jnp.bfloat16
    pair = pl.program_id(0)
    group = LANES // head_dim
    rows = q_ref.shape[0]
    state = state_ref[0, :head_dim, :]
    tall = jnp.concatenate([state] * group, axis=0)
    r_head = lax.broadcasted_iota(jnp.int32, (LANES, LANES), 0) // head_dim
    c_head = lax.broadcasted_iota(jnp.int32, (LANES, LANES), 1) // head_dim
    block = jnp.where(r_head == c_head, tall, 0.0)
    q = q_ref[...]
    inter = jnp.zeros((rows, LANES), f32)
    rest = block
    for _ in range(3):
        part = rest.astype(bf16)
        inter = inter + jnp.dot(q, part, preferred_element_type=f32)
        rest = rest - part.astype(f32)
    cum = cum_ref[...]
    lane_head = lax.broadcasted_iota(jnp.int32, (rows, LANES), 1) // head_dim
    growth = jnp.zeros((rows, LANES), f32)
    for j in range(group):
        growth = jnp.where(lane_head == j, jnp.exp(head_column(cum, pair * group + j)), growth)
    attended = intra_ref[...] + inter * growth
    square = attended * attended
    scale = jnp.zeros((rows, LANES), f32)
    for j in range(group):
        mean = jnp.sum(jnp.where(lane_head == j, square, 0.0), axis=1, keepdims=True) / head_dim
        scale = jnp.where(lane_head == j, lax.rsqrt(mean + 1e-05), scale)
    o_ref[...] = (attended * scale * gain_ref[...]).astype(bf16)


def finish(queries, intra, states, cum, norm_gain, head_dim):
    rows, width = queries.shape
    heads = cum.shape[1]
    pairs = width // LANES
    block = pl.BlockSpec((rows, LANES), lambda p: (0, p))
    return pl.pallas_call(
        functools.partial(finish_kernel, head_dim=head_dim),
        grid=(pairs,),
        in_specs=[
            block,
            block,
            pl.BlockSpec((1,) + states.shape[1:], lambda p: (p, 0, 0)),
            pl.BlockSpec((rows, heads), lambda p: (0, 0)),
            pl.BlockSpec((1, LANES), lambda p: (0, p)),
        ],
        out_specs=block,
        out_shape=jax.ShapeDtypeStruct((rows, width), jnp.bfloat16),
        cost_estimate=pl.CostEstimate(
            flops=6 * rows * LANES * LANES * pairs, transcendentals=rows * heads * 2, bytes_accessed=rows * width * 8
        ),
    )(queries, intra, states, cum, norm_gain.reshape(1, width))


def combine(earlier, later):
    body = earlier.shape[1] - 8
    row = lax.broadcasted_iota(jnp.int32, earlier.shape, 1)
    scale = jnp.where(row < body, jnp.exp(later[:, body : body + 1, :]), 1.0)
    return scale * earlier + later


def exclusive_scan(own, count):
    flat = lax.axis_index(AXES)
    core = flat % 2
    chip = flat // 2
    chips = count // 2
    half = own.shape[0] // 2
    partner = [(i, i ^ 1) for i in range(count)]
    other = lax.ppermute(own, AXES, partner)
    pooled = jnp.where(core == 0, combine(own, other), combine(other, own))
    through = jnp.where(core == 0, pooled[:half], pooled[half:])
    before = jnp.zeros_like(through)
    received = []
    bit = 1
    while bit < chips:
        perm = [(i, i ^ (2 * bit)) for i in range(count)]
        got = lax.ppermute(through, AXES, perm)
        received.append(got)
        lower = (chip & bit) != 0
        before = jnp.where(lower, combine(got, before), before)
        bit *= 2
        if bit < chips:
            through = jnp.where(lower, combine(got, through), combine(through, got))
    swapped = lax.ppermute(before, AXES, partner)
    whole = jnp.where(
        core == 0, jnp.concatenate([before, swapped]), jnp.concatenate([swapped, before])
    )
    whole = jnp.where(core == 0, whole, combine(whole, other))
    return whole, received


def layer(count, tokens, log_decay, query_weight, key_weight, value_weight, norm_gain, output_weight):
    f32 = jnp.float32
    bf16 = jnp.bfloat16
    heads = log_decay.shape[1]
    dim = key_weight.shape[1] // heads
    keys = jax.nn.silu(jnp.dot(tokens, key_weight, preferred_element_type=f32)).astype(bf16)
    value_rows = jnp.dot(tokens, value_weight, preferred_element_type=f32).astype(bf16)
    cum = jnp.cumsum(log_decay, axis=0)
    packed = local_states(keys, value_rows, cum, dim)
    incoming, _ = exclusive_scan(packed, count)

    queries = jax.nn.silu(jnp.dot(tokens, query_weight, preferred_element_type=f32)).astype(bf16)
    blocks = keys.shape[1] // LANES
    intra = None
    for first, stop in ((0, blocks // 2), (blocks // 2, blocks)):
        intra = intra_attention(queries, keys, value_rows, cum, dim, first, stop, intra)
    normalized_output = finish(queries, intra, incoming, cum, norm_gain, dim)
    return jnp.dot(normalized_output, output_weight, preferred_element_type=f32).astype(bf16)


def solution(mesh):
    count = mesh.shape["outer"] * mesh.shape["inner"]
    in_specs = (P(AXES, None), P(AXES, None), P(), P(), P(), P(), P())
    out_specs = P(AXES, None)
    body = lambda *args: layer(count, *args)
    return jax.shard_map(body, mesh=mesh, in_specs=in_specs, out_specs=out_specs, check_vma=False)
```

```python
import functools

import jax
import jax.numpy as jnp
from jax import lax
from jax.experimental import pallas as pl
from jax.sharding import PartitionSpec as P


AXES = ("outer", "inner")

LANES = 128
PER_STEP = 4


def intra_kernel(q_ref, k_ref, v_ref, cum_ref, cum_t_ref, *rest, head_dim, first):
    o_ref = rest[-1]
    f32 = jnp.float32
    pair = pl.program_id(0) + first
    group = LANES // head_dim
    rows = q_ref.shape[0]
    q = q_ref[...]
    k = k_ref[...]
    v = v_ref[...]
    lane_head = lax.broadcasted_iota(jnp.int32, q.shape, 1) // head_dim
    t_i = lax.broadcasted_iota(jnp.int32, (rows, rows), 0)
    s_i = lax.broadcasted_iota(jnp.int32, (rows, rows), 1)
    lower = s_i <= t_i
    cum = cum_ref[...]
    cum_t = cum_t_ref[...]
    col_head = lax.broadcasted_iota(jnp.int32, cum.shape, 1)
    row_head = lax.broadcasted_iota(jnp.int32, cum_t.shape, 0)
    out = None
    for j in range(group):
        head = pair * group + j
        mine = lane_head == j
        q_j = jnp.where(mine, q, jnp.zeros_like(q))
        scores = lax.dot_general(q_j, k, (((1,), (1,)), ((), ())), preferred_element_type=f32)
        col = jnp.sum(jnp.where(col_head == head, cum, 0.0), axis=1, keepdims=True)
        row = jnp.sum(jnp.where(row_head == head, cum_t, 0.0), axis=0, keepdims=True)
        diff = jnp.where(lower, col - row, 0.0)
        decay = jnp.where(lower, jnp.exp(diff), 0.0)
        weights = (scores * decay).astype(jnp.bfloat16)
        o_j = jnp.dot(weights, v, preferred_element_type=f32)
        out = o_j if out is None else jnp.where(mine, o_j, out)
    o_ref[...] = out


def intra_attention(queries, keys, value_rows, cum, head_dim, first, stop, into=None):
    rows, width = queries.shape
    heads = cum.shape[1]
    block = pl.BlockSpec((rows, LANES), lambda p: (0, p + first))
    out_block = block
    extra = () if into is None else (into,)
    extra_specs = [] if into is None else [pl.BlockSpec(memory_space=pl.ANY)]
    whole = lambda shape: pl.BlockSpec(shape, lambda p: (0, 0))
    steps = stop - first
    flops = 4 * rows * rows * LANES * (LANES // head_dim) * steps
    return pl.pallas_call(
        functools.partial(intra_kernel, head_dim=head_dim, first=first),
        grid=(steps,),
        in_specs=[block, block, block, whole((rows, heads)), whole((heads, rows))] + extra_specs,
        out_specs=out_block,
        out_shape=jax.ShapeDtypeStruct((rows, width), jnp.float32),
        input_output_aliases={} if into is None else {5: 0},
        cost_estimate=pl.CostEstimate(
            flops=flops,
            transcendentals=rows * rows * steps * (LANES // head_dim),
            bytes_accessed=rows * steps * LANES * 10,
        ),
    )(queries, keys, value_rows, cum, cum.T, *extra)


def head_column(table, head):
    lane = lax.broadcasted_iota(jnp.int32, table.shape, 1)
    return jnp.sum(jnp.where(lane == head, table, 0.0), axis=1, keepdims=True)


def local_kernel(k_ref, v_ref, cum_ref, o_ref, *, head_dim):
    for step in range(o_ref.shape[0]):
        local_pair(k_ref, v_ref, cum_ref, o_ref, head_dim, step)


def local_pair(k_ref, v_ref, cum_ref, o_ref, head_dim, step):
    f32 = jnp.float32
    pair = pl.program_id(0) * o_ref.shape[0] + step
    cols = pl.ds(step * LANES, LANES)
    group = LANES // head_dim
    rows = k_ref.shape[0]
    cum = cum_ref[...]
    lane_head = lax.broadcasted_iota(jnp.int32, (rows, LANES), 1) // head_dim
    weight = jnp.zeros((rows, LANES), f32)
    logs = jnp.zeros((1, LANES), f32)
    for j in range(group):
        col = head_column(cum, pair * group + j)
        last = col[rows - 1 :, :]
        weight = jnp.where(lane_head == j, jnp.exp(last - col), weight)
        logs = jnp.where(lane_head[:1] == j, last, logs)
    scaled = (k_ref[:, cols].astype(f32) * weight).astype(jnp.bfloat16)
    state = lax.dot_general(scaled, v_ref[:, cols], (((0,), (0,)), ((), ())), preferred_element_type=f32)
    lane = lax.broadcasted_iota(jnp.int32, (head_dim, LANES), 1) // head_dim
    packed = state[:head_dim]
    for j in range(1, group):
        packed = jnp.where(lane == j, state[j * head_dim : (j + 1) * head_dim], packed)
    o_ref[step, :head_dim, :] = packed
    tail_row = lax.broadcasted_iota(jnp.int32, (8, LANES), 0)
    o_ref[step, head_dim:, :] = jnp.where(tail_row == 0, jnp.broadcast_to(logs, (8, LANES)), 0.0)


def local_states(keys, value_rows, cum, head_dim):
    rows, width = keys.shape
    heads = cum.shape[1]
    pairs = width // LANES
    per = PER_STEP if pairs % PER_STEP == 0 else 1
    block = pl.BlockSpec((rows, per * LANES), lambda p: (0, p))
    return pl.pallas_call(
        functools.partial(local_kernel, head_dim=head_dim),
        grid=(pairs // per,),
        in_specs=[block, block, pl.BlockSpec((rows, heads), lambda p: (0, 0))],
        out_specs=pl.BlockSpec((per, head_dim + 8, LANES), lambda p: (p, 0, 0)),
        out_shape=jax.ShapeDtypeStruct((pairs, head_dim + 8, LANES), jnp.float32),
        cost_estimate=pl.CostEstimate(
            flops=2 * rows * LANES * LANES * pairs, transcendentals=rows * heads, bytes_accessed=rows * width * 4
        ),
    )(keys, value_rows, cum)


def finish_kernel(q_ref, intra_ref, state_ref, cum_ref, gain_ref, o_ref, *, head_dim):
    for step in range(state_ref.shape[0]):
        finish_pair(q_ref, intra_ref, state_ref, cum_ref, gain_ref, o_ref, head_dim, step)


def finish_pair(q_ref, intra_ref, state_ref, cum_ref, gain_ref, o_ref, head_dim, step):
    f32 = jnp.float32
    bf16 = jnp.bfloat16
    pair = pl.program_id(0) * state_ref.shape[0] + step
    cols = pl.ds(step * LANES, LANES)
    group = LANES // head_dim
    rows = q_ref.shape[0]
    state = state_ref[step, :head_dim, :]
    tall = jnp.concatenate([state] * group, axis=0)
    r_head = lax.broadcasted_iota(jnp.int32, (LANES, LANES), 0) // head_dim
    c_head = lax.broadcasted_iota(jnp.int32, (LANES, LANES), 1) // head_dim
    block = jnp.where(r_head == c_head, tall, 0.0)
    q = q_ref[:, cols]
    inter = jnp.zeros((rows, LANES), f32)
    rest = block
    for _ in range(3):
        part = rest.astype(bf16)
        inter = inter + jnp.dot(q, part, preferred_element_type=f32)
        rest = rest - part.astype(f32)
    cum = cum_ref[...]
    lane_head = lax.broadcasted_iota(jnp.int32, (rows, LANES), 1) // head_dim
    growth = jnp.zeros((rows, LANES), f32)
    for j in range(group):
        growth = jnp.where(lane_head == j, jnp.exp(head_column(cum, pair * group + j)), growth)
    attended = intra_ref[:, cols] + inter * growth
    square = attended * attended
    scale = jnp.zeros((rows, LANES), f32)
    for j in range(group):
        mean = jnp.sum(jnp.where(lane_head == j, square, 0.0), axis=1, keepdims=True) / head_dim
        scale = jnp.where(lane_head == j, lax.rsqrt(mean + 1e-05), scale)
    o_ref[:, cols] = (attended * scale * gain_ref[:, cols]).astype(bf16)


def finish(queries, intra, states, cum, norm_gain, head_dim):
    rows, width = queries.shape
    heads = cum.shape[1]
    pairs = width // LANES
    per = PER_STEP if pairs % PER_STEP == 0 else 1
    block = pl.BlockSpec((rows, per * LANES), lambda p: (0, p))
    return pl.pallas_call(
        functools.partial(finish_kernel, head_dim=head_dim),
        grid=(pairs // per,),
        in_specs=[
            block,
            block,
            pl.BlockSpec((per,) + states.shape[1:], lambda p: (p, 0, 0)),
            pl.BlockSpec((rows, heads), lambda p: (0, 0)),
            pl.BlockSpec((1, per * LANES), lambda p: (0, p)),
        ],
        out_specs=block,
        out_shape=jax.ShapeDtypeStruct((rows, width), jnp.bfloat16),
        cost_estimate=pl.CostEstimate(
            flops=6 * rows * LANES * LANES * pairs, transcendentals=rows * heads * 2, bytes_accessed=rows * width * 8
        ),
    )(queries, intra, states, cum, norm_gain.reshape(1, width))


def combine(earlier, later):
    body = earlier.shape[1] - 8
    row = lax.broadcasted_iota(jnp.int32, earlier.shape, 1)
    scale = jnp.where(row < body, jnp.exp(later[:, body : body + 1, :]), 1.0)
    return scale * earlier + later


def exclusive_scan(own, count):
    flat = lax.axis_index(AXES)
    core = flat % 2
    chip = flat // 2
    chips = count // 2
    half = own.shape[0] // 2
    partner = [(i, i ^ 1) for i in range(count)]
    other = lax.ppermute(own, AXES, partner)
    pooled = jnp.where(core == 0, combine(own, other), combine(other, own))
    through = jnp.where(core == 0, pooled[:half], pooled[half:])
    before = jnp.zeros_like(through)
    received = []
    bit = 1
    while bit < chips:
        perm = [(i, i ^ (2 * bit)) for i in range(count)]
        got = lax.ppermute(through, AXES, perm)
        received.append(got)
        lower = (chip & bit) != 0
        before = jnp.where(lower, combine(got, before), before)
        bit *= 2
        if bit < chips:
            through = jnp.where(lower, combine(got, through), combine(through, got))
    swapped = lax.ppermute(before, AXES, partner)
    whole = jnp.where(
        core == 0, jnp.concatenate([before, swapped]), jnp.concatenate([swapped, before])
    )
    whole = jnp.where(core == 0, whole, combine(whole, other))
    return whole, received


def layer(count, tokens, log_decay, query_weight, key_weight, value_weight, norm_gain, output_weight):
    f32 = jnp.float32
    bf16 = jnp.bfloat16
    heads = log_decay.shape[1]
    dim = key_weight.shape[1] // heads
    keys = jax.nn.silu(jnp.dot(tokens, key_weight, preferred_element_type=f32)).astype(bf16)
    value_rows = jnp.dot(tokens, value_weight, preferred_element_type=f32).astype(bf16)
    cum = jnp.cumsum(log_decay, axis=0)
    packed = local_states(keys, value_rows, cum, dim)
    incoming, _ = exclusive_scan(packed, count)

    queries = jax.nn.silu(jnp.dot(tokens, query_weight, preferred_element_type=f32)).astype(bf16)
    blocks = keys.shape[1] // LANES
    intra = None
    for first, stop in ((0, blocks // 2), (blocks // 2, blocks)):
        intra = intra_attention(queries, keys, value_rows, cum, dim, first, stop, intra)
    normalized_output = finish(queries, intra, incoming, cum, norm_gain, dim)
    return jnp.dot(normalized_output, output_weight, preferred_element_type=f32).astype(bf16)


def solution(mesh):
    count = mesh.shape["outer"] * mesh.shape["inner"]
    in_specs = (P(AXES, None), P(AXES, None), P(), P(), P(), P(), P())
    out_specs = P(AXES, None)
    body = lambda *args: layer(count, *args)
    return jax.shard_map(body, mesh=mesh, in_specs=in_specs, out_specs=out_specs, check_vma=False)
```

```python
import functools

import jax
import jax.numpy as jnp
from jax import lax
from jax.experimental import pallas as pl
from jax.sharding import PartitionSpec as P


AXES = ("outer", "inner")

LANES = 128
PER_STEP = 4


def intra_kernel(q_ref, k_ref, v_ref, cum_ref, cum_t_ref, *rest, head_dim, first):
    o_ref = rest[-1]
    f32 = jnp.float32
    pair = pl.program_id(0) + first
    group = LANES // head_dim
    rows = q_ref.shape[0]
    q = q_ref[...]
    k = k_ref[...]
    v = v_ref[...]
    lane_head = lax.broadcasted_iota(jnp.int32, q.shape, 1) // head_dim
    t_i = lax.broadcasted_iota(jnp.int32, (rows, rows), 0)
    s_i = lax.broadcasted_iota(jnp.int32, (rows, rows), 1)
    lower = s_i <= t_i
    cum = cum_ref[...]
    cum_t = cum_t_ref[...]
    col_head = lax.broadcasted_iota(jnp.int32, cum.shape, 1)
    row_head = lax.broadcasted_iota(jnp.int32, cum_t.shape, 0)
    out = None
    for j in range(group):
        head = pair * group + j
        mine = lane_head == j
        q_j = jnp.where(mine, q, jnp.zeros_like(q))
        scores = lax.dot_general(q_j, k, (((1,), (1,)), ((), ())), preferred_element_type=f32)
        col = jnp.sum(jnp.where(col_head == head, cum, 0.0), axis=1, keepdims=True)
        row = jnp.sum(jnp.where(row_head == head, cum_t, 0.0), axis=0, keepdims=True)
        diff = jnp.where(lower, col - row, 0.0)
        decay = jnp.where(lower, jnp.exp(diff), 0.0)
        weights = (scores * decay).astype(jnp.bfloat16)
        o_j = jnp.dot(weights, v, preferred_element_type=f32)
        out = o_j if out is None else jnp.where(mine, o_j, out)
    o_ref[...] = out


def intra_attention(queries, keys, value_rows, cum, head_dim, first, stop, into=None):
    rows, width = queries.shape
    heads = cum.shape[1]
    block = pl.BlockSpec((rows, LANES), lambda p: (0, p + first))
    out_block = block
    extra = () if into is None else (into,)
    extra_specs = [] if into is None else [pl.BlockSpec(memory_space=pl.ANY)]
    whole = lambda shape: pl.BlockSpec(shape, lambda p: (0, 0))
    steps = stop - first
    flops = 4 * rows * rows * LANES * (LANES // head_dim) * steps
    return pl.pallas_call(
        functools.partial(intra_kernel, head_dim=head_dim, first=first),
        grid=(steps,),
        in_specs=[block, block, block, whole((rows, heads)), whole((heads, rows))] + extra_specs,
        out_specs=out_block,
        out_shape=jax.ShapeDtypeStruct((rows, width), jnp.float32),
        input_output_aliases={} if into is None else {5: 0},
        cost_estimate=pl.CostEstimate(
            flops=flops,
            transcendentals=rows * rows * steps * (LANES // head_dim),
            bytes_accessed=rows * steps * LANES * 10,
        ),
    )(queries, keys, value_rows, cum, cum.T, *extra)


def head_column(table, head):
    lane = lax.broadcasted_iota(jnp.int32, table.shape, 1)
    return jnp.sum(jnp.where(lane == head, table, 0.0), axis=1, keepdims=True)


def local_pair(k_ref, v_ref, cum_ref, o_ref, head_dim, step):
    f32 = jnp.float32
    pair = pl.program_id(0) * o_ref.shape[0] + step
    cols = pl.ds(step * LANES, LANES)
    group = LANES // head_dim
    rows = k_ref.shape[0]
    cum = cum_ref[...]
    lane_head = lax.broadcasted_iota(jnp.int32, (rows, LANES), 1) // head_dim
    weight = jnp.zeros((rows, LANES), f32)
    logs = jnp.zeros((1, LANES), f32)
    for j in range(group):
        col = head_column(cum, pair * group + j)
        last = col[rows - 1 :, :]
        weight = jnp.where(lane_head == j, jnp.exp(last - col), weight)
        logs = jnp.where(lane_head[:1] == j, last, logs)
    scaled = (k_ref[:, cols].astype(f32) * weight).astype(jnp.bfloat16)
    state = lax.dot_general(scaled, v_ref[:, cols], (((0,), (0,)), ((), ())), preferred_element_type=f32)
    lane = lax.broadcasted_iota(jnp.int32, (head_dim, LANES), 1) // head_dim
    packed = state[:head_dim]
    for j in range(1, group):
        packed = jnp.where(lane == j, state[j * head_dim : (j + 1) * head_dim], packed)
    o_ref[step, :head_dim, :] = packed
    tail_row = lax.broadcasted_iota(jnp.int32, (8, LANES), 0)
    o_ref[step, head_dim:, :] = jnp.where(tail_row == 0, jnp.broadcast_to(logs, (8, LANES)), 0.0)


def project_kernel(x_ref, wk_ref, wv_ref, cum_ref, k_ref, v_ref, o_ref, *, head_dim):
    f32 = jnp.float32
    x = x_ref[...]
    key_sum = jnp.dot(x, wk_ref[...], preferred_element_type=f32)
    k_ref[...] = (key_sum / (1.0 + jnp.exp(-key_sum))).astype(jnp.bfloat16)
    v_ref[...] = jnp.dot(x, wv_ref[...], preferred_element_type=f32).astype(jnp.bfloat16)
    for step in range(o_ref.shape[0]):
        local_pair(k_ref, v_ref, cum_ref, o_ref, head_dim, step)


def project_keys_values(tokens, key_weight, value_weight, cum, head_dim):
    rows, depth = tokens.shape
    width = key_weight.shape[1]
    heads = cum.shape[1]
    pairs = width // LANES
    per = 2 if pairs % 2 == 0 else 1
    block = pl.BlockSpec((rows, per * LANES), lambda p: (0, p))
    weights = pl.BlockSpec((depth, per * LANES), lambda p: (0, p))
    return pl.pallas_call(
        functools.partial(project_kernel, head_dim=head_dim),
        grid=(pairs // per,),
        in_specs=[pl.BlockSpec((rows, depth), lambda p: (0, 0)), weights, weights, pl.BlockSpec((rows, heads), lambda p: (0, 0))],
        out_specs=[block, block, pl.BlockSpec((per, head_dim + 8, LANES), lambda p: (p, 0, 0))],
        out_shape=[
            jax.ShapeDtypeStruct((rows, width), jnp.bfloat16),
            jax.ShapeDtypeStruct((rows, width), jnp.bfloat16),
            jax.ShapeDtypeStruct((pairs, head_dim + 8, LANES), jnp.float32),
        ],
        cost_estimate=pl.CostEstimate(
            flops=4 * rows * depth * width + 2 * rows * LANES * width,
            transcendentals=rows * width + rows * heads,
            bytes_accessed=2 * depth * width * 2 + rows * depth * 2 + rows * width * 4,
        ),
    )(tokens, key_weight, value_weight, cum)


def finish_kernel(q_ref, intra_ref, state_ref, cum_ref, gain_ref, o_ref, *, head_dim):
    for step in range(state_ref.shape[0]):
        finish_pair(q_ref, intra_ref, state_ref, cum_ref, gain_ref, o_ref, head_dim, step)


def finish_pair(q_ref, intra_ref, state_ref, cum_ref, gain_ref, o_ref, head_dim, step):
    f32 = jnp.float32
    bf16 = jnp.bfloat16
    pair = pl.program_id(0) * state_ref.shape[0] + step
    cols = pl.ds(step * LANES, LANES)
    group = LANES // head_dim
    rows = q_ref.shape[0]
    state = state_ref[step, :head_dim, :]
    tall = jnp.concatenate([state] * group, axis=0)
    r_head = lax.broadcasted_iota(jnp.int32, (LANES, LANES), 0) // head_dim
    c_head = lax.broadcasted_iota(jnp.int32, (LANES, LANES), 1) // head_dim
    block = jnp.where(r_head == c_head, tall, 0.0)
    q = q_ref[:, cols]
    inter = jnp.zeros((rows, LANES), f32)
    rest = block
    for _ in range(3):
        part = rest.astype(bf16)
        inter = inter + jnp.dot(q, part, preferred_element_type=f32)
        rest = rest - part.astype(f32)
    cum = cum_ref[...]
    lane_head = lax.broadcasted_iota(jnp.int32, (rows, LANES), 1) // head_dim
    growth = jnp.zeros((rows, LANES), f32)
    for j in range(group):
        growth = jnp.where(lane_head == j, jnp.exp(head_column(cum, pair * group + j)), growth)
    attended = intra_ref[:, cols] + inter * growth
    square = attended * attended
    scale = jnp.zeros((rows, LANES), f32)
    for j in range(group):
        mean = jnp.sum(jnp.where(lane_head == j, square, 0.0), axis=1, keepdims=True) / head_dim
        scale = jnp.where(lane_head == j, lax.rsqrt(mean + 1e-05), scale)
    o_ref[:, cols] = (attended * scale * gain_ref[:, cols]).astype(bf16)


def finish(queries, intra, states, cum, norm_gain, head_dim):
    rows, width = queries.shape
    heads = cum.shape[1]
    pairs = width // LANES
    per = PER_STEP if pairs % PER_STEP == 0 else 1
    block = pl.BlockSpec((rows, per * LANES), lambda p: (0, p))
    return pl.pallas_call(
        functools.partial(finish_kernel, head_dim=head_dim),
        grid=(pairs // per,),
        in_specs=[
            block,
            block,
            pl.BlockSpec((per,) + states.shape[1:], lambda p: (p, 0, 0)),
            pl.BlockSpec((rows, heads), lambda p: (0, 0)),
            pl.BlockSpec((1, per * LANES), lambda p: (0, p)),
        ],
        out_specs=block,
        out_shape=jax.ShapeDtypeStruct((rows, width), jnp.bfloat16),
        cost_estimate=pl.CostEstimate(
            flops=6 * rows * LANES * LANES * pairs, transcendentals=rows * heads * 2, bytes_accessed=rows * width * 8
        ),
    )(queries, intra, states, cum, norm_gain.reshape(1, width))


def combine(earlier, later):
    body = earlier.shape[1] - 8
    row = lax.broadcasted_iota(jnp.int32, earlier.shape, 1)
    scale = jnp.where(row < body, jnp.exp(later[:, body : body + 1, :]), 1.0)
    return scale * earlier + later


def exclusive_scan(own, count):
    flat = lax.axis_index(AXES)
    core = flat % 2
    chip = flat // 2
    chips = count // 2
    half = own.shape[0] // 2
    partner = [(i, i ^ 1) for i in range(count)]
    other = lax.ppermute(own, AXES, partner)
    pooled = jnp.where(core == 0, combine(own, other), combine(other, own))
    through = jnp.where(core == 0, pooled[:half], pooled[half:])
    before = jnp.zeros_like(through)
    received = []
    bit = 1
    while bit < chips:
        perm = [(i, i ^ (2 * bit)) for i in range(count)]
        got = lax.ppermute(through, AXES, perm)
        received.append(got)
        lower = (chip & bit) != 0
        before = jnp.where(lower, combine(got, before), before)
        bit *= 2
        if bit < chips:
            through = jnp.where(lower, combine(got, through), combine(through, got))
    swapped = lax.ppermute(before, AXES, partner)
    whole = jnp.where(
        core == 0, jnp.concatenate([before, swapped]), jnp.concatenate([swapped, before])
    )
    whole = jnp.where(core == 0, whole, combine(whole, other))
    return whole, received


def layer(count, tokens, log_decay, query_weight, key_weight, value_weight, norm_gain, output_weight):
    f32 = jnp.float32
    bf16 = jnp.bfloat16
    heads = log_decay.shape[1]
    dim = key_weight.shape[1] // heads
    cum = jnp.cumsum(log_decay, axis=0)
    keys, value_rows, packed = project_keys_values(tokens, key_weight, value_weight, cum, dim)
    incoming, _ = exclusive_scan(packed, count)

    queries = jax.nn.silu(jnp.dot(tokens, query_weight, preferred_element_type=f32)).astype(bf16)
    blocks = keys.shape[1] // LANES
    intra = None
    for first, stop in ((0, blocks // 2), (blocks // 2, blocks)):
        intra = intra_attention(queries, keys, value_rows, cum, dim, first, stop, intra)
    normalized_output = finish(queries, intra, incoming, cum, norm_gain, dim)
    return jnp.dot(normalized_output, output_weight, preferred_element_type=f32).astype(bf16)


def solution(mesh):
    count = mesh.shape["outer"] * mesh.shape["inner"]
    in_specs = (P(AXES, None), P(AXES, None), P(), P(), P(), P(), P())
    out_specs = P(AXES, None)
    body = lambda *args: layer(count, *args)
    return jax.shard_map(body, mesh=mesh, in_specs=in_specs, out_specs=out_specs, check_vma=False)
```

```python
import functools

import jax
import jax.numpy as jnp
from jax import lax
from jax.experimental import pallas as pl
from jax.experimental.pallas import tpu as pltpu
from jax.sharding import PartitionSpec as P


AXES = ("outer", "inner")

LANES = 128
PER_STEP = 4


def intra_kernel(q_ref, k_ref, v_ref, cum_ref, cum_t_ref, *rest, head_dim, first):
    o_ref = rest[-1]
    f32 = jnp.float32
    pair = pl.program_id(0) + first
    group = LANES // head_dim
    rows = q_ref.shape[0]
    q = q_ref[...]
    k = k_ref[...]
    v = v_ref[...]
    lane_head = lax.broadcasted_iota(jnp.int32, q.shape, 1) // head_dim
    t_i = lax.broadcasted_iota(jnp.int32, (rows, rows), 0)
    s_i = lax.broadcasted_iota(jnp.int32, (rows, rows), 1)
    lower = s_i <= t_i
    cum = cum_ref[...]
    cum_t = cum_t_ref[...]
    col_head = lax.broadcasted_iota(jnp.int32, cum.shape, 1)
    row_head = lax.broadcasted_iota(jnp.int32, cum_t.shape, 0)
    out = None
    for j in range(group):
        head = pair * group + j
        mine = lane_head == j
        q_j = jnp.where(mine, q, jnp.zeros_like(q))
        scores = lax.dot_general(q_j, k, (((1,), (1,)), ((), ())), preferred_element_type=f32)
        col = jnp.sum(jnp.where(col_head == head, cum, 0.0), axis=1, keepdims=True)
        row = jnp.sum(jnp.where(row_head == head, cum_t, 0.0), axis=0, keepdims=True)
        diff = jnp.where(lower, col - row, 0.0)
        decay = jnp.where(lower, jnp.exp(diff), 0.0)
        weights = (scores * decay).astype(jnp.bfloat16)
        o_j = jnp.dot(weights, v, preferred_element_type=f32)
        out = o_j if out is None else jnp.where(mine, o_j, out)
    o_ref[...] = out


def intra_attention(queries, keys, value_rows, cum, head_dim, first, stop, into=None):
    rows, width = queries.shape
    heads = cum.shape[1]
    block = pl.BlockSpec((rows, LANES), lambda p: (0, p + first))
    out_block = block
    extra = () if into is None else (into,)
    extra_specs = [] if into is None else [pl.BlockSpec(memory_space=pl.ANY)]
    whole = lambda shape: pl.BlockSpec(shape, lambda p: (0, 0))
    steps = stop - first
    flops = 4 * rows * rows * LANES * (LANES // head_dim) * steps
    return pl.pallas_call(
        functools.partial(intra_kernel, head_dim=head_dim, first=first),
        grid=(steps,),
        in_specs=[block, block, block, whole((rows, heads)), whole((heads, rows))] + extra_specs,
        out_specs=out_block,
        out_shape=jax.ShapeDtypeStruct((rows, width), jnp.float32),
        input_output_aliases={} if into is None else {5: 0},
        cost_estimate=pl.CostEstimate(
            flops=flops,
            transcendentals=rows * rows * steps * (LANES // head_dim),
            bytes_accessed=rows * steps * LANES * 10,
        ),
    )(queries, keys, value_rows, cum, cum.T, *extra)


def head_column(table, head):
    lane = lax.broadcasted_iota(jnp.int32, table.shape, 1)
    return jnp.sum(jnp.where(lane == head, table, 0.0), axis=1, keepdims=True)


def local_pair(k_ref, v_ref, cum_ref, o_ref, head_dim, step):
    f32 = jnp.float32
    pair = pl.program_id(0) * o_ref.shape[0] + step
    cols = pl.ds(step * LANES, LANES)
    group = LANES // head_dim
    rows = k_ref.shape[0]
    cum = cum_ref[...]
    lane_head = lax.broadcasted_iota(jnp.int32, (rows, LANES), 1) // head_dim
    weight = jnp.zeros((rows, LANES), f32)
    logs = jnp.zeros((1, LANES), f32)
    for j in range(group):
        col = head_column(cum, pair * group + j)
        last = col[rows - 1 :, :]
        weight = jnp.where(lane_head == j, jnp.exp(last - col), weight)
        logs = jnp.where(lane_head[:1] == j, last, logs)
    scaled = (k_ref[:, cols].astype(f32) * weight).astype(jnp.bfloat16)
    state = lax.dot_general(scaled, v_ref[:, cols], (((0,), (0,)), ((), ())), preferred_element_type=f32)
    lane = lax.broadcasted_iota(jnp.int32, (head_dim, LANES), 1) // head_dim
    packed = state[:head_dim]
    for j in range(1, group):
        packed = jnp.where(lane == j, state[j * head_dim : (j + 1) * head_dim], packed)
    o_ref[step, :head_dim, :] = packed
    tail_row = lax.broadcasted_iota(jnp.int32, (8, LANES), 0)
    o_ref[step, head_dim:, :] = jnp.where(tail_row == 0, jnp.broadcast_to(logs, (8, LANES)), 0.0)


def project_kernel(x_ref, wk_ref, wv_ref, cum_ref, k_ref, v_ref, o_ref, *, head_dim):
    f32 = jnp.float32
    x = x_ref[...]
    key_sum = jnp.dot(x, wk_ref[...], preferred_element_type=f32)
    k_ref[...] = (key_sum / (1.0 + jnp.exp(-key_sum))).astype(jnp.bfloat16)
    v_ref[...] = jnp.dot(x, wv_ref[...], preferred_element_type=f32).astype(jnp.bfloat16)
    for step in range(o_ref.shape[0]):
        local_pair(k_ref, v_ref, cum_ref, o_ref, head_dim, step)


def project_keys_values(tokens, key_weight, value_weight, cum, head_dim):
    rows, depth = tokens.shape
    width = key_weight.shape[1]
    heads = cum.shape[1]
    pairs = width // LANES
    per = 2 if pairs % 2 == 0 else 1
    block = pl.BlockSpec((rows, per * LANES), lambda p: (0, p))
    weights = pl.BlockSpec((depth, per * LANES), lambda p: (0, p))
    return pl.pallas_call(
        functools.partial(project_kernel, head_dim=head_dim),
        grid=(pairs // per,),
        in_specs=[pl.BlockSpec((rows, depth), lambda p: (0, 0)), weights, weights, pl.BlockSpec((rows, heads), lambda p: (0, 0))],
        out_specs=[block, block, pl.BlockSpec((per, head_dim + 8, LANES), lambda p: (p, 0, 0))],
        out_shape=[
            jax.ShapeDtypeStruct((rows, width), jnp.bfloat16),
            jax.ShapeDtypeStruct((rows, width), jnp.bfloat16),
            jax.ShapeDtypeStruct((pairs, head_dim + 8, LANES), jnp.float32),
        ],
        cost_estimate=pl.CostEstimate(
            flops=4 * rows * depth * width + 2 * rows * LANES * width,
            transcendentals=rows * width + rows * heads,
            bytes_accessed=2 * depth * width * 2 + rows * depth * 2 + rows * width * 4,
        ),
    )(tokens, key_weight, value_weight, cum)


def finish_kernel(q_ref, intra_ref, state_ref, cum_ref, gain_ref, w_ref, o_ref, normed_ref, acc_ref, *, head_dim):
    for step in range(state_ref.shape[0]):
        finish_pair(q_ref, intra_ref, state_ref, cum_ref, gain_ref, normed_ref, head_dim, step)
    part = jnp.dot(normed_ref[...], w_ref[...], preferred_element_type=jnp.float32)
    index = pl.program_id(0)

    @pl.when(index == 0)
    def _():
        acc_ref[...] = part

    @pl.when(index > 0)
    def _():
        acc_ref[...] += part

    @pl.when(index == pl.num_programs(0) - 1)
    def _():
        o_ref[...] = acc_ref[...].astype(o_ref.dtype)


def finish_pair(q_ref, intra_ref, state_ref, cum_ref, gain_ref, o_ref, head_dim, step):
    f32 = jnp.float32
    bf16 = jnp.bfloat16
    pair = pl.program_id(0) * state_ref.shape[0] + step
    cols = pl.ds(step * LANES, LANES)
    group = LANES // head_dim
    rows = q_ref.shape[0]
    state = state_ref[step, :head_dim, :]
    tall = jnp.concatenate([state] * group, axis=0)
    r_head = lax.broadcasted_iota(jnp.int32, (LANES, LANES), 0) // head_dim
    c_head = lax.broadcasted_iota(jnp.int32, (LANES, LANES), 1) // head_dim
    block = jnp.where(r_head == c_head, tall, 0.0)
    q = q_ref[:, cols]
    inter = jnp.zeros((rows, LANES), f32)
    rest = block
    for _ in range(3):
        part = rest.astype(bf16)
        inter = inter + jnp.dot(q, part, preferred_element_type=f32)
        rest = rest - part.astype(f32)
    cum = cum_ref[...]
    lane_head = lax.broadcasted_iota(jnp.int32, (rows, LANES), 1) // head_dim
    growth = jnp.zeros((rows, LANES), f32)
    for j in range(group):
        growth = jnp.where(lane_head == j, jnp.exp(head_column(cum, pair * group + j)), growth)
    attended = intra_ref[:, cols] + inter * growth
    square = attended * attended
    scale = jnp.zeros((rows, LANES), f32)
    for j in range(group):
        mean = jnp.sum(jnp.where(lane_head == j, square, 0.0), axis=1, keepdims=True) / head_dim
        scale = jnp.where(lane_head == j, lax.rsqrt(mean + 1e-05), scale)
    o_ref[:, cols] = (attended * scale * gain_ref[:, cols]).astype(bf16)


def finish(queries, intra, states, cum, norm_gain, output_weight, head_dim):
    rows, width = queries.shape
    heads = cum.shape[1]
    pairs = width // LANES
    out_width = output_weight.shape[1]
    per = PER_STEP if pairs % PER_STEP == 0 else 1
    block = pl.BlockSpec((rows, per * LANES), lambda p: (0, p))
    return pl.pallas_call(
        functools.partial(finish_kernel, head_dim=head_dim),
        grid=(pairs // per,),
        in_specs=[
            block,
            block,
            pl.BlockSpec((per,) + states.shape[1:], lambda p: (p, 0, 0)),
            pl.BlockSpec((rows, heads), lambda p: (0, 0)),
            pl.BlockSpec((1, per * LANES), lambda p: (0, p)),
            pl.BlockSpec((per * LANES, out_width), lambda p: (p, 0)),
        ],
        out_specs=pl.BlockSpec((rows, out_width), lambda p: (0, 0)),
        out_shape=jax.ShapeDtypeStruct((rows, out_width), jnp.bfloat16),
        scratch_shapes=[pltpu.VMEM((rows, per * LANES), jnp.bfloat16), pltpu.VMEM((rows, out_width), jnp.float32)],
        cost_estimate=pl.CostEstimate(
            flops=6 * rows * LANES * LANES * pairs + 2 * rows * width * out_width,
            transcendentals=rows * heads * 2,
            bytes_accessed=rows * width * 8 + width * out_width * 2,
        ),
    )(queries, intra, states, cum, norm_gain.reshape(1, width), output_weight)


def combine(earlier, later):
    body = earlier.shape[1] - 8
    row = lax.broadcasted_iota(jnp.int32, earlier.shape, 1)
    scale = jnp.where(row < body, jnp.exp(later[:, body : body + 1, :]), 1.0)
    return scale * earlier + later


def exclusive_scan(own, count):
    flat = lax.axis_index(AXES)
    core = flat % 2
    chip = flat // 2
    chips = count // 2
    half = own.shape[0] // 2
    partner = [(i, i ^ 1) for i in range(count)]
    other = lax.ppermute(own, AXES, partner)
    pooled = jnp.where(core == 0, combine(own, other), combine(other, own))
    through = jnp.where(core == 0, pooled[:half], pooled[half:])
    before = jnp.zeros_like(through)
    received = []
    bit = 1
    while bit < chips:
        perm = [(i, i ^ (2 * bit)) for i in range(count)]
        got = lax.ppermute(through, AXES, perm)
        received.append(got)
        lower = (chip & bit) != 0
        before = jnp.where(lower, combine(got, before), before)
        bit *= 2
        if bit < chips:
            through = jnp.where(lower, combine(got, through), combine(through, got))
    swapped = lax.ppermute(before, AXES, partner)
    whole = jnp.where(
        core == 0, jnp.concatenate([before, swapped]), jnp.concatenate([swapped, before])
    )
    whole = jnp.where(core == 0, whole, combine(whole, other))
    return whole, received


def layer(count, tokens, log_decay, query_weight, key_weight, value_weight, norm_gain, output_weight):
    f32 = jnp.float32
    bf16 = jnp.bfloat16
    heads = log_decay.shape[1]
    dim = key_weight.shape[1] // heads
    cum = jnp.cumsum(log_decay, axis=0)
    keys, value_rows, packed = project_keys_values(tokens, key_weight, value_weight, cum, dim)
    incoming, _ = exclusive_scan(packed, count)

    queries = jax.nn.silu(jnp.dot(tokens, query_weight, preferred_element_type=f32)).astype(bf16)
    blocks = keys.shape[1] // LANES
    intra = None
    for first, stop in ((0, blocks // 2), (blocks // 2, blocks)):
        intra = intra_attention(queries, keys, value_rows, cum, dim, first, stop, intra)
    return finish(queries, intra, incoming, cum, norm_gain, output_weight, dim)


def solution(mesh):
    count = mesh.shape["outer"] * mesh.shape["inner"]
    in_specs = (P(AXES, None), P(AXES, None), P(), P(), P(), P(), P())
    out_specs = P(AXES, None)
    body = lambda *args: layer(count, *args)
    return jax.shard_map(body, mesh=mesh, in_specs=in_specs, out_specs=out_specs, check_vma=False)
```

```python
import functools

import jax
import jax.numpy as jnp
from jax import lax
from jax.experimental import pallas as pl
from jax.experimental.pallas import tpu as pltpu
from jax.sharding import PartitionSpec as P


AXES = ("outer", "inner")

LANES = 128
PER_STEP = 4


def intra_kernel(q_ref, k_ref, v_ref, cum_ref, cum_t_ref, *rest, head_dim, first):
    o_ref = rest[-1]
    f32 = jnp.float32
    pair = pl.program_id(0) + first
    group = LANES // head_dim
    rows = q_ref.shape[0]
    q = q_ref[...]
    k = k_ref[...]
    v = v_ref[...]
    lane_head = lax.broadcasted_iota(jnp.int32, q.shape, 1) // head_dim
    t_i = lax.broadcasted_iota(jnp.int32, (rows, rows), 0)
    s_i = lax.broadcasted_iota(jnp.int32, (rows, rows), 1)
    lower = s_i <= t_i
    cum = cum_ref[...]
    cum_t = cum_t_ref[...]
    col_head = lax.broadcasted_iota(jnp.int32, cum.shape, 1)
    row_head = lax.broadcasted_iota(jnp.int32, cum_t.shape, 0)
    out = None
    for j in range(group):
        head = pair * group + j
        mine = lane_head == j
        q_j = jnp.where(mine, q, jnp.zeros_like(q))
        scores = lax.dot_general(q_j, k, (((1,), (1,)), ((), ())), preferred_element_type=f32)
        col = jnp.sum(jnp.where(col_head == head, cum, 0.0), axis=1, keepdims=True)
        row = jnp.sum(jnp.where(row_head == head, cum_t, 0.0), axis=0, keepdims=True)
        diff = jnp.where(lower, col - row, 0.0)
        decay = jnp.where(lower, jnp.exp(diff), 0.0)
        weights = (scores * decay).astype(jnp.bfloat16)
        o_j = jnp.dot(weights, v, preferred_element_type=f32)
        out = o_j if out is None else jnp.where(mine, o_j, out)
    o_ref[...] = out


def intra_attention(queries, keys, value_rows, cum, cum_t, head_dim, first, stop, into=None):
    rows, width = queries.shape
    heads = cum.shape[1]
    block = pl.BlockSpec((rows, LANES), lambda p: (0, p + first))
    out_block = block
    extra = () if into is None else (into,)
    extra_specs = [] if into is None else [pl.BlockSpec(memory_space=pl.ANY)]
    whole = lambda shape: pl.BlockSpec(shape, lambda p: (0, 0))
    steps = stop - first
    flops = 4 * rows * rows * LANES * (LANES // head_dim) * steps
    return pl.pallas_call(
        functools.partial(intra_kernel, head_dim=head_dim, first=first),
        grid=(steps,),
        in_specs=[block, block, block, whole((rows, heads)), whole((heads, rows))] + extra_specs,
        out_specs=out_block,
        out_shape=jax.ShapeDtypeStruct((rows, width), jnp.float32),
        input_output_aliases={} if into is None else {5: 0},
        cost_estimate=pl.CostEstimate(
            flops=flops,
            transcendentals=rows * rows * steps * (LANES // head_dim),
            bytes_accessed=rows * steps * LANES * 10,
        ),
    )(queries, keys, value_rows, cum, cum_t, *extra)


def head_column(table, head):
    lane = lax.broadcasted_iota(jnp.int32, table.shape, 1)
    return jnp.sum(jnp.where(lane == head, table, 0.0), axis=1, keepdims=True)


def local_pair(k_ref, v_ref, cum_ref, o_ref, head_dim, step):
    f32 = jnp.float32
    pair = pl.program_id(0) * o_ref.shape[0] + step
    cols = pl.ds(step * LANES, LANES)
    group = LANES // head_dim
    rows = k_ref.shape[0]
    cum = cum_ref[...]
    lane_head = lax.broadcasted_iota(jnp.int32, (rows, LANES), 1) // head_dim
    weight = jnp.zeros((rows, LANES), f32)
    logs = jnp.zeros((1, LANES), f32)
    for j in range(group):
        col = head_column(cum, pair * group + j)
        last = col[rows - 1 :, :]
        weight = jnp.where(lane_head == j, jnp.exp(last - col), weight)
        logs = jnp.where(lane_head[:1] == j, last, logs)
    scaled = (k_ref[:, cols].astype(f32) * weight).astype(jnp.bfloat16)
    state = lax.dot_general(scaled, v_ref[:, cols], (((0,), (0,)), ((), ())), preferred_element_type=f32)
    lane = lax.broadcasted_iota(jnp.int32, (head_dim, LANES), 1) // head_dim
    packed = state[:head_dim]
    for j in range(1, group):
        packed = jnp.where(lane == j, state[j * head_dim : (j + 1) * head_dim], packed)
    o_ref[step, :head_dim, :] = packed
    tail_row = lax.broadcasted_iota(jnp.int32, (8, LANES), 0)
    o_ref[step, head_dim:, :] = jnp.where(tail_row == 0, jnp.broadcast_to(logs, (8, LANES)), 0.0)


def project_kernel(x_ref, wk_ref, wv_ref, g_ref, k_ref, v_ref, o_ref, cum_ref, cum_t_ref, *, head_dim):
    f32 = jnp.float32
    bf16 = jnp.bfloat16
    rows = g_ref.shape[0]
    t_i = lax.broadcasted_iota(jnp.int32, (rows, rows), 0)
    s_i = lax.broadcasted_iota(jnp.int32, (rows, rows), 1)
    lower = jnp.where(s_i <= t_i, 1.0, 0.0).astype(bf16)
    upper = jnp.where(t_i <= s_i, 1.0, 0.0).astype(bf16)
    rest = g_ref[...]
    cum = jnp.zeros(cum_ref.shape, f32)
    cum_t = jnp.zeros(cum_t_ref.shape, f32)
    for _ in range(3):
        part = rest.astype(bf16)
        cum = cum + jnp.dot(lower, part, preferred_element_type=f32)
        cum_t = cum_t + lax.dot_general(part, upper, (((0,), (0,)), ((), ())), preferred_element_type=f32)
        rest = rest - part.astype(f32)
    cum_ref[...] = cum
    cum_t_ref[...] = cum_t
    x = x_ref[...]
    key_sum = jnp.dot(x, wk_ref[...], preferred_element_type=f32)
    k_ref[...] = (key_sum / (1.0 + jnp.exp(-key_sum))).astype(jnp.bfloat16)
    v_ref[...] = jnp.dot(x, wv_ref[...], preferred_element_type=f32).astype(jnp.bfloat16)
    for step in range(o_ref.shape[0]):
        local_pair(k_ref, v_ref, cum_ref, o_ref, head_dim, step)


def project_keys_values(tokens, key_weight, value_weight, log_decay, head_dim):
    rows, depth = tokens.shape
    width = key_weight.shape[1]
    heads = log_decay.shape[1]
    pairs = width // LANES
    per = 2 if pairs % 2 == 0 else 1
    block = pl.BlockSpec((rows, per * LANES), lambda p: (0, p))
    weights = pl.BlockSpec((depth, per * LANES), lambda p: (0, p))
    return pl.pallas_call(
        functools.partial(project_kernel, head_dim=head_dim),
        grid=(pairs // per,),
        in_specs=[pl.BlockSpec((rows, depth), lambda p: (0, 0)), weights, weights, pl.BlockSpec((rows, heads), lambda p: (0, 0))],
        out_specs=[
            block,
            block,
            pl.BlockSpec((per, head_dim + 8, LANES), lambda p: (p, 0, 0)),
            pl.BlockSpec((rows, heads), lambda p: (0, 0)),
            pl.BlockSpec((heads, rows), lambda p: (0, 0)),
        ],
        out_shape=[
            jax.ShapeDtypeStruct((rows, width), jnp.bfloat16),
            jax.ShapeDtypeStruct((rows, width), jnp.bfloat16),
            jax.ShapeDtypeStruct((pairs, head_dim + 8, LANES), jnp.float32),
            jax.ShapeDtypeStruct((rows, heads), jnp.float32),
            jax.ShapeDtypeStruct((heads, rows), jnp.float32),
        ],
        cost_estimate=pl.CostEstimate(
            flops=4 * rows * depth * width + 2 * rows * LANES * width,
            transcendentals=rows * width + rows * heads,
            bytes_accessed=2 * depth * width * 2 + rows * depth * 2 + rows * width * 4,
        ),
    )(tokens, key_weight, value_weight, log_decay)


def finish_kernel(q_ref, intra_ref, state_ref, cum_ref, gain_ref, w_ref, o_ref, normed_ref, acc_ref, *, head_dim):
    for step in range(state_ref.shape[0]):
        finish_pair(q_ref, intra_ref, state_ref, cum_ref, gain_ref, normed_ref, head_dim, step)
    part = jnp.dot(normed_ref[...], w_ref[...], preferred_element_type=jnp.float32)
    index = pl.program_id(0)

    @pl.when(index == 0)
    def _():
        acc_ref[...] = part

    @pl.when(index > 0)
    def _():
        acc_ref[...] += part

    @pl.when(index == pl.num_programs(0) - 1)
    def _():
        o_ref[...] = acc_ref[...].astype(o_ref.dtype)


def finish_pair(q_ref, intra_ref, state_ref, cum_ref, gain_ref, o_ref, head_dim, step):
    f32 = jnp.float32
    bf16 = jnp.bfloat16
    pair = pl.program_id(0) * state_ref.shape[0] + step
    cols = pl.ds(step * LANES, LANES)
    group = LANES // head_dim
    rows = q_ref.shape[0]
    state = state_ref[step, :head_dim, :]
    tall = jnp.concatenate([state] * group, axis=0)
    r_head = lax.broadcasted_iota(jnp.int32, (LANES, LANES), 0) // head_dim
    c_head = lax.broadcasted_iota(jnp.int32, (LANES, LANES), 1) // head_dim
    block = jnp.where(r_head == c_head, tall, 0.0)
    q = q_ref[:, cols]
    inter = jnp.zeros((rows, LANES), f32)
    rest = block
    for _ in range(3):
        part = rest.astype(bf16)
        inter = inter + jnp.dot(q, part, preferred_element_type=f32)
        rest = rest - part.astype(f32)
    cum = cum_ref[...]
    lane_head = lax.broadcasted_iota(jnp.int32, (rows, LANES), 1) // head_dim
    growth = jnp.zeros((rows, LANES), f32)
    for j in range(group):
        growth = jnp.where(lane_head == j, jnp.exp(head_column(cum, pair * group + j)), growth)
    attended = intra_ref[:, cols] + inter * growth
    square = attended * attended
    scale = jnp.zeros((rows, LANES), f32)
    for j in range(group):
        mean = jnp.sum(jnp.where(lane_head == j, square, 0.0), axis=1, keepdims=True) / head_dim
        scale = jnp.where(lane_head == j, lax.rsqrt(mean + 1e-05), scale)
    o_ref[:, cols] = (attended * scale * gain_ref[:, cols]).astype(bf16)


def finish(queries, intra, states, cum, norm_gain, output_weight, head_dim):
    rows, width = queries.shape
    heads = cum.shape[1]
    pairs = width // LANES
    out_width = output_weight.shape[1]
    per = PER_STEP if pairs % PER_STEP == 0 else 1
    block = pl.BlockSpec((rows, per * LANES), lambda p: (0, p))
    return pl.pallas_call(
        functools.partial(finish_kernel, head_dim=head_dim),
        grid=(pairs // per,),
        in_specs=[
            block,
            block,
            pl.BlockSpec((per,) + states.shape[1:], lambda p: (p, 0, 0)),
            pl.BlockSpec((rows, heads), lambda p: (0, 0)),
            pl.BlockSpec((1, per * LANES), lambda p: (0, p)),
            pl.BlockSpec((per * LANES, out_width), lambda p: (p, 0)),
        ],
        out_specs=pl.BlockSpec((rows, out_width), lambda p: (0, 0)),
        out_shape=jax.ShapeDtypeStruct((rows, out_width), jnp.bfloat16),
        scratch_shapes=[pltpu.VMEM((rows, per * LANES), jnp.bfloat16), pltpu.VMEM((rows, out_width), jnp.float32)],
        cost_estimate=pl.CostEstimate(
            flops=6 * rows * LANES * LANES * pairs + 2 * rows * width * out_width,
            transcendentals=rows * heads * 2,
            bytes_accessed=rows * width * 8 + width * out_width * 2,
        ),
    )(queries, intra, states, cum, norm_gain.reshape(1, width), output_weight)


def combine(earlier, later):
    body = earlier.shape[1] - 8
    row = lax.broadcasted_iota(jnp.int32, earlier.shape, 1)
    scale = jnp.where(row < body, jnp.exp(later[:, body : body + 1, :]), 1.0)
    return scale * earlier + later


def exclusive_scan(own, count):
    flat = lax.axis_index(AXES)
    core = flat % 2
    chip = flat // 2
    chips = count // 2
    half = own.shape[0] // 2
    partner = [(i, i ^ 1) for i in range(count)]
    other = lax.ppermute(own, AXES, partner)
    pooled = jnp.where(core == 0, combine(own, other), combine(other, own))
    through = jnp.where(core == 0, pooled[:half], pooled[half:])
    before = jnp.zeros_like(through)
    received = []
    bit = 1
    while bit < chips:
        perm = [(i, i ^ (2 * bit)) for i in range(count)]
        got = lax.ppermute(through, AXES, perm)
        received.append(got)
        lower = (chip & bit) != 0
        before = jnp.where(lower, combine(got, before), before)
        bit *= 2
        if bit < chips:
            through = jnp.where(lower, combine(got, through), combine(through, got))
    swapped = lax.ppermute(before, AXES, partner)
    whole = jnp.where(
        core == 0, jnp.concatenate([before, swapped]), jnp.concatenate([swapped, before])
    )
    whole = jnp.where(core == 0, whole, combine(whole, other))
    return whole, received


def layer(count, tokens, log_decay, query_weight, key_weight, value_weight, norm_gain, output_weight):
    f32 = jnp.float32
    bf16 = jnp.bfloat16
    heads = log_decay.shape[1]
    dim = key_weight.shape[1] // heads
    keys, value_rows, packed, cum, cum_t = project_keys_values(tokens, key_weight, value_weight, log_decay, dim)
    incoming, _ = exclusive_scan(packed, count)

    queries = jax.nn.silu(jnp.dot(tokens, query_weight, preferred_element_type=f32)).astype(bf16)
    blocks = keys.shape[1] // LANES
    intra = None
    cuts = (0, blocks // 2, (3 * blocks) // 4, blocks)
    for part in range(3):
        intra = intra_attention(queries, keys, value_rows, cum, cum_t, dim, cuts[part], cuts[part + 1], intra)
    return finish(queries, intra, incoming, cum, norm_gain, output_weight, dim)


def solution(mesh):
    count = mesh.shape["outer"] * mesh.shape["inner"]
    in_specs = (P(AXES, None), P(AXES, None), P(), P(), P(), P(), P())
    out_specs = P(AXES, None)
    body = lambda *args: layer(count, *args)
    return jax.shard_map(body, mesh=mesh, in_specs=in_specs, out_specs=out_specs, check_vma=False)
```

```python
import functools

import jax
import jax.numpy as jnp
from jax import lax
from jax.experimental import pallas as pl
from jax.experimental.pallas import tpu as pltpu
from jax.sharding import PartitionSpec as P


AXES = ("outer", "inner")

LANES = 128
PER_STEP = 4


def intra_kernel(q_ref, k_ref, v_ref, cum_ref, cum_t_ref, *rest, head_dim, first):
    o_ref = rest[-1]
    f32 = jnp.float32
    pair = pl.program_id(0) + first
    group = LANES // head_dim
    rows = q_ref.shape[0]
    q = q_ref[...]
    k = k_ref[...]
    v = v_ref[...]
    lane_head = lax.broadcasted_iota(jnp.int32, q.shape, 1) // head_dim
    t_i = lax.broadcasted_iota(jnp.int32, (rows, rows), 0)
    s_i = lax.broadcasted_iota(jnp.int32, (rows, rows), 1)
    lower = s_i <= t_i
    cum = cum_ref[...]
    cum_t = cum_t_ref[...]
    col_head = lax.broadcasted_iota(jnp.int32, cum.shape, 1)
    row_head = lax.broadcasted_iota(jnp.int32, cum_t.shape, 0)
    out = None
    for j in range(group):
        head = pair * group + j
        mine = lane_head == j
        q_j = jnp.where(mine, q, jnp.zeros_like(q))
        scores = lax.dot_general(q_j, k, (((1,), (1,)), ((), ())), preferred_element_type=f32)
        col = jnp.sum(jnp.where(col_head == head, cum, 0.0), axis=1, keepdims=True)
        row = jnp.sum(jnp.where(row_head == head, cum_t, 0.0), axis=0, keepdims=True)
        diff = jnp.where(lower, col - row, 0.0)
        decay = jnp.where(lower, jnp.exp(diff), 0.0)
        weights = (scores * decay).astype(jnp.bfloat16)
        o_j = jnp.dot(weights, v, preferred_element_type=f32)
        out = o_j if out is None else jnp.where(mine, o_j, out)
    o_ref[...] = out


def intra_attention(queries, keys, value_rows, cum, cum_t, head_dim, first, stop, into=None):
    rows, width = queries.shape
    heads = cum.shape[1]
    block = pl.BlockSpec((rows, LANES), lambda p: (0, p + first))
    out_block = block
    extra = () if into is None else (into,)
    extra_specs = [] if into is None else [pl.BlockSpec(memory_space=pl.ANY)]
    whole = lambda shape: pl.BlockSpec(shape, lambda p: (0, 0))
    steps = stop - first
    flops = 4 * rows * rows * LANES * (LANES // head_dim) * steps
    return pl.pallas_call(
        functools.partial(intra_kernel, head_dim=head_dim, first=first),
        grid=(steps,),
        in_specs=[block, block, block, whole((rows, heads)), whole((heads, rows))] + extra_specs,
        out_specs=out_block,
        out_shape=jax.ShapeDtypeStruct((rows, width), jnp.float32),
        input_output_aliases={} if into is None else {5: 0},
        cost_estimate=pl.CostEstimate(
            flops=flops,
            transcendentals=rows * rows * steps * (LANES // head_dim),
            bytes_accessed=rows * steps * LANES * 10,
        ),
    )(queries, keys, value_rows, cum, cum_t, *extra)


def head_column(table, head):
    lane = lax.broadcasted_iota(jnp.int32, table.shape, 1)
    return jnp.sum(jnp.where(lane == head, table, 0.0), axis=1, keepdims=True)


def local_pair(k_ref, v_ref, cum_ref, o_ref, head_dim, step):
    f32 = jnp.float32
    pair = pl.program_id(0) * o_ref.shape[0] + step
    cols = pl.ds(step * LANES, LANES)
    group = LANES // head_dim
    rows = k_ref.shape[0]
    cum = cum_ref[...]
    lane_head = lax.broadcasted_iota(jnp.int32, (rows, LANES), 1) // head_dim
    weight = jnp.zeros((rows, LANES), f32)
    logs = jnp.zeros((1, LANES), f32)
    for j in range(group):
        col = head_column(cum, pair * group + j)
        last = col[rows - 1 :, :]
        weight = jnp.where(lane_head == j, jnp.exp(last - col), weight)
        logs = jnp.where(lane_head[:1] == j, last, logs)
    scaled = (k_ref[:, cols].astype(f32) * weight).astype(jnp.bfloat16)
    state = lax.dot_general(scaled, v_ref[:, cols], (((0,), (0,)), ((), ())), preferred_element_type=f32)
    lane = lax.broadcasted_iota(jnp.int32, (head_dim, LANES), 1) // head_dim
    packed = state[:head_dim]
    for j in range(1, group):
        packed = jnp.where(lane == j, state[j * head_dim : (j + 1) * head_dim], packed)
    o_ref[step, :head_dim, :] = packed
    tail_row = lax.broadcasted_iota(jnp.int32, (8, LANES), 0)
    o_ref[step, head_dim:, :] = jnp.where(tail_row == 0, jnp.broadcast_to(logs, (8, LANES)), 0.0)


def project_kernel(x_ref, wk_ref, wv_ref, g_ref, k_ref, v_ref, o_ref, cum_ref, cum_t_ref, *, head_dim):
    f32 = jnp.float32
    bf16 = jnp.bfloat16

    @pl.when(pl.program_id(0) == 0)
    def _():
        rows = g_ref.shape[1]
        t_i = lax.broadcasted_iota(jnp.int32, (rows, rows), 0)
        s_i = lax.broadcasted_iota(jnp.int32, (rows, rows), 1)
        lower = jnp.where(s_i <= t_i, 1.0, 0.0).astype(bf16)
        upper = jnp.where(t_i <= s_i, 1.0, 0.0).astype(bf16)
        rest = g_ref[...]
        cum = jnp.zeros(cum_ref.shape, f32)
        cum_t = jnp.zeros(cum_t_ref.shape, f32)
        for _ in range(3):
            part = rest.astype(bf16)
            cum = cum + lax.dot_general(lower, part, (((1,), (1,)), ((), ())), preferred_element_type=f32)
            cum_t = cum_t + jnp.dot(part, upper, preferred_element_type=f32)
            rest = rest - part.astype(f32)
        cum_ref[...] = cum
        cum_t_ref[...] = cum_t

    x = x_ref[...]
    key_sum = jnp.dot(x, wk_ref[...], preferred_element_type=f32)
    k_ref[...] = (key_sum / (1.0 + jnp.exp(-key_sum))).astype(jnp.bfloat16)
    v_ref[...] = jnp.dot(x, wv_ref[...], preferred_element_type=f32).astype(jnp.bfloat16)
    for step in range(o_ref.shape[0]):
        local_pair(k_ref, v_ref, cum_ref, o_ref, head_dim, step)


def project_keys_values(tokens, key_weight, value_weight, log_decay, head_dim):
    rows, depth = tokens.shape
    width = key_weight.shape[1]
    heads = log_decay.shape[1]
    pairs = width // LANES
    per = 2 if pairs % 2 == 0 else 1
    block = pl.BlockSpec((rows, per * LANES), lambda p: (0, p))
    weights = pl.BlockSpec((depth, per * LANES), lambda p: (0, p))
    return pl.pallas_call(
        functools.partial(project_kernel, head_dim=head_dim),
        grid=(pairs // per,),
        in_specs=[
            pl.BlockSpec((rows, depth), lambda p: (0, 0)),
            weights,
            weights,
            pl.BlockSpec((heads, rows), lambda p: (0, 0)),
        ],
        out_specs=[
            block,
            block,
            pl.BlockSpec((per, head_dim + 8, LANES), lambda p: (p, 0, 0)),
            pl.BlockSpec((rows, heads), lambda p: (0, 0)),
            pl.BlockSpec((heads, rows), lambda p: (0, 0)),
        ],
        out_shape=[
            jax.ShapeDtypeStruct((rows, width), jnp.bfloat16),
            jax.ShapeDtypeStruct((rows, width), jnp.bfloat16),
            jax.ShapeDtypeStruct((pairs, head_dim + 8, LANES), jnp.float32),
            jax.ShapeDtypeStruct((rows, heads), jnp.float32),
            jax.ShapeDtypeStruct((heads, rows), jnp.float32),
        ],
        cost_estimate=pl.CostEstimate(
            flops=4 * rows * depth * width + 2 * rows * LANES * width,
            transcendentals=rows * width + rows * heads,
            bytes_accessed=2 * depth * width * 2 + rows * depth * 2 + rows * width * 4,
        ),
    )(tokens, key_weight, value_weight, log_decay.T)


def finish_kernel(q_ref, intra_ref, state_ref, cum_ref, gain_ref, w_ref, o_ref, normed_ref, acc_ref, *, head_dim):
    for step in range(state_ref.shape[0]):
        finish_pair(q_ref, intra_ref, state_ref, cum_ref, gain_ref, normed_ref, head_dim, step)
    part = jnp.dot(normed_ref[...], w_ref[...], preferred_element_type=jnp.float32)
    index = pl.program_id(0)

    @pl.when(index == 0)
    def _():
        acc_ref[...] = part

    @pl.when(index > 0)
    def _():
        acc_ref[...] += part

    @pl.when(index == pl.num_programs(0) - 1)
    def _():
        o_ref[...] = acc_ref[...].astype(o_ref.dtype)


def finish_pair(q_ref, intra_ref, state_ref, cum_ref, gain_ref, o_ref, head_dim, step):
    f32 = jnp.float32
    bf16 = jnp.bfloat16
    pair = pl.program_id(0) * state_ref.shape[0] + step
    cols = pl.ds(step * LANES, LANES)
    group = LANES // head_dim
    rows = q_ref.shape[0]
    state = state_ref[step, :head_dim, :]
    tall = jnp.concatenate([state] * group, axis=0)
    r_head = lax.broadcasted_iota(jnp.int32, (LANES, LANES), 0) // head_dim
    c_head = lax.broadcasted_iota(jnp.int32, (LANES, LANES), 1) // head_dim
    block = jnp.where(r_head == c_head, tall, 0.0)
    q = q_ref[:, cols]
    inter = jnp.zeros((rows, LANES), f32)
    rest = block
    for _ in range(3):
        part = rest.astype(bf16)
        inter = inter + jnp.dot(q, part, preferred_element_type=f32)
        rest = rest - part.astype(f32)
    cum = cum_ref[...]
    lane_head = lax.broadcasted_iota(jnp.int32, (rows, LANES), 1) // head_dim
    growth = jnp.zeros((rows, LANES), f32)
    for j in range(group):
        growth = jnp.where(lane_head == j, jnp.exp(head_column(cum, pair * group + j)), growth)
    attended = intra_ref[:, cols] + inter * growth
    square = attended * attended
    scale = jnp.zeros((rows, LANES), f32)
    for j in range(group):
        mean = jnp.sum(jnp.where(lane_head == j, square, 0.0), axis=1, keepdims=True) / head_dim
        scale = jnp.where(lane_head == j, lax.rsqrt(mean + 1e-05), scale)
    o_ref[:, cols] = (attended * scale * gain_ref[:, cols]).astype(bf16)


def finish(queries, intra, states, cum, norm_gain, output_weight, head_dim):
    rows, width = queries.shape
    heads = cum.shape[1]
    pairs = width // LANES
    out_width = output_weight.shape[1]
    per = PER_STEP if pairs % PER_STEP == 0 else 1
    block = pl.BlockSpec((rows, per * LANES), lambda p: (0, p))
    return pl.pallas_call(
        functools.partial(finish_kernel, head_dim=head_dim),
        grid=(pairs // per,),
        in_specs=[
            block,
            block,
            pl.BlockSpec((per,) + states.shape[1:], lambda p: (p, 0, 0)),
            pl.BlockSpec((rows, heads), lambda p: (0, 0)),
            pl.BlockSpec((1, per * LANES), lambda p: (0, p)),
            pl.BlockSpec((per * LANES, out_width), lambda p: (p, 0)),
        ],
        out_specs=pl.BlockSpec((rows, out_width), lambda p: (0, 0)),
        out_shape=jax.ShapeDtypeStruct((rows, out_width), jnp.bfloat16),
        scratch_shapes=[pltpu.VMEM((rows, per * LANES), jnp.bfloat16), pltpu.VMEM((rows, out_width), jnp.float32)],
        cost_estimate=pl.CostEstimate(
            flops=6 * rows * LANES * LANES * pairs + 2 * rows * width * out_width,
            transcendentals=rows * heads * 2,
            bytes_accessed=rows * width * 8 + width * out_width * 2,
        ),
    )(queries, intra, states, cum, norm_gain.reshape(1, width), output_weight)


def combine(earlier, later):
    body = earlier.shape[1] - 8
    row = lax.broadcasted_iota(jnp.int32, earlier.shape, 1)
    scale = jnp.where(row < body, jnp.exp(later[:, body : body + 1, :]), 1.0)
    return scale * earlier + later


def exclusive_scan(own, count):
    flat = lax.axis_index(AXES)
    core = flat % 2
    chip = flat // 2
    chips = count // 2
    half = own.shape[0] // 2
    partner = [(i, i ^ 1) for i in range(count)]
    other = lax.ppermute(own, AXES, partner)
    pooled = jnp.where(core == 0, combine(own, other), combine(other, own))
    through = jnp.where(core == 0, pooled[:half], pooled[half:])
    before = jnp.zeros_like(through)
    received = []
    bit = 1
    while bit < chips:
        perm = [(i, i ^ (2 * bit)) for i in range(count)]
        got = lax.ppermute(through, AXES, perm)
        received.append(got)
        lower = (chip & bit) != 0
        before = jnp.where(lower, combine(got, before), before)
        bit *= 2
        if bit < chips:
            through = jnp.where(lower, combine(got, through), combine(through, got))
    swapped = lax.ppermute(before, AXES, partner)
    whole = jnp.where(
        core == 0, jnp.concatenate([before, swapped]), jnp.concatenate([swapped, before])
    )
    whole = jnp.where(core == 0, whole, combine(whole, other))
    return whole, received


def layer(count, tokens, log_decay, query_weight, key_weight, value_weight, norm_gain, output_weight):
    f32 = jnp.float32
    bf16 = jnp.bfloat16
    heads = log_decay.shape[1]
    dim = key_weight.shape[1] // heads
    keys, value_rows, packed, cum, cum_t = project_keys_values(tokens, key_weight, value_weight, log_decay, dim)
    incoming, _ = exclusive_scan(packed, count)

    queries = jax.nn.silu(jnp.dot(tokens, query_weight, preferred_element_type=f32)).astype(bf16)
    blocks = keys.shape[1] // LANES
    intra = None
    cuts = (0, blocks // 2, (3 * blocks) // 4, blocks)
    for part in range(3):
        intra = intra_attention(queries, keys, value_rows, cum, cum_t, dim, cuts[part], cuts[part + 1], intra)
    return finish(queries, intra, incoming, cum, norm_gain, output_weight, dim)


def solution(mesh):
    count = mesh.shape["outer"] * mesh.shape["inner"]
    in_specs = (P(AXES, None), P(AXES, None), P(), P(), P(), P(), P())
    out_specs = P(AXES, None)
    body = lambda *args: layer(count, *args)
    return jax.shard_map(body, mesh=mesh, in_specs=in_specs, out_specs=out_specs, check_vma=False)
```

```python
import functools

import jax
import jax.numpy as jnp
from jax import lax
from jax.experimental import pallas as pl
from jax.experimental.pallas import tpu as pltpu
from jax.sharding import PartitionSpec as P


AXES = ("outer", "inner")

LANES = 128
PER_STEP = 4


def intra_kernel(q_ref, k_ref, v_ref, cum_ref, cum_t_ref, *rest, head_dim, first):
    o_ref = rest[-1]
    f32 = jnp.float32
    pair = pl.program_id(0) + first
    group = LANES // head_dim
    rows = q_ref.shape[0]
    q = q_ref[...]
    k = k_ref[...]
    v = v_ref[...]
    lane_head = lax.broadcasted_iota(jnp.int32, q.shape, 1) // head_dim
    t_i = lax.broadcasted_iota(jnp.int32, (rows, rows), 0)
    s_i = lax.broadcasted_iota(jnp.int32, (rows, rows), 1)
    lower = s_i <= t_i
    cum = cum_ref[...]
    cum_t = cum_t_ref[...]
    col_head = lax.broadcasted_iota(jnp.int32, cum.shape, 1)
    row_head = lax.broadcasted_iota(jnp.int32, cum_t.shape, 0)
    out = None
    for j in range(group):
        head = pair * group + j
        mine = lane_head == j
        q_j = jnp.where(mine, q, jnp.zeros_like(q))
        scores = lax.dot_general(q_j, k, (((1,), (1,)), ((), ())), preferred_element_type=f32)
        col = jnp.sum(jnp.where(col_head == head, cum, 0.0), axis=1, keepdims=True)
        row = jnp.sum(jnp.where(row_head == head, cum_t, 0.0), axis=0, keepdims=True)
        diff = jnp.where(lower, col - row, 0.0)
        decay = jnp.where(lower, jnp.exp(diff), 0.0)
        weights = (scores * decay).astype(jnp.bfloat16)
        o_j = jnp.dot(weights, v, preferred_element_type=f32)
        out = o_j if out is None else jnp.where(mine, o_j, out)
    o_ref[...] = out


def intra_attention(queries, keys, value_rows, cum, cum_t, head_dim, first, stop, into=None):
    rows, width = queries.shape
    heads = cum.shape[1]
    block = pl.BlockSpec((rows, LANES), lambda p: (0, p + first))
    out_block = block
    extra = () if into is None else (into,)
    extra_specs = [] if into is None else [pl.BlockSpec(memory_space=pl.ANY)]
    whole = lambda shape: pl.BlockSpec(shape, lambda p: (0, 0))
    steps = stop - first
    flops = 4 * rows * rows * LANES * (LANES // head_dim) * steps
    return pl.pallas_call(
        functools.partial(intra_kernel, head_dim=head_dim, first=first),
        grid=(steps,),
        in_specs=[block, block, block, whole((rows, heads)), whole((heads, rows))] + extra_specs,
        out_specs=out_block,
        out_shape=jax.ShapeDtypeStruct((rows, width), jnp.float32),
        input_output_aliases={} if into is None else {5: 0},
        cost_estimate=pl.CostEstimate(
            flops=flops,
            transcendentals=rows * rows * steps * (LANES // head_dim),
            bytes_accessed=rows * steps * LANES * 10,
        ),
    )(queries, keys, value_rows, cum, cum_t, *extra)


def head_column(table, head):
    lane = lax.broadcasted_iota(jnp.int32, table.shape, 1)
    return jnp.sum(jnp.where(lane == head, table, 0.0), axis=1, keepdims=True)


def local_pair(k_ref, v_ref, cum_ref, o_ref, head_dim, step, pair=None):
    f32 = jnp.float32
    if pair is None:
        pair = pl.program_id(0) * o_ref.shape[0] + step
    cols = pl.ds(step * LANES, LANES)
    group = LANES // head_dim
    rows = k_ref.shape[0]
    cum = cum_ref[...]
    lane_head = lax.broadcasted_iota(jnp.int32, (rows, LANES), 1) // head_dim
    weight = jnp.zeros((rows, LANES), f32)
    logs = jnp.zeros((1, LANES), f32)
    for j in range(group):
        col = head_column(cum, pair * group + j)
        last = col[rows - 1 :, :]
        weight = jnp.where(lane_head == j, jnp.exp(last - col), weight)
        logs = jnp.where(lane_head[:1] == j, last, logs)
    scaled = (k_ref[:, cols].astype(f32) * weight).astype(jnp.bfloat16)
    state = lax.dot_general(scaled, v_ref[:, cols], (((0,), (0,)), ((), ())), preferred_element_type=f32)
    lane = lax.broadcasted_iota(jnp.int32, (head_dim, LANES), 1) // head_dim
    packed = state[:head_dim]
    for j in range(1, group):
        packed = jnp.where(lane == j, state[j * head_dim : (j + 1) * head_dim], packed)
    o_ref[step, :head_dim, :] = packed
    tail_row = lax.broadcasted_iota(jnp.int32, (8, LANES), 0)
    o_ref[step, head_dim:, :] = jnp.where(tail_row == 0, jnp.broadcast_to(logs, (8, LANES)), 0.0)


def project_kernel(
    core_ref, x_ref, wk_ref, wv_ref, g_ref, k_ref, v_ref, send_ref, keep_ref, cum_ref, cum_t_ref, *, head_dim
):
    f32 = jnp.float32
    bf16 = jnp.bfloat16
    index = pl.program_id(0)
    half = (index + 1 + core_ref[0]) % 2

    @pl.when(index == 0)
    def _():
        rows = g_ref.shape[1]
        t_i = lax.broadcasted_iota(jnp.int32, (rows, rows), 0)
        s_i = lax.broadcasted_iota(jnp.int32, (rows, rows), 1)
        lower = jnp.where(s_i <= t_i, 1.0, 0.0).astype(bf16)
        upper = jnp.where(t_i <= s_i, 1.0, 0.0).astype(bf16)
        rest = g_ref[...]
        cum = jnp.zeros(cum_ref.shape, f32)
        cum_t = jnp.zeros(cum_t_ref.shape, f32)
        for _ in range(3):
            part = rest.astype(bf16)
            cum = cum + lax.dot_general(lower, part, (((1,), (1,)), ((), ())), preferred_element_type=f32)
            cum_t = cum_t + jnp.dot(part, upper, preferred_element_type=f32)
            rest = rest - part.astype(f32)
        cum_ref[...] = cum
        cum_t_ref[...] = cum_t

    x = x_ref[...]
    key_sum = jnp.dot(x, wk_ref[...], preferred_element_type=f32)
    k_ref[...] = (key_sum / (1.0 + jnp.exp(-key_sum))).astype(jnp.bfloat16)
    v_ref[...] = jnp.dot(x, wv_ref[...], preferred_element_type=f32).astype(jnp.bfloat16)
    per = send_ref.shape[0]

    @pl.when(index == 0)
    def _():
        for step in range(per):
            local_pair(k_ref, v_ref, cum_ref, send_ref, head_dim, step, half * per + step)

    @pl.when(index == 1)
    def _():
        for step in range(per):
            local_pair(k_ref, v_ref, cum_ref, keep_ref, head_dim, step, half * per + step)


def project_keys_values(tokens, key_weight, value_weight, log_decay, head_dim, core):
    rows, depth = tokens.shape
    width = key_weight.shape[1]
    heads = log_decay.shape[1]
    pairs = width // LANES
    per = pairs // 2
    columns = lambda p, core_ref: (0, (p + 1 + core_ref[0]) % 2)
    whole = lambda shape: pl.BlockSpec(shape, lambda p, core_ref: (0,) * len(shape))
    block = pl.BlockSpec((rows, per * LANES), columns)
    weights = pl.BlockSpec((depth, per * LANES), columns)
    half = jax.ShapeDtypeStruct((per, head_dim + 8, LANES), jnp.float32)
    return pl.pallas_call(
        functools.partial(project_kernel, head_dim=head_dim),
        grid_spec=pltpu.PrefetchScalarGridSpec(
            num_scalar_prefetch=1,
            grid=(2,),
            in_specs=[whole((rows, depth)), weights, weights, whole((heads, rows))],
            out_specs=[
                block,
                block,
                whole((per, head_dim + 8, LANES)),
                whole((per, head_dim + 8, LANES)),
                whole((rows, heads)),
                whole((heads, rows)),
            ],
        ),
        out_shape=[
            jax.ShapeDtypeStruct((rows, width), jnp.bfloat16),
            jax.ShapeDtypeStruct((rows, width), jnp.bfloat16),
            half,
            half,
            jax.ShapeDtypeStruct((rows, heads), jnp.float32),
            jax.ShapeDtypeStruct((heads, rows), jnp.float32),
        ],
        cost_estimate=pl.CostEstimate(
            flops=4 * rows * depth * width + 2 * rows * LANES * width,
            transcendentals=rows * width + rows * heads,
            bytes_accessed=2 * depth * width * 2 + rows * depth * 2 + rows * width * 4,
        ),
    )(jnp.reshape(core, (1,)).astype(jnp.int32), tokens, key_weight, value_weight, log_decay.T)


def finish_kernel(q_ref, intra_ref, state_ref, cum_ref, gain_ref, w_ref, o_ref, normed_ref, acc_ref, *, head_dim):
    for step in range(state_ref.shape[0]):
        finish_pair(q_ref, intra_ref, state_ref, cum_ref, gain_ref, normed_ref, head_dim, step)
    part = jnp.dot(normed_ref[...], w_ref[...], preferred_element_type=jnp.float32)
    index = pl.program_id(0)

    @pl.when(index == 0)
    def _():
        acc_ref[...] = part

    @pl.when(index > 0)
    def _():
        acc_ref[...] += part

    @pl.when(index == pl.num_programs(0) - 1)
    def _():
        o_ref[...] = acc_ref[...].astype(o_ref.dtype)


def finish_pair(q_ref, intra_ref, state_ref, cum_ref, gain_ref, o_ref, head_dim, step):
    f32 = jnp.float32
    bf16 = jnp.bfloat16
    pair = pl.program_id(0) * state_ref.shape[0] + step
    cols = pl.ds(step * LANES, LANES)
    group = LANES // head_dim
    rows = q_ref.shape[0]
    state = state_ref[step, :head_dim, :]
    tall = jnp.concatenate([state] * group, axis=0)
    r_head = lax.broadcasted_iota(jnp.int32, (LANES, LANES), 0) // head_dim
    c_head = lax.broadcasted_iota(jnp.int32, (LANES, LANES), 1) // head_dim
    block = jnp.where(r_head == c_head, tall, 0.0)
    q = q_ref[:, cols]
    inter = jnp.zeros((rows, LANES), f32)
    rest = block
    for _ in range(3):
        part = rest.astype(bf16)
        inter = inter + jnp.dot(q, part, preferred_element_type=f32)
        rest = rest - part.astype(f32)
    cum = cum_ref[...]
    lane_head = lax.broadcasted_iota(jnp.int32, (rows, LANES), 1) // head_dim
    growth = jnp.zeros((rows, LANES), f32)
    for j in range(group):
        growth = jnp.where(lane_head == j, jnp.exp(head_column(cum, pair * group + j)), growth)
    attended = intra_ref[:, cols] + inter * growth
    square = attended * attended
    scale = jnp.zeros((rows, LANES), f32)
    for j in range(group):
        mean = jnp.sum(jnp.where(lane_head == j, square, 0.0), axis=1, keepdims=True) / head_dim
        scale = jnp.where(lane_head == j, lax.rsqrt(mean + 1e-05), scale)
    o_ref[:, cols] = (attended * scale * gain_ref[:, cols]).astype(bf16)


def finish(queries, intra, states, cum, norm_gain, output_weight, head_dim):
    rows, width = queries.shape
    heads = cum.shape[1]
    pairs = width // LANES
    out_width = output_weight.shape[1]
    per = PER_STEP if pairs % PER_STEP == 0 else 1
    block = pl.BlockSpec((rows, per * LANES), lambda p: (0, p))
    return pl.pallas_call(
        functools.partial(finish_kernel, head_dim=head_dim),
        grid=(pairs // per,),
        in_specs=[
            block,
            block,
            pl.BlockSpec((per,) + states.shape[1:], lambda p: (p, 0, 0)),
            pl.BlockSpec((rows, heads), lambda p: (0, 0)),
            pl.BlockSpec((1, per * LANES), lambda p: (0, p)),
            pl.BlockSpec((per * LANES, out_width), lambda p: (p, 0)),
        ],
        out_specs=pl.BlockSpec((rows, out_width), lambda p: (0, 0)),
        out_shape=jax.ShapeDtypeStruct((rows, out_width), jnp.bfloat16),
        scratch_shapes=[pltpu.VMEM((rows, per * LANES), jnp.bfloat16), pltpu.VMEM((rows, out_width), jnp.float32)],
        cost_estimate=pl.CostEstimate(
            flops=6 * rows * LANES * LANES * pairs + 2 * rows * width * out_width,
            transcendentals=rows * heads * 2,
            bytes_accessed=rows * width * 8 + width * out_width * 2,
        ),
    )(queries, intra, states, cum, norm_gain.reshape(1, width), output_weight)


def combine(earlier, later):
    body = earlier.shape[1] - 8
    row = lax.broadcasted_iota(jnp.int32, earlier.shape, 1)
    scale = jnp.where(row < body, jnp.exp(later[:, body : body + 1, :]), 1.0)
    return scale * earlier + later


def exclusive_scan(send, keep, count):
    flat = lax.axis_index(AXES)
    core = flat % 2
    chip = flat // 2
    chips = count // 2
    partner = [(i, i ^ 1) for i in range(count)]
    got = lax.ppermute(send, AXES, partner)
    through = jnp.where(core == 0, combine(keep, got), combine(got, keep))
    before = jnp.zeros_like(through)
    received = []
    bit = 1
    while bit < chips:
        perm = [(i, i ^ (2 * bit)) for i in range(count)]
        exchanged = lax.ppermute(through, AXES, perm)
        received.append(exchanged)
        lower = (chip & bit) != 0
        before = jnp.where(lower, combine(exchanged, before), before)
        bit *= 2
        if bit < chips:
            through = jnp.where(lower, combine(exchanged, through), combine(through, exchanged))
    back = lax.ppermute(jnp.where(core == 0, combine(before, keep), before), AXES, partner)
    whole = jnp.where(
        core == 0, jnp.concatenate([before, back]), jnp.concatenate([back, combine(before, got)])
    )
    return whole, received


def layer(count, tokens, log_decay, query_weight, key_weight, value_weight, norm_gain, output_weight):
    f32 = jnp.float32
    bf16 = jnp.bfloat16
    heads = log_decay.shape[1]
    dim = key_weight.shape[1] // heads
    core = lax.axis_index(AXES) % 2
    keys, value_rows, send, keep, cum, cum_t = project_keys_values(
        tokens, key_weight, value_weight, log_decay, dim, core
    )
    incoming, _ = exclusive_scan(send, keep, count)

    queries = jax.nn.silu(jnp.dot(tokens, query_weight, preferred_element_type=f32)).astype(bf16)
    blocks = keys.shape[1] // LANES
    intra = None
    cuts = (0, blocks // 2, (3 * blocks) // 4, blocks)
    for part in range(3):
        intra = intra_attention(queries, keys, value_rows, cum, cum_t, dim, cuts[part], cuts[part + 1], intra)
    return finish(queries, intra, incoming, cum, norm_gain, output_weight, dim)


def solution(mesh):
    count = mesh.shape["outer"] * mesh.shape["inner"]
    in_specs = (P(AXES, None), P(AXES, None), P(), P(), P(), P(), P())
    out_specs = P(AXES, None)
    body = lambda *args: layer(count, *args)
    return jax.shard_map(body, mesh=mesh, in_specs=in_specs, out_specs=out_specs, check_vma=False)
```

```python
import functools

import jax
import jax.numpy as jnp
from jax import lax
from jax.experimental import pallas as pl
from jax.experimental.pallas import tpu as pltpu
from jax.sharding import PartitionSpec as P


AXES = ("outer", "inner")

LANES = 128
PER_STEP = 4


def intra_kernel(q_ref, k_ref, v_ref, cum_ref, cum_t_ref, *rest, head_dim, first):
    o_ref = rest[-1]
    f32 = jnp.float32
    pair = pl.program_id(0) + first
    group = LANES // head_dim
    rows = q_ref.shape[0]
    q = q_ref[...]
    k = k_ref[...]
    v = v_ref[...]
    lane_head = lax.broadcasted_iota(jnp.int32, q.shape, 1) // head_dim
    t_i = lax.broadcasted_iota(jnp.int32, (rows, rows), 0)
    s_i = lax.broadcasted_iota(jnp.int32, (rows, rows), 1)
    lower = s_i <= t_i
    cum = cum_ref[...]
    cum_t = cum_t_ref[...]
    col_head = lax.broadcasted_iota(jnp.int32, cum.shape, 1)
    row_head = lax.broadcasted_iota(jnp.int32, cum_t.shape, 0)
    out = None
    for j in range(group):
        head = pair * group + j
        mine = lane_head == j
        q_j = jnp.where(mine, q, jnp.zeros_like(q))
        scores = lax.dot_general(q_j, k, (((1,), (1,)), ((), ())), preferred_element_type=f32)
        col = jnp.sum(jnp.where(col_head == head, cum, 0.0), axis=1, keepdims=True)
        row = jnp.sum(jnp.where(row_head == head, cum_t, 0.0), axis=0, keepdims=True)
        diff = jnp.where(lower, col - row, 0.0)
        decay = jnp.where(lower, jnp.exp(diff), 0.0)
        weights = (scores * decay).astype(jnp.bfloat16)
        o_j = jnp.dot(weights, v, preferred_element_type=f32)
        out = o_j if out is None else jnp.where(mine, o_j, out)
    o_ref[...] = out


def intra_attention(queries, keys, value_rows, cum, cum_t, head_dim, first, stop, into=None):
    rows, width = queries.shape
    heads = cum.shape[1]
    block = pl.BlockSpec((rows, LANES), lambda p: (0, p + first))
    out_block = block
    extra = () if into is None else (into,)
    extra_specs = [] if into is None else [pl.BlockSpec(memory_space=pl.ANY)]
    whole = lambda shape: pl.BlockSpec(shape, lambda p: (0, 0))
    steps = stop - first
    flops = 4 * rows * rows * LANES * (LANES // head_dim) * steps
    return pl.pallas_call(
        functools.partial(intra_kernel, head_dim=head_dim, first=first),
        grid=(steps,),
        in_specs=[block, block, block, whole((rows, heads)), whole((heads, rows))] + extra_specs,
        out_specs=out_block,
        out_shape=jax.ShapeDtypeStruct((rows, width), jnp.float32),
        input_output_aliases={} if into is None else {5: 0},
        cost_estimate=pl.CostEstimate(
            flops=flops,
            transcendentals=rows * rows * steps * (LANES // head_dim),
            bytes_accessed=rows * steps * LANES * 10,
        ),
    )(queries, keys, value_rows, cum, cum_t, *extra)


def head_column(table, head):
    lane = lax.broadcasted_iota(jnp.int32, table.shape, 1)
    return jnp.sum(jnp.where(lane == head, table, 0.0), axis=1, keepdims=True)


def local_pair(k_ref, v_ref, cum_ref, o_ref, head_dim, step):
    f32 = jnp.float32
    pair = pl.program_id(0) * o_ref.shape[0] + step
    cols = pl.ds(step * LANES, LANES)
    group = LANES // head_dim
    rows = k_ref.shape[0]
    cum = cum_ref[...]
    lane_head = lax.broadcasted_iota(jnp.int32, (rows, LANES), 1) // head_dim
    weight = jnp.zeros((rows, LANES), f32)
    logs = jnp.zeros((1, LANES), f32)
    for j in range(group):
        col = head_column(cum, pair * group + j)
        last = col[rows - 1 :, :]
        weight = jnp.where(lane_head == j, jnp.exp(last - col), weight)
        logs = jnp.where(lane_head[:1] == j, last, logs)
    scaled = (k_ref[:, cols].astype(f32) * weight).astype(jnp.bfloat16)
    state = lax.dot_general(scaled, v_ref[:, cols], (((0,), (0,)), ((), ())), preferred_element_type=f32)
    lane = lax.broadcasted_iota(jnp.int32, (head_dim, LANES), 1) // head_dim
    packed = state[:head_dim]
    for j in range(1, group):
        packed = jnp.where(lane == j, state[j * head_dim : (j + 1) * head_dim], packed)
    o_ref[step, :head_dim, :] = packed
    tail_row = lax.broadcasted_iota(jnp.int32, (8, LANES), 0)
    o_ref[step, head_dim:, :] = jnp.where(tail_row == 0, jnp.broadcast_to(logs, (8, LANES)), 0.0)


def project_kernel(x_ref, wk_ref, wv_ref, g_ref, k_ref, v_ref, o_ref, cum_ref, cum_t_ref, *, head_dim):
    f32 = jnp.float32
    bf16 = jnp.bfloat16

    @pl.when(pl.program_id(0) == 0)
    def _():
        rows = g_ref.shape[1]
        t_i = lax.broadcasted_iota(jnp.int32, (rows, rows), 0)
        s_i = lax.broadcasted_iota(jnp.int32, (rows, rows), 1)
        lower = jnp.where(s_i <= t_i, 1.0, 0.0).astype(bf16)
        upper = jnp.where(t_i <= s_i, 1.0, 0.0).astype(bf16)
        rest = g_ref[...]
        cum = jnp.zeros(cum_ref.shape, f32)
        cum_t = jnp.zeros(cum_t_ref.shape, f32)
        for _ in range(3):
            part = rest.astype(bf16)
            cum = cum + lax.dot_general(lower, part, (((1,), (1,)), ((), ())), preferred_element_type=f32)
            cum_t = cum_t + jnp.dot(part, upper, preferred_element_type=f32)
            rest = rest - part.astype(f32)
        cum_ref[...] = cum
        cum_t_ref[...] = cum_t

    x = x_ref[...]
    key_sum = jnp.dot(x, wk_ref[...], preferred_element_type=f32)
    k_ref[...] = (key_sum / (1.0 + jnp.exp(-key_sum))).astype(jnp.bfloat16)
    v_ref[...] = jnp.dot(x, wv_ref[...], preferred_element_type=f32).astype(jnp.bfloat16)
    for step in range(o_ref.shape[0]):
        local_pair(k_ref, v_ref, cum_ref, o_ref, head_dim, step)


def project_keys_values(tokens, key_weight, value_weight, log_decay, head_dim):
    rows, depth = tokens.shape
    width = key_weight.shape[1]
    heads = log_decay.shape[1]
    pairs = width // LANES
    per = PER_STEP if pairs % PER_STEP == 0 else 1
    block = pl.BlockSpec((rows, per * LANES), lambda p: (0, p))
    weights = pl.BlockSpec((depth, per * LANES), lambda p: (0, p))
    return pl.pallas_call(
        functools.partial(project_kernel, head_dim=head_dim),
        grid=(pairs // per,),
        in_specs=[
            pl.BlockSpec((rows, depth), lambda p: (0, 0)),
            weights,
            weights,
            pl.BlockSpec((heads, rows), lambda p: (0, 0)),
        ],
        out_specs=[
            block,
            block,
            pl.BlockSpec((per, head_dim + 8, LANES), lambda p: (p, 0, 0)),
            pl.BlockSpec((rows, heads), lambda p: (0, 0)),
            pl.BlockSpec((heads, rows), lambda p: (0, 0)),
        ],
        out_shape=[
            jax.ShapeDtypeStruct((rows, width), jnp.bfloat16),
            jax.ShapeDtypeStruct((rows, width), jnp.bfloat16),
            jax.ShapeDtypeStruct((pairs, head_dim + 8, LANES), jnp.float32),
            jax.ShapeDtypeStruct((rows, heads), jnp.float32),
            jax.ShapeDtypeStruct((heads, rows), jnp.float32),
        ],
        cost_estimate=pl.CostEstimate(
            flops=4 * rows * depth * width + 2 * rows * LANES * width,
            transcendentals=rows * width + rows * heads,
            bytes_accessed=2 * depth * width * 2 + rows * depth * 2 + rows * width * 4,
        ),
    )(tokens, key_weight, value_weight, log_decay.T)


def finish_kernel(q_ref, intra_ref, state_ref, cum_ref, gain_ref, w_ref, o_ref, normed_ref, acc_ref, *, head_dim):
    for step in range(state_ref.shape[0]):
        finish_pair(q_ref, intra_ref, state_ref, cum_ref, gain_ref, normed_ref, head_dim, step)
    part = jnp.dot(normed_ref[...], w_ref[...], preferred_element_type=jnp.float32)
    index = pl.program_id(0)

    @pl.when(index == 0)
    def _():
        acc_ref[...] = part

    @pl.when(index > 0)
    def _():
        acc_ref[...] += part

    @pl.when(index == pl.num_programs(0) - 1)
    def _():
        o_ref[...] = acc_ref[...].astype(o_ref.dtype)


def finish_pair(q_ref, intra_ref, state_ref, cum_ref, gain_ref, o_ref, head_dim, step):
    f32 = jnp.float32
    bf16 = jnp.bfloat16
    pair = pl.program_id(0) * state_ref.shape[0] + step
    cols = pl.ds(step * LANES, LANES)
    group = LANES // head_dim
    rows = q_ref.shape[0]
    state = state_ref[step, :head_dim, :]
    tall = jnp.concatenate([state] * group, axis=0)
    r_head = lax.broadcasted_iota(jnp.int32, (LANES, LANES), 0) // head_dim
    c_head = lax.broadcasted_iota(jnp.int32, (LANES, LANES), 1) // head_dim
    block = jnp.where(r_head == c_head, tall, 0.0)
    q = q_ref[:, cols]
    inter = jnp.zeros((rows, LANES), f32)
    rest = block
    for _ in range(3):
        part = rest.astype(bf16)
        inter = inter + jnp.dot(q, part, preferred_element_type=f32)
        rest = rest - part.astype(f32)
    heads = cum_ref.shape[1]
    pick_h = lax.broadcasted_iota(jnp.int32, (heads, LANES), 0)
    pick_l = lax.broadcasted_iota(jnp.int32, (heads, LANES), 1) // head_dim + pair * group
    pick = jnp.where(pick_h == pick_l, 1.0, 0.0).astype(bf16)
    rest = cum_ref[...]
    lane_cum = jnp.zeros((rows, LANES), f32)
    for _ in range(3):
        part = rest.astype(bf16)
        lane_cum = lane_cum + jnp.dot(part, pick, preferred_element_type=f32)
        rest = rest - part.astype(f32)
    attended = intra_ref[:, cols] + inter * jnp.exp(lane_cum)
    square = attended * attended
    average = jnp.where(r_head == c_head, 1.0 / head_dim, 0.0).astype(bf16)
    rest = square
    mean = jnp.zeros((rows, LANES), f32)
    for _ in range(3):
        part = rest.astype(bf16)
        mean = mean + jnp.dot(part, average, preferred_element_type=f32)
        rest = rest - part.astype(f32)
    scale = lax.rsqrt(mean + 1e-05)
    o_ref[:, cols] = (attended * scale * gain_ref[:, cols]).astype(bf16)


def finish(queries, intra, states, cum, norm_gain, output_weight, head_dim):
    rows, width = queries.shape
    heads = cum.shape[1]
    pairs = width // LANES
    out_width = output_weight.shape[1]
    per = PER_STEP if pairs % PER_STEP == 0 else 1
    block = pl.BlockSpec((rows, per * LANES), lambda p: (0, p))
    return pl.pallas_call(
        functools.partial(finish_kernel, head_dim=head_dim),
        grid=(pairs // per,),
        in_specs=[
            block,
            block,
            pl.BlockSpec((per,) + states.shape[1:], lambda p: (p, 0, 0)),
            pl.BlockSpec((rows, heads), lambda p: (0, 0)),
            pl.BlockSpec((1, per * LANES), lambda p: (0, p)),
            pl.BlockSpec((per * LANES, out_width), lambda p: (p, 0)),
        ],
        out_specs=pl.BlockSpec((rows, out_width), lambda p: (0, 0)),
        out_shape=jax.ShapeDtypeStruct((rows, out_width), jnp.bfloat16),
        scratch_shapes=[pltpu.VMEM((rows, per * LANES), jnp.bfloat16), pltpu.VMEM((rows, out_width), jnp.float32)],
        cost_estimate=pl.CostEstimate(
            flops=6 * rows * LANES * LANES * pairs + 2 * rows * width * out_width,
            transcendentals=rows * heads * 2,
            bytes_accessed=rows * width * 8 + width * out_width * 2,
        ),
    )(queries, intra, states, cum, norm_gain.reshape(1, width), output_weight)


def combine(earlier, later):
    body = earlier.shape[1] - 8
    row = lax.broadcasted_iota(jnp.int32, earlier.shape, 1)
    scale = jnp.where(row < body, jnp.exp(later[:, body : body + 1, :]), 1.0)
    return scale * earlier + later


def exclusive_scan(own, count):
    flat = lax.axis_index(AXES)
    core = flat % 2
    chip = flat // 2
    chips = count // 2
    half = own.shape[0] // 2
    partner = [(i, i ^ 1) for i in range(count)]
    got = lax.ppermute(jnp.where(core == 0, own[half:], own[:half]), AXES, partner)
    through = jnp.where(core == 0, combine(own[:half], got), combine(got, own[half:]))
    before = jnp.zeros_like(through)
    received = []
    bit = 1
    while bit < chips:
        perm = [(i, i ^ (2 * bit)) for i in range(count)]
        exchanged = lax.ppermute(through, AXES, perm)
        received.append(exchanged)
        lower = (chip & bit) != 0
        before = jnp.where(lower, combine(exchanged, before), before)
        bit *= 2
        if bit < chips:
            through = jnp.where(lower, combine(exchanged, through), combine(through, exchanged))
    back = lax.ppermute(jnp.where(core == 0, combine(before, own[:half]), before), AXES, partner)
    whole = jnp.where(
        core == 0, jnp.concatenate([before, back]), jnp.concatenate([back, combine(before, got)])
    )
    return whole, received


def layer(count, tokens, log_decay, query_weight, key_weight, value_weight, norm_gain, output_weight):
    f32 = jnp.float32
    bf16 = jnp.bfloat16
    heads = log_decay.shape[1]
    dim = key_weight.shape[1] // heads
    keys, value_rows, packed, cum, cum_t = project_keys_values(tokens, key_weight, value_weight, log_decay, dim)
    incoming, _ = exclusive_scan(packed, count)

    queries = jax.nn.silu(jnp.dot(tokens, query_weight, preferred_element_type=f32)).astype(bf16)
    blocks = keys.shape[1] // LANES
    intra = None
    cuts = (0, blocks // 2, (3 * blocks) // 4, blocks)
    for part in range(3):
        intra = intra_attention(queries, keys, value_rows, cum, cum_t, dim, cuts[part], cuts[part + 1], intra)
    return finish(queries, intra, incoming, cum, norm_gain, output_weight, dim)


def solution(mesh):
    count = mesh.shape["outer"] * mesh.shape["inner"]
    in_specs = (P(AXES, None), P(AXES, None), P(), P(), P(), P(), P())
    out_specs = P(AXES, None)
    body = lambda *args: layer(count, *args)
    return jax.shard_map(body, mesh=mesh, in_specs=in_specs, out_specs=out_specs, check_vma=False)
```

```python
import functools

import jax
import jax.numpy as jnp
from jax import lax
from jax.experimental import pallas as pl
from jax.experimental.pallas import tpu as pltpu
from jax.sharding import PartitionSpec as P


AXES = ("outer", "inner")

LANES = 128
PER_STEP = 4


def intra_kernel(q_ref, k_ref, v_ref, cum_ref, cum_t_ref, *rest, head_dim, first):
    o_ref = rest[-1]
    f32 = jnp.float32
    pair = pl.program_id(0) + first
    group = LANES // head_dim
    rows = q_ref.shape[0]
    q = q_ref[...]
    k = k_ref[...]
    v = v_ref[...]
    lane_head = lax.broadcasted_iota(jnp.int32, q.shape, 1) // head_dim
    t_i = lax.broadcasted_iota(jnp.int32, (rows, rows), 0)
    s_i = lax.broadcasted_iota(jnp.int32, (rows, rows), 1)
    lower = s_i <= t_i
    cum = cum_ref[...]
    cum_t = cum_t_ref[...]
    col_head = lax.broadcasted_iota(jnp.int32, cum.shape, 1)
    row_head = lax.broadcasted_iota(jnp.int32, cum_t.shape, 0)
    out = None
    for j in range(group):
        head = pair * group + j
        mine = lane_head == j
        q_j = jnp.where(mine, q, jnp.zeros_like(q))
        scores = lax.dot_general(q_j, k, (((1,), (1,)), ((), ())), preferred_element_type=f32)
        col = jnp.sum(jnp.where(col_head == head, cum, 0.0), axis=1, keepdims=True)
        row = jnp.sum(jnp.where(row_head == head, cum_t, 0.0), axis=0, keepdims=True)
        diff = jnp.where(lower, col - row, 0.0)
        decay = jnp.where(lower, jnp.exp(diff), 0.0)
        weights = (scores * decay).astype(jnp.bfloat16)
        o_j = jnp.dot(weights, v, preferred_element_type=f32)
        out = o_j if out is None else jnp.where(mine, o_j, out)
    o_ref[...] = out


def intra_attention(queries, keys, value_rows, cum, cum_t, head_dim, first, stop, into=None):
    rows, width = queries.shape
    heads = cum.shape[1]
    block = pl.BlockSpec((rows, LANES), lambda p: (0, p + first))
    out_block = block
    extra = () if into is None else (into,)
    extra_specs = [] if into is None else [pl.BlockSpec(memory_space=pl.ANY)]
    whole = lambda shape: pl.BlockSpec(shape, lambda p: (0, 0))
    steps = stop - first
    flops = 4 * rows * rows * LANES * (LANES // head_dim) * steps
    return pl.pallas_call(
        functools.partial(intra_kernel, head_dim=head_dim, first=first),
        grid=(steps,),
        in_specs=[block, block, block, whole((rows, heads)), whole((heads, rows))] + extra_specs,
        out_specs=out_block,
        out_shape=jax.ShapeDtypeStruct((rows, width), jnp.float32),
        input_output_aliases={} if into is None else {5: 0},
        cost_estimate=pl.CostEstimate(
            flops=flops,
            transcendentals=rows * rows * steps * (LANES // head_dim),
            bytes_accessed=rows * steps * LANES * 10,
        ),
    )(queries, keys, value_rows, cum, cum_t, *extra)


def head_column(table, head):
    lane = lax.broadcasted_iota(jnp.int32, table.shape, 1)
    return jnp.sum(jnp.where(lane == head, table, 0.0), axis=1, keepdims=True)


def local_pair(k_ref, v_ref, cum_ref, o_ref, head_dim, step):
    f32 = jnp.float32
    pair = pl.program_id(0) * o_ref.shape[0] + step
    cols = pl.ds(step * LANES, LANES)
    group = LANES // head_dim
    rows = k_ref.shape[0]
    cum = cum_ref[...]
    lane_head = lax.broadcasted_iota(jnp.int32, (rows, LANES), 1) // head_dim
    weight = jnp.zeros((rows, LANES), f32)
    logs = jnp.zeros((1, LANES), f32)
    for j in range(group):
        col = head_column(cum, pair * group + j)
        last = col[rows - 1 :, :]
        weight = jnp.where(lane_head == j, jnp.exp(last - col), weight)
        logs = jnp.where(lane_head[:1] == j, last, logs)
    scaled = (k_ref[:, cols].astype(f32) * weight).astype(jnp.bfloat16)
    state = lax.dot_general(scaled, v_ref[:, cols], (((0,), (0,)), ((), ())), preferred_element_type=f32)
    lane = lax.broadcasted_iota(jnp.int32, (head_dim, LANES), 1) // head_dim
    packed = state[:head_dim]
    for j in range(1, group):
        packed = jnp.where(lane == j, state[j * head_dim : (j + 1) * head_dim], packed)
    o_ref[step, :head_dim, :] = packed
    tail_row = lax.broadcasted_iota(jnp.int32, (8, LANES), 0)
    o_ref[step, head_dim:, :] = jnp.where(tail_row == 0, jnp.broadcast_to(logs, (8, LANES)), 0.0)


def project_kernel(x_ref, wk_ref, wv_ref, g_ref, k_ref, v_ref, o_ref, cum_ref, cum_t_ref, *, head_dim):
    f32 = jnp.float32
    bf16 = jnp.bfloat16

    @pl.when(pl.program_id(0) == 0)
    def _():
        rows = g_ref.shape[1]
        t_i = lax.broadcasted_iota(jnp.int32, (rows, rows), 0)
        s_i = lax.broadcasted_iota(jnp.int32, (rows, rows), 1)
        lower = jnp.where(s_i <= t_i, 1.0, 0.0).astype(bf16)
        upper = jnp.where(t_i <= s_i, 1.0, 0.0).astype(bf16)
        rest = g_ref[...]
        cum = jnp.zeros(cum_ref.shape, f32)
        cum_t = jnp.zeros(cum_t_ref.shape, f32)
        for _ in range(3):
            part = rest.astype(bf16)
            cum = cum + lax.dot_general(lower, part, (((1,), (1,)), ((), ())), preferred_element_type=f32)
            cum_t = cum_t + jnp.dot(part, upper, preferred_element_type=f32)
            rest = rest - part.astype(f32)
        cum_ref[...] = cum
        cum_t_ref[...] = cum_t

    x = x_ref[...]
    key_sum = jnp.dot(x, wk_ref[...], preferred_element_type=f32)
    k_ref[...] = (key_sum / (1.0 + jnp.exp(-key_sum))).astype(jnp.bfloat16)
    v_ref[...] = jnp.dot(x, wv_ref[...], preferred_element_type=f32).astype(jnp.bfloat16)
    for step in range(o_ref.shape[0]):
        local_pair(k_ref, v_ref, cum_ref, o_ref, head_dim, step)


def project_keys_values(tokens, key_weight, value_weight, log_decay, head_dim):
    rows, depth = tokens.shape
    width = key_weight.shape[1]
    heads = log_decay.shape[1]
    pairs = width // LANES
    per = PER_STEP if pairs % PER_STEP == 0 else 1
    block = pl.BlockSpec((rows, per * LANES), lambda p: (0, p))
    weights = pl.BlockSpec((depth, per * LANES), lambda p: (0, p))
    return pl.pallas_call(
        functools.partial(project_kernel, head_dim=head_dim),
        grid=(pairs // per,),
        in_specs=[
            pl.BlockSpec((rows, depth), lambda p: (0, 0)),
            weights,
            weights,
            pl.BlockSpec((heads, rows), lambda p: (0, 0)),
        ],
        out_specs=[
            block,
            block,
            pl.BlockSpec((per, head_dim + 8, LANES), lambda p: (p, 0, 0)),
            pl.BlockSpec((rows, heads), lambda p: (0, 0)),
            pl.BlockSpec((heads, rows), lambda p: (0, 0)),
        ],
        out_shape=[
            jax.ShapeDtypeStruct((rows, width), jnp.bfloat16),
            jax.ShapeDtypeStruct((rows, width), jnp.bfloat16),
            jax.ShapeDtypeStruct((pairs, head_dim + 8, LANES), jnp.float32),
            jax.ShapeDtypeStruct((rows, heads), jnp.float32),
            jax.ShapeDtypeStruct((heads, rows), jnp.float32),
        ],
        cost_estimate=pl.CostEstimate(
            flops=4 * rows * depth * width + 2 * rows * LANES * width,
            transcendentals=rows * width + rows * heads,
            bytes_accessed=2 * depth * width * 2 + rows * depth * 2 + rows * width * 4,
        ),
    )(tokens, key_weight, value_weight, log_decay.T)


def finish_kernel(q_ref, intra_ref, state_ref, cum_ref, gain_ref, w_ref, o_ref, normed_ref, acc_ref, *, head_dim):
    for step in range(state_ref.shape[0]):
        finish_pair(q_ref, intra_ref, state_ref, cum_ref, gain_ref, normed_ref, head_dim, step)
    part = jnp.dot(normed_ref[...], w_ref[...], preferred_element_type=jnp.float32)
    index = pl.program_id(0)

    @pl.when(index == 0)
    def _():
        acc_ref[...] = part

    @pl.when(index > 0)
    def _():
        acc_ref[...] += part

    @pl.when(index == pl.num_programs(0) - 1)
    def _():
        o_ref[...] = acc_ref[...].astype(o_ref.dtype)


def finish_pair(q_ref, intra_ref, state_ref, cum_ref, gain_ref, o_ref, head_dim, step):
    f32 = jnp.float32
    bf16 = jnp.bfloat16
    pair = pl.program_id(0) * state_ref.shape[0] + step
    cols = pl.ds(step * LANES, LANES)
    group = LANES // head_dim
    rows = q_ref.shape[0]
    state = state_ref[step, :head_dim, :]
    tall = jnp.concatenate([state] * group, axis=0)
    r_head = lax.broadcasted_iota(jnp.int32, (LANES, LANES), 0) // head_dim
    c_head = lax.broadcasted_iota(jnp.int32, (LANES, LANES), 1) // head_dim
    block = jnp.where(r_head == c_head, tall, 0.0)
    q = q_ref[:, cols]
    inter = jnp.zeros((rows, LANES), f32)
    rest = block
    for _ in range(3):
        part = rest.astype(bf16)
        inter = inter + jnp.dot(q, part, preferred_element_type=f32)
        rest = rest - part.astype(f32)
    cum = cum_ref[...]
    lane_head = lax.broadcasted_iota(jnp.int32, (rows, LANES), 1) // head_dim
    growth = jnp.zeros((rows, LANES), f32)
    for j in range(group):
        growth = jnp.where(lane_head == j, jnp.exp(head_column(cum, pair * group + j)), growth)
    attended = intra_ref[:, cols] + inter * growth
    square = attended * attended
    scale = jnp.zeros((rows, LANES), f32)
    for j in range(group):
        mean = jnp.sum(jnp.where(lane_head == j, square, 0.0), axis=1, keepdims=True) / head_dim
        scale = jnp.where(lane_head == j, lax.rsqrt(mean + 1e-05), scale)
    o_ref[:, cols] = (attended * scale * gain_ref[:, cols]).astype(bf16)


def finish(queries, intra, states, cum, norm_gain, output_weight, head_dim):
    rows, width = queries.shape
    heads = cum.shape[1]
    pairs = width // LANES
    out_width = output_weight.shape[1]
    per = 2 if pairs % 2 == 0 else 1
    block = pl.BlockSpec((rows, per * LANES), lambda p: (0, p))
    return pl.pallas_call(
        functools.partial(finish_kernel, head_dim=head_dim),
        grid=(pairs // per,),
        in_specs=[
            block,
            block,
            pl.BlockSpec((per,) + states.shape[1:], lambda p: (p, 0, 0)),
            pl.BlockSpec((rows, heads), lambda p: (0, 0)),
            pl.BlockSpec((1, per * LANES), lambda p: (0, p)),
            pl.BlockSpec((per * LANES, out_width), lambda p: (p, 0)),
        ],
        out_specs=pl.BlockSpec((rows, out_width), lambda p: (0, 0)),
        out_shape=jax.ShapeDtypeStruct((rows, out_width), jnp.bfloat16),
        scratch_shapes=[pltpu.VMEM((rows, per * LANES), jnp.bfloat16), pltpu.VMEM((rows, out_width), jnp.float32)],
        cost_estimate=pl.CostEstimate(
            flops=6 * rows * LANES * LANES * pairs + 2 * rows * width * out_width,
            transcendentals=rows * heads * 2,
            bytes_accessed=rows * width * 8 + width * out_width * 2,
        ),
    )(queries, intra, states, cum, norm_gain.reshape(1, width), output_weight)


def combine(earlier, later):
    body = earlier.shape[1] - 8
    row = lax.broadcasted_iota(jnp.int32, earlier.shape, 1)
    scale = jnp.where(row < body, jnp.exp(later[:, body : body + 1, :]), 1.0)
    return scale * earlier + later


def exclusive_scan(own, count):
    flat = lax.axis_index(AXES)
    core = flat % 2
    chip = flat // 2
    chips = count // 2
    half = own.shape[0] // 2
    partner = [(i, i ^ 1) for i in range(count)]
    got = lax.ppermute(jnp.where(core == 0, own[half:], own[:half]), AXES, partner)
    through = jnp.where(core == 0, combine(own[:half], got), combine(got, own[half:]))
    before = jnp.zeros_like(through)
    received = []
    bit = 1
    while bit < chips:
        perm = [(i, i ^ (2 * bit)) for i in range(count)]
        exchanged = lax.ppermute(through, AXES, perm)
        received.append(exchanged)
        lower = (chip & bit) != 0
        before = jnp.where(lower, combine(exchanged, before), before)
        bit *= 2
        if bit < chips:
            through = jnp.where(lower, combine(exchanged, through), combine(through, exchanged))
    back = lax.ppermute(jnp.where(core == 0, combine(before, own[:half]), before), AXES, partner)
    whole = jnp.where(
        core == 0, jnp.concatenate([before, back]), jnp.concatenate([back, combine(before, got)])
    )
    return whole, received


def layer(count, tokens, log_decay, query_weight, key_weight, value_weight, norm_gain, output_weight):
    f32 = jnp.float32
    bf16 = jnp.bfloat16
    heads = log_decay.shape[1]
    dim = key_weight.shape[1] // heads
    keys, value_rows, packed, cum, cum_t = project_keys_values(tokens, key_weight, value_weight, log_decay, dim)
    incoming, _ = exclusive_scan(packed, count)

    queries = jax.nn.silu(jnp.dot(tokens, query_weight, preferred_element_type=f32)).astype(bf16)
    blocks = keys.shape[1] // LANES
    intra = None
    cuts = (0, blocks // 2, (3 * blocks) // 4, blocks)
    for part in range(3):
        intra = intra_attention(queries, keys, value_rows, cum, cum_t, dim, cuts[part], cuts[part + 1], intra)
    return finish(queries, intra, incoming, cum, norm_gain, output_weight, dim)


def solution(mesh):
    count = mesh.shape["outer"] * mesh.shape["inner"]
    in_specs = (P(AXES, None), P(AXES, None), P(), P(), P(), P(), P())
    out_specs = P(AXES, None)
    body = lambda *args: layer(count, *args)
    return jax.shard_map(body, mesh=mesh, in_specs=in_specs, out_specs=out_specs, check_vma=False)
```

```python
import functools

import jax
import jax.numpy as jnp
from jax import lax
from jax.experimental import pallas as pl
from jax.experimental.pallas import tpu as pltpu
from jax.sharding import PartitionSpec as P


AXES = ("outer", "inner")

LANES = 128
PER_STEP = 4


def intra_kernel(q_ref, k_ref, v_ref, cum_ref, cum_t_ref, *rest, head_dim, first):
    o_ref = rest[-1]
    f32 = jnp.float32
    pair = pl.program_id(0) + first
    group = LANES // head_dim
    rows = q_ref.shape[0]
    q = q_ref[...]
    k = k_ref[...]
    v = v_ref[...]
    lane_head = lax.broadcasted_iota(jnp.int32, q.shape, 1) // head_dim
    t_i = lax.broadcasted_iota(jnp.int32, (rows, rows), 0)
    s_i = lax.broadcasted_iota(jnp.int32, (rows, rows), 1)
    lower = s_i <= t_i
    cum = cum_ref[...]
    cum_t = cum_t_ref[...]
    col_head = lax.broadcasted_iota(jnp.int32, cum.shape, 1)
    row_head = lax.broadcasted_iota(jnp.int32, cum_t.shape, 0)
    out = None
    for j in range(group):
        head = pair * group + j
        mine = lane_head == j
        q_j = jnp.where(mine, q, jnp.zeros_like(q))
        scores = lax.dot_general(q_j, k, (((1,), (1,)), ((), ())), preferred_element_type=f32)
        col = jnp.sum(jnp.where(col_head == head, cum, 0.0), axis=1, keepdims=True)
        row = jnp.sum(jnp.where(row_head == head, cum_t, 0.0), axis=0, keepdims=True)
        diff = jnp.where(lower, col - row, 0.0)
        decay = jnp.where(lower, jnp.exp(diff), 0.0)
        weights = (scores * decay).astype(jnp.bfloat16)
        o_j = jnp.dot(weights, v, preferred_element_type=f32)
        out = o_j if out is None else jnp.where(mine, o_j, out)
    o_ref[...] = out


def intra_attention(queries, keys, value_rows, cum, cum_t, head_dim, first, stop, into=None):
    rows, width = queries.shape
    heads = cum.shape[1]
    block = pl.BlockSpec((rows, LANES), lambda p: (0, p + first))
    out_block = block
    extra = () if into is None else (into,)
    extra_specs = [] if into is None else [pl.BlockSpec(memory_space=pl.ANY)]
    whole = lambda shape: pl.BlockSpec(shape, lambda p: (0, 0))
    steps = stop - first
    flops = 4 * rows * rows * LANES * (LANES // head_dim) * steps
    return pl.pallas_call(
        functools.partial(intra_kernel, head_dim=head_dim, first=first),
        grid=(steps,),
        in_specs=[block, block, block, whole((rows, heads)), whole((heads, rows))] + extra_specs,
        out_specs=out_block,
        out_shape=jax.ShapeDtypeStruct((rows, width), jnp.float32),
        input_output_aliases={} if into is None else {5: 0},
        cost_estimate=pl.CostEstimate(
            flops=flops,
            transcendentals=rows * rows * steps * (LANES // head_dim),
            bytes_accessed=rows * steps * LANES * 10,
        ),
    )(queries, keys, value_rows, cum, cum_t, *extra)


def head_column(table, head):
    lane = lax.broadcasted_iota(jnp.int32, table.shape, 1)
    return jnp.sum(jnp.where(lane == head, table, 0.0), axis=1, keepdims=True)


def local_pair(k_ref, v_ref, cum_ref, o_ref, head_dim, step):
    f32 = jnp.float32
    pair = pl.program_id(0) * o_ref.shape[0] + step
    cols = pl.ds(step * LANES, LANES)
    group = LANES // head_dim
    rows = k_ref.shape[0]
    cum = cum_ref[...]
    lane_head = lax.broadcasted_iota(jnp.int32, (rows, LANES), 1) // head_dim
    weight = jnp.zeros((rows, LANES), f32)
    logs = jnp.zeros((1, LANES), f32)
    for j in range(group):
        col = head_column(cum, pair * group + j)
        last = col[rows - 1 :, :]
        weight = jnp.where(lane_head == j, jnp.exp(last - col), weight)
        logs = jnp.where(lane_head[:1] == j, last, logs)
    scaled = (k_ref[:, cols].astype(f32) * weight).astype(jnp.bfloat16)
    state = lax.dot_general(scaled, v_ref[:, cols], (((0,), (0,)), ((), ())), preferred_element_type=f32)
    lane = lax.broadcasted_iota(jnp.int32, (head_dim, LANES), 1) // head_dim
    packed = state[:head_dim]
    for j in range(1, group):
        packed = jnp.where(lane == j, state[j * head_dim : (j + 1) * head_dim], packed)
    o_ref[step, :head_dim, :] = packed
    tail_row = lax.broadcasted_iota(jnp.int32, (8, LANES), 0)
    o_ref[step, head_dim:, :] = jnp.where(tail_row == 0, jnp.broadcast_to(logs, (8, LANES)), 0.0)


def project_kernel(x_ref, wk_ref, wv_ref, g_ref, k_ref, v_ref, o_ref, cum_ref, cum_t_ref, *, head_dim):
    f32 = jnp.float32
    bf16 = jnp.bfloat16

    @pl.when(pl.program_id(0) == 0)
    def _():
        rows = g_ref.shape[1]
        t_i = lax.broadcasted_iota(jnp.int32, (rows, rows), 0)
        s_i = lax.broadcasted_iota(jnp.int32, (rows, rows), 1)
        lower = jnp.where(s_i <= t_i, 1.0, 0.0).astype(bf16)
        upper = jnp.where(t_i <= s_i, 1.0, 0.0).astype(bf16)
        rest = g_ref[...]
        cum = jnp.zeros(cum_ref.shape, f32)
        cum_t = jnp.zeros(cum_t_ref.shape, f32)
        for _ in range(3):
            part = rest.astype(bf16)
            cum = cum + lax.dot_general(lower, part, (((1,), (1,)), ((), ())), preferred_element_type=f32)
            cum_t = cum_t + jnp.dot(part, upper, preferred_element_type=f32)
            rest = rest - part.astype(f32)
        cum_ref[...] = cum
        cum_t_ref[...] = cum_t

    x = x_ref[...]
    key_sum = jnp.dot(x, wk_ref[...], preferred_element_type=f32)
    k_ref[...] = (key_sum / (1.0 + jnp.exp(-key_sum))).astype(jnp.bfloat16)
    v_ref[...] = jnp.dot(x, wv_ref[...], preferred_element_type=f32).astype(jnp.bfloat16)
    for step in range(o_ref.shape[0]):
        local_pair(k_ref, v_ref, cum_ref, o_ref, head_dim, step)


def project_keys_values(tokens, key_weight, value_weight, log_decay, head_dim):
    rows, depth = tokens.shape
    width = key_weight.shape[1]
    heads = log_decay.shape[1]
    pairs = width // LANES
    per = PER_STEP if pairs % PER_STEP == 0 else 1
    block = pl.BlockSpec((rows, per * LANES), lambda p: (0, p))
    weights = pl.BlockSpec((depth, per * LANES), lambda p: (0, p))
    return pl.pallas_call(
        functools.partial(project_kernel, head_dim=head_dim),
        grid=(pairs // per,),
        in_specs=[
            pl.BlockSpec((rows, depth), lambda p: (0, 0)),
            weights,
            weights,
            pl.BlockSpec((heads, rows), lambda p: (0, 0)),
        ],
        out_specs=[
            block,
            block,
            pl.BlockSpec((per, head_dim + 8, LANES), lambda p: (p, 0, 0)),
            pl.BlockSpec((rows, heads), lambda p: (0, 0)),
            pl.BlockSpec((heads, rows), lambda p: (0, 0)),
        ],
        out_shape=[
            jax.ShapeDtypeStruct((rows, width), jnp.bfloat16),
            jax.ShapeDtypeStruct((rows, width), jnp.bfloat16),
            jax.ShapeDtypeStruct((pairs, head_dim + 8, LANES), jnp.float32),
            jax.ShapeDtypeStruct((rows, heads), jnp.float32),
            jax.ShapeDtypeStruct((heads, rows), jnp.float32),
        ],
        cost_estimate=pl.CostEstimate(
            flops=4 * rows * depth * width + 2 * rows * LANES * width,
            transcendentals=rows * width + rows * heads,
            bytes_accessed=2 * depth * width * 2 + rows * depth * 2 + rows * width * 4,
        ),
    )(tokens, key_weight, value_weight, log_decay.T)


def finish_kernel(q_ref, intra_ref, state_ref, cum_ref, gain_ref, w_ref, o_ref, normed_ref, acc_ref, *, head_dim):
    for step in range(state_ref.shape[0]):
        finish_pair(q_ref, intra_ref, state_ref, cum_ref, gain_ref, normed_ref, head_dim, step)
    part = jnp.dot(normed_ref[...], w_ref[...], preferred_element_type=jnp.float32)
    index = pl.program_id(0)

    @pl.when(index == 0)
    def _():
        acc_ref[...] = part

    @pl.when(index > 0)
    def _():
        acc_ref[...] += part

    @pl.when(index == pl.num_programs(0) - 1)
    def _():
        o_ref[...] = acc_ref[...].astype(o_ref.dtype)


def finish_pair(q_ref, intra_ref, state_ref, cum_ref, gain_ref, o_ref, head_dim, step):
    f32 = jnp.float32
    bf16 = jnp.bfloat16
    pair = pl.program_id(0) * state_ref.shape[0] + step
    cols = pl.ds(step * LANES, LANES)
    group = LANES // head_dim
    rows = q_ref.shape[0]
    state = state_ref[step, :head_dim, :]
    tall = jnp.concatenate([state] * group, axis=0)
    r_head = lax.broadcasted_iota(jnp.int32, (LANES, LANES), 0) // head_dim
    c_head = lax.broadcasted_iota(jnp.int32, (LANES, LANES), 1) // head_dim
    block = jnp.where(r_head == c_head, tall, 0.0)
    q = q_ref[:, cols]
    inter = jnp.zeros((rows, LANES), f32)
    rest = block
    for _ in range(3):
        part = rest.astype(bf16)
        inter = inter + jnp.dot(q, part, preferred_element_type=f32)
        rest = rest - part.astype(f32)
    cum = cum_ref[...]
    lane_head = lax.broadcasted_iota(jnp.int32, (rows, LANES), 1) // head_dim
    growth = jnp.zeros((rows, LANES), f32)
    for j in range(group):
        growth = jnp.where(lane_head == j, jnp.exp(head_column(cum, pair * group + j)), growth)
    attended = intra_ref[:, cols] + inter * growth
    square = attended * attended
    scale = jnp.zeros((rows, LANES), f32)
    for j in range(group):
        mean = jnp.sum(jnp.where(lane_head == j, square, 0.0), axis=1, keepdims=True) / head_dim
        scale = jnp.where(lane_head == j, lax.rsqrt(mean + 1e-05), scale)
    o_ref[:, cols] = (attended * scale * gain_ref[:, cols]).astype(bf16)


def finish(queries, intra, states, cum, norm_gain, output_weight, head_dim):
    rows, width = queries.shape
    heads = cum.shape[1]
    pairs = width // LANES
    out_width = output_weight.shape[1]
    per = pairs
    block = pl.BlockSpec((rows, per * LANES), lambda p: (0, p))
    return pl.pallas_call(
        functools.partial(finish_kernel, head_dim=head_dim),
        grid=(pairs // per,),
        in_specs=[
            block,
            block,
            pl.BlockSpec((per,) + states.shape[1:], lambda p: (p, 0, 0)),
            pl.BlockSpec((rows, heads), lambda p: (0, 0)),
            pl.BlockSpec((1, per * LANES), lambda p: (0, p)),
            pl.BlockSpec((per * LANES, out_width), lambda p: (p, 0)),
        ],
        out_specs=pl.BlockSpec((rows, out_width), lambda p: (0, 0)),
        out_shape=jax.ShapeDtypeStruct((rows, out_width), jnp.bfloat16),
        scratch_shapes=[pltpu.VMEM((rows, per * LANES), jnp.bfloat16), pltpu.VMEM((rows, out_width), jnp.float32)],
        cost_estimate=pl.CostEstimate(
            flops=6 * rows * LANES * LANES * pairs + 2 * rows * width * out_width,
            transcendentals=rows * heads * 2,
            bytes_accessed=rows * width * 8 + width * out_width * 2,
        ),
    )(queries, intra, states, cum, norm_gain.reshape(1, width), output_weight)


def combine(earlier, later):
    body = earlier.shape[1] - 8
    row = lax.broadcasted_iota(jnp.int32, earlier.shape, 1)
    scale = jnp.where(row < body, jnp.exp(later[:, body : body + 1, :]), 1.0)
    return scale * earlier + later


def exclusive_scan(own, count):
    flat = lax.axis_index(AXES)
    core = flat % 2
    chip = flat // 2
    chips = count // 2
    half = own.shape[0] // 2
    partner = [(i, i ^ 1) for i in range(count)]
    other = lax.ppermute(own, AXES, partner)
    got = jnp.where(core == 0, other[:half], other[half:])
    through = jnp.where(core == 0, combine(own[:half], got), combine(got, own[half:]))
    before = jnp.zeros_like(through)
    received = []
    bit = 1
    while bit < chips:
        perm = [(i, i ^ (2 * bit)) for i in range(count)]
        exchanged = lax.ppermute(through, AXES, perm)
        received.append(exchanged)
        lower = (chip & bit) != 0
        before = jnp.where(lower, combine(exchanged, before), before)
        bit *= 2
        if bit < chips:
            through = jnp.where(lower, combine(exchanged, through), combine(through, exchanged))
    back = lax.ppermute(jnp.where(core == 0, combine(before, own[:half]), before), AXES, partner)
    whole = jnp.where(
        core == 0, jnp.concatenate([before, back]), jnp.concatenate([back, combine(before, got)])
    )
    return whole, received


def layer(count, tokens, log_decay, query_weight, key_weight, value_weight, norm_gain, output_weight):
    f32 = jnp.float32
    bf16 = jnp.bfloat16
    heads = log_decay.shape[1]
    dim = key_weight.shape[1] // heads
    keys, value_rows, packed, cum, cum_t = project_keys_values(tokens, key_weight, value_weight, log_decay, dim)
    incoming, _ = exclusive_scan(packed, count)

    queries = jax.nn.silu(jnp.dot(tokens, query_weight, preferred_element_type=f32)).astype(bf16)
    blocks = keys.shape[1] // LANES
    intra = None
    cuts = (0, blocks // 2, (3 * blocks) // 4, blocks)
    for part in range(3):
        intra = intra_attention(queries, keys, value_rows, cum, cum_t, dim, cuts[part], cuts[part + 1], intra)
    return finish(queries, intra, incoming, cum, norm_gain, output_weight, dim)


def solution(mesh):
    count = mesh.shape["outer"] * mesh.shape["inner"]
    in_specs = (P(AXES, None), P(AXES, None), P(), P(), P(), P(), P())
    out_specs = P(AXES, None)
    body = lambda *args: layer(count, *args)
    return jax.shard_map(body, mesh=mesh, in_specs=in_specs, out_specs=out_specs, check_vma=False)
```

```python
import functools

import jax
import jax.numpy as jnp
from jax import lax
from jax.experimental import pallas as pl
from jax.experimental.pallas import tpu as pltpu
from jax.sharding import PartitionSpec as P


AXES = ("outer", "inner")

LANES = 128
PER_STEP = 4


def intra_kernel(q_ref, k_ref, v_ref, cum_ref, cum_t_ref, *rest, head_dim, first):
    o_ref = rest[-1]
    f32 = jnp.float32
    pair = pl.program_id(0) + first
    group = LANES // head_dim
    rows = q_ref.shape[0]
    q = q_ref[...]
    k = k_ref[...]
    v = v_ref[...]
    lane_head = lax.broadcasted_iota(jnp.int32, q.shape, 1) // head_dim
    t_i = lax.broadcasted_iota(jnp.int32, (rows, rows), 0)
    s_i = lax.broadcasted_iota(jnp.int32, (rows, rows), 1)
    lower = s_i <= t_i
    cum = cum_ref[...]
    cum_t = cum_t_ref[...]
    col_head = lax.broadcasted_iota(jnp.int32, cum.shape, 1)
    row_head = lax.broadcasted_iota(jnp.int32, cum_t.shape, 0)
    out = None
    for j in range(group):
        head = pair * group + j
        mine = lane_head == j
        q_j = jnp.where(mine, q, jnp.zeros_like(q))
        scores = lax.dot_general(q_j, k, (((1,), (1,)), ((), ())), preferred_element_type=f32)
        col = jnp.sum(jnp.where(col_head == head, cum, 0.0), axis=1, keepdims=True)
        row = jnp.sum(jnp.where(row_head == head, cum_t, 0.0), axis=0, keepdims=True)
        diff = jnp.where(lower, col - row, 0.0)
        decay = jnp.where(lower, jnp.exp(diff), 0.0)
        weights = (scores * decay).astype(jnp.bfloat16)
        o_j = jnp.dot(weights, v, preferred_element_type=f32)
        out = o_j if out is None else jnp.where(mine, o_j, out)
    o_ref[...] = out


def intra_attention(queries, keys, value_rows, cum, cum_t, head_dim, first, stop, into=None):
    rows, width = queries.shape
    heads = cum.shape[1]
    block = pl.BlockSpec((rows, LANES), lambda p: (0, p + first))
    out_block = block
    extra = () if into is None else (into,)
    extra_specs = [] if into is None else [pl.BlockSpec(memory_space=pl.ANY)]
    whole = lambda shape: pl.BlockSpec(shape, lambda p: (0, 0))
    steps = stop - first
    flops = 4 * rows * rows * LANES * (LANES // head_dim) * steps
    return pl.pallas_call(
        functools.partial(intra_kernel, head_dim=head_dim, first=first),
        grid=(steps,),
        in_specs=[block, block, block, whole((rows, heads)), whole((heads, rows))] + extra_specs,
        out_specs=out_block,
        out_shape=jax.ShapeDtypeStruct((rows, width), jnp.float32),
        input_output_aliases={} if into is None else {5: 0},
        cost_estimate=pl.CostEstimate(
            flops=flops,
            transcendentals=rows * rows * steps * (LANES // head_dim),
            bytes_accessed=rows * steps * LANES * 10,
        ),
    )(queries, keys, value_rows, cum, cum_t, *extra)


def head_column(table, head):
    lane = lax.broadcasted_iota(jnp.int32, table.shape, 1)
    return jnp.sum(jnp.where(lane == head, table, 0.0), axis=1, keepdims=True)


def local_pair(k_ref, v_ref, cum_ref, o_ref, head_dim, step):
    f32 = jnp.float32
    pair = pl.program_id(0) * o_ref.shape[0] + step
    cols = pl.ds(step * LANES, LANES)
    group = LANES // head_dim
    rows = k_ref.shape[0]
    cum = cum_ref[...]
    lane_head = lax.broadcasted_iota(jnp.int32, (rows, LANES), 1) // head_dim
    weight = jnp.zeros((rows, LANES), f32)
    logs = jnp.zeros((1, LANES), f32)
    for j in range(group):
        col = head_column(cum, pair * group + j)
        last = col[rows - 1 :, :]
        weight = jnp.where(lane_head == j, jnp.exp(last - col), weight)
        logs = jnp.where(lane_head[:1] == j, last, logs)
    scaled = (k_ref[:, cols].astype(f32) * weight).astype(jnp.bfloat16)
    state = lax.dot_general(scaled, v_ref[:, cols], (((0,), (0,)), ((), ())), preferred_element_type=f32)
    lane = lax.broadcasted_iota(jnp.int32, (head_dim, LANES), 1) // head_dim
    packed = state[:head_dim]
    for j in range(1, group):
        packed = jnp.where(lane == j, state[j * head_dim : (j + 1) * head_dim], packed)
    o_ref[step, :head_dim, :] = packed
    tail_row = lax.broadcasted_iota(jnp.int32, (8, LANES), 0)
    o_ref[step, head_dim:, :] = jnp.where(tail_row == 0, jnp.broadcast_to(logs, (8, LANES)), 0.0)


def project_kernel(x_ref, wk_ref, wv_ref, g_ref, k_ref, v_ref, o_ref, cum_ref, cum_t_ref, *, head_dim):
    f32 = jnp.float32
    bf16 = jnp.bfloat16
    @pl.when(pl.program_id(0) == 0)
    def _():
        rows = g_ref.shape[1]
        t_i = lax.broadcasted_iota(jnp.int32, (rows, rows), 0)
        s_i = lax.broadcasted_iota(jnp.int32, (rows, rows), 1)
        lower = jnp.where(s_i <= t_i, 1.0, 0.0).astype(bf16)
        upper = jnp.where(t_i <= s_i, 1.0, 0.0).astype(bf16)
        rest = g_ref[...]
        cum = jnp.zeros(cum_ref.shape, f32)
        cum_t = jnp.zeros(cum_t_ref.shape, f32)
        for _ in range(3):
            part = rest.astype(bf16)
            cum = cum + lax.dot_general(lower, part, (((1,), (1,)), ((), ())), preferred_element_type=f32)
            cum_t = cum_t + jnp.dot(part, upper, preferred_element_type=f32)
            rest = rest - part.astype(f32)
        cum_ref[...] = cum
        cum_t_ref[...] = cum_t

    x = x_ref[...]
    key_sum = jnp.dot(x, wk_ref[...], preferred_element_type=f32)
    k_ref[...] = (key_sum / (1.0 + jnp.exp(-key_sum))).astype(jnp.bfloat16)
    v_ref[...] = jnp.dot(x, wv_ref[...], preferred_element_type=f32).astype(jnp.bfloat16)
    for step in range(o_ref.shape[0]):
        local_pair(k_ref, v_ref, cum_ref, o_ref, head_dim, step)


def project_keys_values(tokens, key_weight, value_weight, log_decay, head_dim):
    rows, depth = tokens.shape
    width = key_weight.shape[1]
    heads = log_decay.shape[1]
    pairs = width // LANES
    per = PER_STEP if pairs % PER_STEP == 0 else 1
    block = pl.BlockSpec((rows, per * LANES), lambda p: (0, p))
    weights = pl.BlockSpec((depth, per * LANES), lambda p: (0, p))
    return pl.pallas_call(
        functools.partial(project_kernel, head_dim=head_dim),
        grid=(pairs // per,),
        in_specs=[
            pl.BlockSpec((rows, depth), lambda p: (0, 0)),
            weights,
            weights,
            pl.BlockSpec((heads, rows), lambda p: (0, 0)),
        ],
        out_specs=[
            block,
            block,
            pl.BlockSpec((per, head_dim + 8, LANES), lambda p: (p, 0, 0)),
            pl.BlockSpec((rows, heads), lambda p: (0, 0)),
            pl.BlockSpec((heads, rows), lambda p: (0, 0)),
        ],
        out_shape=[
            jax.ShapeDtypeStruct((rows, width), jnp.bfloat16),
            jax.ShapeDtypeStruct((rows, width), jnp.bfloat16),
            jax.ShapeDtypeStruct((pairs, head_dim + 8, LANES), jnp.float32),
            jax.ShapeDtypeStruct((rows, heads), jnp.float32),
            jax.ShapeDtypeStruct((heads, rows), jnp.float32),
        ],
        cost_estimate=pl.CostEstimate(
            flops=4 * rows * depth * width + 2 * rows * LANES * width,
            transcendentals=rows * width + rows * heads,
            bytes_accessed=2 * depth * width * 2 + rows * depth * 2 + rows * width * 4,
        ),
    )(tokens, key_weight, value_weight, log_decay.T)


def finish_kernel(
    core_ref, q_ref, intra_ref, mine_ref, back_ref, mixed_ref, cum_ref, gain_ref, w_ref, o_ref, normed_ref, *, head_dim
):
    head_dim_rows = slice(0, head_dim)
    half = mine_ref.shape[0]
    first = core_ref[0] == 0
    for step in range(2 * half):
        if step < half:
            state = jnp.where(first, mine_ref[step, head_dim_rows, :], back_ref[step, head_dim_rows, :])
        else:
            other = step - half
            state = jnp.where(first, back_ref[other, head_dim_rows, :], mixed_ref[other, head_dim_rows, :])
        finish_pair(q_ref, intra_ref, state, cum_ref, gain_ref, normed_ref, head_dim, step)
    o_ref[...] = jnp.dot(normed_ref[...], w_ref[...], preferred_element_type=jnp.float32).astype(o_ref.dtype)


def finish_pair(q_ref, intra_ref, state, cum_ref, gain_ref, o_ref, head_dim, step):
    f32 = jnp.float32
    bf16 = jnp.bfloat16
    pair = step
    cols = pl.ds(step * LANES, LANES)
    group = LANES // head_dim
    rows = q_ref.shape[0]
    tall = jnp.concatenate([state] * group, axis=0)
    r_head = lax.broadcasted_iota(jnp.int32, (LANES, LANES), 0) // head_dim
    c_head = lax.broadcasted_iota(jnp.int32, (LANES, LANES), 1) // head_dim
    block = jnp.where(r_head == c_head, tall, 0.0)
    q = q_ref[:, cols]
    inter = jnp.zeros((rows, LANES), f32)
    rest = block
    for _ in range(3):
        part = rest.astype(bf16)
        inter = inter + jnp.dot(q, part, preferred_element_type=f32)
        rest = rest - part.astype(f32)
    cum = cum_ref[...]
    lane_head = lax.broadcasted_iota(jnp.int32, (rows, LANES), 1) // head_dim
    growth = jnp.zeros((rows, LANES), f32)
    for j in range(group):
        growth = jnp.where(lane_head == j, jnp.exp(head_column(cum, pair * group + j)), growth)
    attended = intra_ref[:, cols] + inter * growth
    square = attended * attended
    scale = jnp.zeros((rows, LANES), f32)
    for j in range(group):
        mean = jnp.sum(jnp.where(lane_head == j, square, 0.0), axis=1, keepdims=True) / head_dim
        scale = jnp.where(lane_head == j, lax.rsqrt(mean + 1e-05), scale)
    o_ref[:, cols] = (attended * scale * gain_ref[:, cols]).astype(bf16)


def finish(queries, intra, states, core, cum, norm_gain, output_weight, head_dim):
    rows, width = queries.shape
    heads = cum.shape[1]
    pairs = width // LANES
    out_width = output_weight.shape[1]
    whole = lambda shape: pl.BlockSpec(shape, lambda p: (0,) * len(shape))
    return pl.pallas_call(
        functools.partial(finish_kernel, head_dim=head_dim),
        grid=(1,),
        in_specs=[pl.BlockSpec(memory_space=pltpu.SMEM), whole((rows, width)), whole((rows, width))]
        + [whole(part.shape) for part in states]
        + [whole((rows, heads)), whole((1, width)), whole((width, out_width))],
        out_specs=whole((rows, out_width)),
        out_shape=jax.ShapeDtypeStruct((rows, out_width), jnp.bfloat16),
        scratch_shapes=[pltpu.VMEM((rows, width), jnp.bfloat16)],
        cost_estimate=pl.CostEstimate(
            flops=6 * rows * LANES * LANES * pairs + 2 * rows * width * out_width,
            transcendentals=rows * heads * 2,
            bytes_accessed=rows * width * 8 + width * out_width * 2,
        ),
    )(jnp.reshape(core, (1,)).astype(jnp.int32), queries, intra, *states, cum, norm_gain.reshape(1, width), output_weight)


def combine(earlier, later):
    body = earlier.shape[1] - 8
    row = lax.broadcasted_iota(jnp.int32, earlier.shape, 1)
    scale = jnp.where(row < body, jnp.exp(later[:, body : body + 1, :]), 1.0)
    return scale * earlier + later


def exclusive_scan(own, count):
    flat = lax.axis_index(AXES)
    core = flat % 2
    chip = flat // 2
    chips = count // 2
    half = own.shape[0] // 2
    partner = [(i, i ^ 1) for i in range(count)]
    other = lax.ppermute(own, AXES, partner)
    got = jnp.where(core == 0, other[:half], other[half:])
    through = jnp.where(core == 0, combine(own[:half], got), combine(got, own[half:]))
    before = jnp.zeros_like(through)
    received = []
    bit = 1
    while bit < chips:
        perm = [(i, i ^ (2 * bit)) for i in range(count)]
        exchanged = lax.ppermute(through, AXES, perm)
        received.append(exchanged)
        lower = (chip & bit) != 0
        before = jnp.where(lower, combine(exchanged, before), before)
        bit *= 2
        if bit < chips:
            through = jnp.where(lower, combine(exchanged, through), combine(through, exchanged))
    back = lax.ppermute(jnp.where(core == 0, combine(before, own[:half]), before), AXES, partner)
    return (before, back, combine(before, got)), received


def layer(count, tokens, log_decay, query_weight, key_weight, value_weight, norm_gain, output_weight):
    f32 = jnp.float32
    bf16 = jnp.bfloat16
    heads = log_decay.shape[1]
    dim = key_weight.shape[1] // heads
    keys, value_rows, packed, cum, cum_t = project_keys_values(tokens, key_weight, value_weight, log_decay, dim)
    states, _ = exclusive_scan(packed, count)

    queries = jax.nn.silu(jnp.dot(tokens, query_weight, preferred_element_type=f32)).astype(bf16)
    blocks = keys.shape[1] // LANES
    intra = None
    cuts = (0, blocks // 2, (3 * blocks) // 4, blocks)
    for part in range(3):
        intra = intra_attention(queries, keys, value_rows, cum, cum_t, dim, cuts[part], cuts[part + 1], intra)
    core = lax.axis_index(AXES) % 2
    return finish(queries, intra, states, core, cum, norm_gain, output_weight, dim)


def solution(mesh):
    count = mesh.shape["outer"] * mesh.shape["inner"]
    in_specs = (P(AXES, None), P(AXES, None), P(), P(), P(), P(), P())
    out_specs = P(AXES, None)
    body = lambda *args: layer(count, *args)
    return jax.shard_map(body, mesh=mesh, in_specs=in_specs, out_specs=out_specs, check_vma=False)
```

```python
import functools

import jax
import jax.numpy as jnp
from jax import lax
from jax.experimental import pallas as pl
from jax.experimental.pallas import tpu as pltpu
from jax.sharding import PartitionSpec as P


AXES = ("outer", "inner")

LANES = 128
PER_STEP = 4


def intra_kernel(q_ref, k_ref, v_ref, cum_ref, cum_t_ref, *rest, head_dim, first):
    o_ref = rest[-1]
    f32 = jnp.float32
    pair = pl.program_id(0) + first
    group = LANES // head_dim
    rows = q_ref.shape[0]
    q = q_ref[...]
    k = k_ref[...]
    v = v_ref[...]
    lane_head = lax.broadcasted_iota(jnp.int32, q.shape, 1) // head_dim
    t_i = lax.broadcasted_iota(jnp.int32, (rows, rows), 0)
    s_i = lax.broadcasted_iota(jnp.int32, (rows, rows), 1)
    lower = s_i <= t_i
    cum = cum_ref[...]
    cum_t = cum_t_ref[...]
    col_head = lax.broadcasted_iota(jnp.int32, cum.shape, 1)
    row_head = lax.broadcasted_iota(jnp.int32, cum_t.shape, 0)
    out = None
    for j in range(group):
        head = pair * group + j
        mine = lane_head == j
        q_j = jnp.where(mine, q, jnp.zeros_like(q))
        scores = lax.dot_general(q_j, k, (((1,), (1,)), ((), ())), preferred_element_type=f32)
        col = jnp.sum(jnp.where(col_head == head, cum, 0.0), axis=1, keepdims=True)
        row = jnp.sum(jnp.where(row_head == head, cum_t, 0.0), axis=0, keepdims=True)
        diff = jnp.where(lower, col - row, 0.0)
        decay = jnp.where(lower, jnp.exp(diff), 0.0)
        weights = (scores * decay).astype(jnp.bfloat16)
        o_j = jnp.dot(weights, v, preferred_element_type=f32)
        out = o_j if out is None else jnp.where(mine, o_j, out)
    o_ref[...] = out


def intra_attention(queries, keys, value_rows, cum, cum_t, head_dim, first, stop, into=None):
    rows, width = queries.shape
    heads = cum.shape[1]
    block = pl.BlockSpec((rows, LANES), lambda p: (0, p + first))
    out_block = block
    extra = () if into is None else (into,)
    extra_specs = [] if into is None else [pl.BlockSpec(memory_space=pl.ANY)]
    whole = lambda shape: pl.BlockSpec(shape, lambda p: (0, 0))
    steps = stop - first
    flops = 4 * rows * rows * LANES * (LANES // head_dim) * steps
    return pl.pallas_call(
        functools.partial(intra_kernel, head_dim=head_dim, first=first),
        grid=(steps,),
        in_specs=[block, block, block, whole((rows, heads)), whole((heads, rows))] + extra_specs,
        out_specs=out_block,
        out_shape=jax.ShapeDtypeStruct((rows, width), jnp.float32),
        input_output_aliases={} if into is None else {5: 0},
        cost_estimate=pl.CostEstimate(
            flops=flops,
            transcendentals=rows * rows * steps * (LANES // head_dim),
            bytes_accessed=rows * steps * LANES * 10,
        ),
    )(queries, keys, value_rows, cum, cum_t, *extra)


def head_column(table, head):
    lane = lax.broadcasted_iota(jnp.int32, table.shape, 1)
    return jnp.sum(jnp.where(lane == head, table, 0.0), axis=1, keepdims=True)


def local_pair(k_ref, v_ref, cum_ref, o_ref, head_dim, step):
    f32 = jnp.float32
    pair = pl.program_id(0) * o_ref.shape[0] + step
    cols = pl.ds(step * LANES, LANES)
    group = LANES // head_dim
    rows = k_ref.shape[0]
    cum = cum_ref[...]
    lane_head = lax.broadcasted_iota(jnp.int32, (rows, LANES), 1) // head_dim
    weight = jnp.zeros((rows, LANES), f32)
    logs = jnp.zeros((1, LANES), f32)
    for j in range(group):
        col = head_column(cum, pair * group + j)
        last = col[rows - 1 :, :]
        weight = jnp.where(lane_head == j, jnp.exp(last - col), weight)
        logs = jnp.where(lane_head[:1] == j, last, logs)
    scaled = (k_ref[:, cols].astype(f32) * weight).astype(jnp.bfloat16)
    state = lax.dot_general(scaled, v_ref[:, cols], (((0,), (0,)), ((), ())), preferred_element_type=f32)
    lane = lax.broadcasted_iota(jnp.int32, (head_dim, LANES), 1) // head_dim
    packed = state[:head_dim]
    for j in range(1, group):
        packed = jnp.where(lane == j, state[j * head_dim : (j + 1) * head_dim], packed)
    o_ref[step, :head_dim, :] = packed
    tail_row = lax.broadcasted_iota(jnp.int32, (8, LANES), 0)
    o_ref[step, head_dim:, :] = jnp.where(tail_row == 0, jnp.broadcast_to(logs, (8, LANES)), 0.0)


def project_kernel(x_ref, wk_ref, wv_ref, g_ref, k_ref, v_ref, o_ref, cum_ref, cum_t_ref, *, head_dim):
    f32 = jnp.float32
    bf16 = jnp.bfloat16

    @pl.when(pl.program_id(0) == 0)
    def _():
        rows = g_ref.shape[1]
        t_i = lax.broadcasted_iota(jnp.int32, (rows, rows), 0)
        s_i = lax.broadcasted_iota(jnp.int32, (rows, rows), 1)
        lower = jnp.where(s_i <= t_i, 1.0, 0.0).astype(bf16)
        upper = jnp.where(t_i <= s_i, 1.0, 0.0).astype(bf16)
        rest = g_ref[...]
        cum = jnp.zeros(cum_ref.shape, f32)
        cum_t = jnp.zeros(cum_t_ref.shape, f32)
        for _ in range(3):
            part = rest.astype(bf16)
            cum = cum + lax.dot_general(lower, part, (((1,), (1,)), ((), ())), preferred_element_type=f32)
            cum_t = cum_t + jnp.dot(part, upper, preferred_element_type=f32)
            rest = rest - part.astype(f32)
        cum_ref[...] = cum
        cum_t_ref[...] = cum_t

    x = x_ref[...]
    key_sum = jnp.dot(x, wk_ref[...], preferred_element_type=f32)
    k_ref[...] = (key_sum / (1.0 + jnp.exp(-key_sum))).astype(jnp.bfloat16)
    v_ref[...] = jnp.dot(x, wv_ref[...], preferred_element_type=f32).astype(jnp.bfloat16)
    for step in range(o_ref.shape[0]):
        local_pair(k_ref, v_ref, cum_ref, o_ref, head_dim, step)


def project_keys_values(tokens, key_weight, value_weight, log_decay, head_dim):
    rows, depth = tokens.shape
    width = key_weight.shape[1]
    heads = log_decay.shape[1]
    pairs = width // LANES
    per = PER_STEP if pairs % PER_STEP == 0 else 1
    block = pl.BlockSpec((rows, per * LANES), lambda p: (0, p))
    weights = pl.BlockSpec((depth, per * LANES), lambda p: (0, p))
    return pl.pallas_call(
        functools.partial(project_kernel, head_dim=head_dim),
        grid=(pairs // per,),
        in_specs=[
            pl.BlockSpec((rows, depth), lambda p: (0, 0)),
            weights,
            weights,
            pl.BlockSpec((heads, rows), lambda p: (0, 0)),
        ],
        out_specs=[
            block,
            block,
            pl.BlockSpec((per, head_dim + 8, LANES), lambda p: (p, 0, 0)),
            pl.BlockSpec((rows, heads), lambda p: (0, 0)),
            pl.BlockSpec((heads, rows), lambda p: (0, 0)),
        ],
        out_shape=[
            jax.ShapeDtypeStruct((rows, width), jnp.bfloat16),
            jax.ShapeDtypeStruct((rows, width), jnp.bfloat16),
            jax.ShapeDtypeStruct((pairs, head_dim + 8, LANES), jnp.float32),
            jax.ShapeDtypeStruct((rows, heads), jnp.float32),
            jax.ShapeDtypeStruct((heads, rows), jnp.float32),
        ],
        cost_estimate=pl.CostEstimate(
            flops=4 * rows * depth * width + 2 * rows * LANES * width,
            transcendentals=rows * width + rows * heads,
            bytes_accessed=2 * depth * width * 2 + rows * depth * 2 + rows * width * 4,
        ),
    )(tokens, key_weight, value_weight, log_decay.T)


def finish_kernel(q_ref, intra_ref, state_ref, cum_ref, gain_ref, w_ref, o_ref, normed_ref, acc_ref, *, head_dim):
    for step in range(state_ref.shape[0]):
        finish_pair(q_ref, intra_ref, state_ref, cum_ref, gain_ref, normed_ref, head_dim, step)
    part = jnp.dot(normed_ref[...], w_ref[...], preferred_element_type=jnp.float32)
    index = pl.program_id(0)

    @pl.when(index == 0)
    def _():
        acc_ref[...] = part

    @pl.when(index > 0)
    def _():
        acc_ref[...] += part

    @pl.when(index == pl.num_programs(0) - 1)
    def _():
        o_ref[...] = acc_ref[...].astype(o_ref.dtype)


def finish_pair(q_ref, intra_ref, state_ref, cum_ref, gain_ref, o_ref, head_dim, step):
    f32 = jnp.float32
    bf16 = jnp.bfloat16
    pair = pl.program_id(0) * state_ref.shape[0] + step
    cols = pl.ds(step * LANES, LANES)
    group = LANES // head_dim
    rows = q_ref.shape[0]
    state = state_ref[step, :head_dim, :]
    tall = jnp.concatenate([state] * group, axis=0)
    r_head = lax.broadcasted_iota(jnp.int32, (LANES, LANES), 0) // head_dim
    c_head = lax.broadcasted_iota(jnp.int32, (LANES, LANES), 1) // head_dim
    block = jnp.where(r_head == c_head, tall, 0.0)
    q = q_ref[:, cols]
    inter = jnp.zeros((rows, LANES), f32)
    rest = block
    for _ in range(3):
        part = rest.astype(bf16)
        inter = inter + jnp.dot(q, part, preferred_element_type=f32)
        rest = rest - part.astype(f32)
    cum = cum_ref[...]
    lane_head = lax.broadcasted_iota(jnp.int32, (rows, LANES), 1) // head_dim
    growth = jnp.zeros((rows, LANES), f32)
    for j in range(group):
        growth = jnp.where(lane_head == j, jnp.exp(head_column(cum, pair * group + j)), growth)
    attended = intra_ref[:, cols] + inter * growth
    square = attended * attended
    scale = jnp.zeros((rows, LANES), f32)
    for j in range(group):
        mean = jnp.sum(jnp.where(lane_head == j, square, 0.0), axis=1, keepdims=True) / head_dim
        scale = jnp.where(lane_head == j, lax.rsqrt(mean + 1e-05), scale)
    o_ref[:, cols] = (attended * scale * gain_ref[:, cols]).astype(bf16)


def finish(queries, intra, states, cum, norm_gain, output_weight, head_dim):
    rows, width = queries.shape
    heads = cum.shape[1]
    pairs = width // LANES
    out_width = output_weight.shape[1]
    per = pairs
    block = pl.BlockSpec((rows, per * LANES), lambda p: (0, p))
    return pl.pallas_call(
        functools.partial(finish_kernel, head_dim=head_dim),
        grid=(pairs // per,),
        in_specs=[
            block,
            block,
            pl.BlockSpec((per,) + states.shape[1:], lambda p: (p, 0, 0)),
            pl.BlockSpec((rows, heads), lambda p: (0, 0)),
            pl.BlockSpec((1, per * LANES), lambda p: (0, p)),
            pl.BlockSpec((per * LANES, out_width), lambda p: (p, 0)),
        ],
        out_specs=pl.BlockSpec((rows, out_width), lambda p: (0, 0)),
        out_shape=jax.ShapeDtypeStruct((rows, out_width), jnp.bfloat16),
        scratch_shapes=[pltpu.VMEM((rows, per * LANES), jnp.bfloat16), pltpu.VMEM((rows, out_width), jnp.float32)],
        cost_estimate=pl.CostEstimate(
            flops=6 * rows * LANES * LANES * pairs + 2 * rows * width * out_width,
            transcendentals=rows * heads * 2,
            bytes_accessed=rows * width * 8 + width * out_width * 2,
        ),
    )(queries, intra, states, cum, norm_gain.reshape(1, width), output_weight)


def combine(earlier, later):
    body = earlier.shape[1] - 8
    row = lax.broadcasted_iota(jnp.int32, earlier.shape, 1)
    scale = jnp.where(row < body, jnp.exp(later[:, body : body + 1, :]), 1.0)
    return scale * earlier + later


def exclusive_scan(own, count):
    flat = lax.axis_index(AXES)
    core = flat % 2
    chip = flat // 2
    chips = count // 2
    half = own.shape[0] // 2
    partner = [(i, i ^ 1) for i in range(count)]
    other = lax.ppermute(own, AXES, partner)
    got = jnp.where(core == 0, other[:half], other[half:])
    first = core == 0
    through = combine(
        jnp.where(first, own[:half], other[half:]), jnp.where(first, other[:half], own[half:])
    )
    before = jnp.zeros_like(through)
    received = []
    bit = 1
    while bit < chips:
        perm = [(i, i ^ (2 * bit)) for i in range(count)]
        exchanged = lax.ppermute(through, AXES, perm)
        received.append(exchanged)
        lower = (chip & bit) != 0
        before = jnp.where(lower, combine(exchanged, before), before)
        bit *= 2
        if bit < chips:
            through = jnp.where(lower, combine(exchanged, through), combine(through, exchanged))
    back = lax.ppermute(before, AXES, partner)
    whole = jnp.where(
        core == 0,
        jnp.concatenate([before, back]),
        jnp.concatenate([combine(back, other[:half]), combine(before, got)]),
    )
    return whole, received


def layer(count, tokens, log_decay, query_weight, key_weight, value_weight, norm_gain, output_weight):
    f32 = jnp.float32
    bf16 = jnp.bfloat16
    heads = log_decay.shape[1]
    dim = key_weight.shape[1] // heads
    keys, value_rows, packed, cum, cum_t = project_keys_values(tokens, key_weight, value_weight, log_decay, dim)
    incoming, _ = exclusive_scan(packed, count)

    queries = jax.nn.silu(jnp.dot(tokens, query_weight, preferred_element_type=f32)).astype(bf16)
    blocks = keys.shape[1] // LANES
    intra = None
    cuts = (0, blocks // 2, (3 * blocks) // 4, blocks)
    for part in range(3):
        intra = intra_attention(queries, keys, value_rows, cum, cum_t, dim, cuts[part], cuts[part + 1], intra)
    return finish(queries, intra, incoming, cum, norm_gain, output_weight, dim)


def solution(mesh):
    count = mesh.shape["outer"] * mesh.shape["inner"]
    in_specs = (P(AXES, None), P(AXES, None), P(), P(), P(), P(), P())
    out_specs = P(AXES, None)
    body = lambda *args: layer(count, *args)
    return jax.shard_map(body, mesh=mesh, in_specs=in_specs, out_specs=out_specs, check_vma=False)
```

```python
import functools

import jax
import jax.numpy as jnp
from jax import lax
from jax.experimental import pallas as pl
from jax.experimental.pallas import tpu as pltpu
from jax.sharding import PartitionSpec as P


AXES = ("outer", "inner")

LANES = 128
PER_STEP = 4


def intra_kernel(q_ref, k_ref, v_ref, cum_ref, cum_t_ref, *rest, head_dim, first):
    o_ref = rest[-1]
    f32 = jnp.float32
    pair = pl.program_id(0) + first
    group = LANES // head_dim
    rows = q_ref.shape[0]
    q = q_ref[...]
    k = k_ref[...]
    v = v_ref[...]
    lane_head = lax.broadcasted_iota(jnp.int32, q.shape, 1) // head_dim
    t_i = lax.broadcasted_iota(jnp.int32, (rows, rows), 0)
    s_i = lax.broadcasted_iota(jnp.int32, (rows, rows), 1)
    lower = s_i <= t_i
    cum = cum_ref[...]
    cum_t = cum_t_ref[...]
    col_head = lax.broadcasted_iota(jnp.int32, cum.shape, 1)
    row_head = lax.broadcasted_iota(jnp.int32, cum_t.shape, 0)
    out = None
    for j in range(group):
        head = pair * group + j
        mine = lane_head == j
        q_j = jnp.where(mine, q, jnp.zeros_like(q))
        scores = lax.dot_general(q_j, k, (((1,), (1,)), ((), ())), preferred_element_type=f32)
        col = jnp.sum(jnp.where(col_head == head, cum, 0.0), axis=1, keepdims=True)
        row = jnp.sum(jnp.where(row_head == head, cum_t, 0.0), axis=0, keepdims=True)
        decay = jnp.exp(jnp.where(lower, col - row, -jnp.inf))
        weights = (scores * decay).astype(jnp.bfloat16)
        o_j = jnp.dot(weights, v, preferred_element_type=f32)
        out = o_j if out is None else jnp.where(mine, o_j, out)
    o_ref[...] = out


def intra_attention(queries, keys, value_rows, cum, cum_t, head_dim, first, stop, into=None):
    rows, width = queries.shape
    heads = cum.shape[1]
    block = pl.BlockSpec((rows, LANES), lambda p: (0, p + first))
    out_block = block
    extra = () if into is None else (into,)
    extra_specs = [] if into is None else [pl.BlockSpec(memory_space=pl.ANY)]
    whole = lambda shape: pl.BlockSpec(shape, lambda p: (0, 0))
    steps = stop - first
    flops = 4 * rows * rows * LANES * (LANES // head_dim) * steps
    return pl.pallas_call(
        functools.partial(intra_kernel, head_dim=head_dim, first=first),
        grid=(steps,),
        in_specs=[block, block, block, whole((rows, heads)), whole((heads, rows))] + extra_specs,
        out_specs=out_block,
        out_shape=jax.ShapeDtypeStruct((rows, width), jnp.float32),
        input_output_aliases={} if into is None else {5: 0},
        cost_estimate=pl.CostEstimate(
            flops=flops,
            transcendentals=rows * rows * steps * (LANES // head_dim),
            bytes_accessed=rows * steps * LANES * 10,
        ),
    )(queries, keys, value_rows, cum, cum_t, *extra)


def head_column(table, head):
    lane = lax.broadcasted_iota(jnp.int32, table.shape, 1)
    return jnp.sum(jnp.where(lane == head, table, 0.0), axis=1, keepdims=True)


def local_pair(k_ref, v_ref, cum_ref, o_ref, head_dim, step):
    f32 = jnp.float32
    pair = pl.program_id(0) * o_ref.shape[0] + step
    cols = pl.ds(step * LANES, LANES)
    group = LANES // head_dim
    rows = k_ref.shape[0]
    cum = cum_ref[...]
    lane_head = lax.broadcasted_iota(jnp.int32, (rows, LANES), 1) // head_dim
    weight = jnp.zeros((rows, LANES), f32)
    logs = jnp.zeros((1, LANES), f32)
    for j in range(group):
        col = head_column(cum, pair * group + j)
        last = col[rows - 1 :, :]
        weight = jnp.where(lane_head == j, jnp.exp(last - col), weight)
        logs = jnp.where(lane_head[:1] == j, last, logs)
    scaled = (k_ref[:, cols].astype(f32) * weight).astype(jnp.bfloat16)
    state = lax.dot_general(scaled, v_ref[:, cols], (((0,), (0,)), ((), ())), preferred_element_type=f32)
    lane = lax.broadcasted_iota(jnp.int32, (head_dim, LANES), 1) // head_dim
    packed = state[:head_dim]
    for j in range(1, group):
        packed = jnp.where(lane == j, state[j * head_dim : (j + 1) * head_dim], packed)
    o_ref[step, :head_dim, :] = packed
    tail_row = lax.broadcasted_iota(jnp.int32, (8, LANES), 0)
    o_ref[step, head_dim:, :] = jnp.where(tail_row == 0, jnp.broadcast_to(logs, (8, LANES)), 0.0)


def project_kernel(x_ref, wk_ref, wv_ref, g_ref, k_ref, v_ref, o_ref, cum_ref, cum_t_ref, *, head_dim):
    f32 = jnp.float32
    bf16 = jnp.bfloat16

    @pl.when(pl.program_id(0) == 0)
    def _():
        rows = g_ref.shape[1]
        t_i = lax.broadcasted_iota(jnp.int32, (rows, rows), 0)
        s_i = lax.broadcasted_iota(jnp.int32, (rows, rows), 1)
        lower = jnp.where(s_i <= t_i, 1.0, 0.0).astype(bf16)
        upper = jnp.where(t_i <= s_i, 1.0, 0.0).astype(bf16)
        rest = g_ref[...]
        cum = jnp.zeros(cum_ref.shape, f32)
        cum_t = jnp.zeros(cum_t_ref.shape, f32)
        for _ in range(3):
            part = rest.astype(bf16)
            cum = cum + lax.dot_general(lower, part, (((1,), (1,)), ((), ())), preferred_element_type=f32)
            cum_t = cum_t + jnp.dot(part, upper, preferred_element_type=f32)
            rest = rest - part.astype(f32)
        cum_ref[...] = cum
        cum_t_ref[...] = cum_t

    x = x_ref[...]
    key_sum = jnp.dot(x, wk_ref[...], preferred_element_type=f32)
    k_ref[...] = (key_sum / (1.0 + jnp.exp(-key_sum))).astype(jnp.bfloat16)
    v_ref[...] = jnp.dot(x, wv_ref[...], preferred_element_type=f32).astype(jnp.bfloat16)
    for step in range(o_ref.shape[0]):
        local_pair(k_ref, v_ref, cum_ref, o_ref, head_dim, step)


def project_keys_values(tokens, key_weight, value_weight, log_decay, head_dim):
    rows, depth = tokens.shape
    width = key_weight.shape[1]
    heads = log_decay.shape[1]
    pairs = width // LANES
    per = PER_STEP if pairs % PER_STEP == 0 else 1
    block = pl.BlockSpec((rows, per * LANES), lambda p: (0, p))
    weights = pl.BlockSpec((depth, per * LANES), lambda p: (0, p))
    return pl.pallas_call(
        functools.partial(project_kernel, head_dim=head_dim),
        grid=(pairs // per,),
        in_specs=[
            pl.BlockSpec((rows, depth), lambda p: (0, 0)),
            weights,
            weights,
            pl.BlockSpec((heads, rows), lambda p: (0, 0)),
        ],
        out_specs=[
            block,
            block,
            pl.BlockSpec((per, head_dim + 8, LANES), lambda p: (p, 0, 0)),
            pl.BlockSpec((rows, heads), lambda p: (0, 0)),
            pl.BlockSpec((heads, rows), lambda p: (0, 0)),
        ],
        out_shape=[
            jax.ShapeDtypeStruct((rows, width), jnp.bfloat16),
            jax.ShapeDtypeStruct((rows, width), jnp.bfloat16),
            jax.ShapeDtypeStruct((pairs, head_dim + 8, LANES), jnp.float32),
            jax.ShapeDtypeStruct((rows, heads), jnp.float32),
            jax.ShapeDtypeStruct((heads, rows), jnp.float32),
        ],
        cost_estimate=pl.CostEstimate(
            flops=4 * rows * depth * width + 2 * rows * LANES * width,
            transcendentals=rows * width + rows * heads,
            bytes_accessed=2 * depth * width * 2 + rows * depth * 2 + rows * width * 4,
        ),
    )(tokens, key_weight, value_weight, log_decay.T)


def finish_kernel(q_ref, intra_ref, state_ref, cum_ref, gain_ref, w_ref, o_ref, normed_ref, acc_ref, *, head_dim):
    for step in range(state_ref.shape[0]):
        finish_pair(q_ref, intra_ref, state_ref, cum_ref, gain_ref, normed_ref, head_dim, step)
    part = jnp.dot(normed_ref[...], w_ref[...], preferred_element_type=jnp.float32)
    index = pl.program_id(0)

    @pl.when(index == 0)
    def _():
        acc_ref[...] = part

    @pl.when(index > 0)
    def _():
        acc_ref[...] += part

    @pl.when(index == pl.num_programs(0) - 1)
    def _():
        o_ref[...] = acc_ref[...].astype(o_ref.dtype)


def finish_pair(q_ref, intra_ref, state_ref, cum_ref, gain_ref, o_ref, head_dim, step):
    f32 = jnp.float32
    bf16 = jnp.bfloat16
    pair = pl.program_id(0) * state_ref.shape[0] + step
    cols = pl.ds(step * LANES, LANES)
    group = LANES // head_dim
    rows = q_ref.shape[0]
    state = state_ref[step, :head_dim, :]
    tall = jnp.concatenate([state] * group, axis=0)
    r_head = lax.broadcasted_iota(jnp.int32, (LANES, LANES), 0) // head_dim
    c_head = lax.broadcasted_iota(jnp.int32, (LANES, LANES), 1) // head_dim
    block = jnp.where(r_head == c_head, tall, 0.0)
    q = q_ref[:, cols]
    inter = jnp.zeros((rows, LANES), f32)
    rest = block
    for _ in range(3):
        part = rest.astype(bf16)
        inter = inter + jnp.dot(q, part, preferred_element_type=f32)
        rest = rest - part.astype(f32)
    cum = cum_ref[...]
    lane_head = lax.broadcasted_iota(jnp.int32, (rows, LANES), 1) // head_dim
    growth = jnp.zeros((rows, LANES), f32)
    for j in range(group):
        growth = jnp.where(lane_head == j, jnp.exp(head_column(cum, pair * group + j)), growth)
    attended = intra_ref[:, cols] + inter * growth
    square = attended * attended
    scale = jnp.zeros((rows, LANES), f32)
    for j in range(group):
        mean = jnp.sum(jnp.where(lane_head == j, square, 0.0), axis=1, keepdims=True) / head_dim
        scale = jnp.where(lane_head == j, lax.rsqrt(mean + 1e-05), scale)
    o_ref[:, cols] = (attended * scale * gain_ref[:, cols]).astype(bf16)


def finish(queries, intra, states, cum, norm_gain, output_weight, head_dim):
    rows, width = queries.shape
    heads = cum.shape[1]
    pairs = width // LANES
    out_width = output_weight.shape[1]
    per = pairs
    block = pl.BlockSpec((rows, per * LANES), lambda p: (0, p))
    return pl.pallas_call(
        functools.partial(finish_kernel, head_dim=head_dim),
        grid=(pairs // per,),
        in_specs=[
            block,
            block,
            pl.BlockSpec((per,) + states.shape[1:], lambda p: (p, 0, 0)),
            pl.BlockSpec((rows, heads), lambda p: (0, 0)),
            pl.BlockSpec((1, per * LANES), lambda p: (0, p)),
            pl.BlockSpec((per * LANES, out_width), lambda p: (p, 0)),
        ],
        out_specs=pl.BlockSpec((rows, out_width), lambda p: (0, 0)),
        out_shape=jax.ShapeDtypeStruct((rows, out_width), jnp.bfloat16),
        scratch_shapes=[pltpu.VMEM((rows, per * LANES), jnp.bfloat16), pltpu.VMEM((rows, out_width), jnp.float32)],
        cost_estimate=pl.CostEstimate(
            flops=6 * rows * LANES * LANES * pairs + 2 * rows * width * out_width,
            transcendentals=rows * heads * 2,
            bytes_accessed=rows * width * 8 + width * out_width * 2,
        ),
    )(queries, intra, states, cum, norm_gain.reshape(1, width), output_weight)


def combine(earlier, later):
    body = earlier.shape[1] - 8
    row = lax.broadcasted_iota(jnp.int32, earlier.shape, 1)
    scale = jnp.where(row < body, jnp.exp(later[:, body : body + 1, :]), 1.0)
    return scale * earlier + later


def exclusive_scan(own, count):
    flat = lax.axis_index(AXES)
    core = flat % 2
    chip = flat // 2
    chips = count // 2
    half = own.shape[0] // 2
    partner = [(i, i ^ 1) for i in range(count)]
    other = lax.ppermute(own, AXES, partner)
    got = jnp.where(core == 0, other[:half], other[half:])
    through = jnp.where(core == 0, combine(own[:half], got), combine(got, own[half:]))
    before = jnp.zeros_like(through)
    received = []
    bit = 1
    while bit < chips:
        perm = [(i, i ^ (2 * bit)) for i in range(count)]
        exchanged = lax.ppermute(through, AXES, perm)
        received.append(exchanged)
        lower = (chip & bit) != 0
        before = jnp.where(lower, combine(exchanged, before), before)
        bit *= 2
        if bit < chips:
            through = jnp.where(lower, combine(exchanged, through), combine(through, exchanged))
    back = lax.ppermute(before, AXES, partner)
    whole = jnp.where(
        core == 0,
        jnp.concatenate([before, back]),
        jnp.concatenate([combine(back, other[:half]), combine(before, got)]),
    )
    return whole, received


def layer(count, tokens, log_decay, query_weight, key_weight, value_weight, norm_gain, output_weight):
    f32 = jnp.float32
    bf16 = jnp.bfloat16
    heads = log_decay.shape[1]
    dim = key_weight.shape[1] // heads
    keys, value_rows, packed, cum, cum_t = project_keys_values(tokens, key_weight, value_weight, log_decay, dim)
    incoming, _ = exclusive_scan(packed, count)

    queries = jax.nn.silu(jnp.dot(tokens, query_weight, preferred_element_type=f32)).astype(bf16)
    blocks = keys.shape[1] // LANES
    intra = None
    cuts = (0, blocks // 2, (3 * blocks) // 4, blocks)
    for part in range(3):
        intra = intra_attention(queries, keys, value_rows, cum, cum_t, dim, cuts[part], cuts[part + 1], intra)
    return finish(queries, intra, incoming, cum, norm_gain, output_weight, dim)


def solution(mesh):
    count = mesh.shape["outer"] * mesh.shape["inner"]
    in_specs = (P(AXES, None), P(AXES, None), P(), P(), P(), P(), P())
    out_specs = P(AXES, None)
    body = lambda *args: layer(count, *args)
    return jax.shard_map(body, mesh=mesh, in_specs=in_specs, out_specs=out_specs, check_vma=False)
```
